32 devices in a mesh: groups: 2 (over y), blk: 4 (over z), pool: 4 (over x, core).
Axes of the slice: x: 2, y: 2, z: 4, core: 2. Of those that a mesh axis runs over, the one named last changes fastest.
Arguments:
- q_new: bfloat16 [1024, 8192], P(('groups', 'blk'), 'pool'), parts along dimension 0, may hold values from -64 to 64
- kv_new: bfloat16 [1024, 8, 256], P(('groups', 'blk'), 'pool'), parts along dimension 0, may hold values from -7 to 7
- kv_cache: bfloat16 [256, 8, 128, 256], P(('groups', 'blk'), 'pool'), parts along dimension 0, may hold values from -4.5 to 4.5
- page_table: int32 [16], P('groups'), parts along dimension 0, may hold values from 0 to 127, as said below
- block_offsets: int32 [8], P('groups'), parts along dimension 0, may hold values from 0 to 3, each once
Outputs:
- attended: bfloat16 [1024, 8192], P(('groups', 'blk'), 'pool'), parts along dimension 0
The draws below stay inside these ranges and needn't reach their ends.
There are 2 independent parts, one for each index of `groups`. The reference program is written for one: setup_inputs(seed, part) draws one part's arguments, and reference() takes and returns one part's arrays. A program takes and returns all parts, laid end to end along the dimension named above; each array names one. Nothing has to cross between parts.
Inputs may be any that keep to these rules, and one draw needn't show every extreme that they name: `page_table`: distinct slots; slot s lies on blk index s // 32; at most 4 entries lie on the slots of one blk index, and exactly 4 on some blk index.
All inputs are finite; a program needn't handle non-finite values.
Results may differ from the reference program's by a relative error of at most 0.0045.
Values may be sent and summed in bfloat16 or wider, within the bound.
No kernel may reach another device: no remote copies, remote signals or barrier semaphores. Data moves between devices by JAX's collectives and lax.ppermute only.
A program may use at most 64 MiB of HBM per device.

```python
import math
import jax
import jax.numpy as jnp
from jax import lax

H = 64
KVH = 8
HD = 128
PAGE = 128
Q_DEV = 128
SLOTS_DEV = 32
CAP = 4
BLOCKS = 4
S_NEW = 512
NPAGES = 8
SLOTS = 128


def qkv_pair(key):
    base = jax.random.fold_in(key, 31)
    key_q, key_k = jax.random.split(base, 2)
    entries = jax.random.truncated_normal(key_k, -4.5, 4.5, (S_NEW, KVH, 2 * HD), jnp.float32)
    queries = 2.5 * jax.random.truncated_normal(key_q, -6.0, 6.0, (S_NEW, H * HD), jnp.float32)
    return (queries, entries)


def draw_q_new(key, part):
    queries, entries = qkv_pair(key)
    return queries.astype(jnp.bfloat16)


def draw_kv_new(key, part):
    queries, entries = qkv_pair(key)
    return entries.astype(jnp.bfloat16)


def draw_page_table(key, part):
    base = jax.random.fold_in(key, 53)
    key_full, key_order, key_slots, key_final = jax.random.split(base, 4)
    fullest = jax.random.randint(key_full, (), 0, BLOCKS)
    tickets = jnp.arange(BLOCKS * CAP, dtype=jnp.int32)
    holder = tickets // CAP
    shuffled = jax.random.permutation(key_order, BLOCKS * CAP).astype(jnp.int32)
    priority = jnp.where(holder == fullest, -1, shuffled)
    ordered = jnp.argsort(priority, stable=True)[:NPAGES].astype(jnp.int32)
    owners = ordered // CAP
    within = ordered % CAP
    noise = jax.random.randint(key_slots, (BLOCKS, SLOTS_DEV), 0, 1 << 20) * SLOTS_DEV + jnp.arange(SLOTS_DEV)[None, :]
    layouts = jnp.argsort(noise, axis=1).astype(jnp.int32)
    slots = owners * SLOTS_DEV + layouts[owners, within]
    return slots[jax.random.permutation(key_final, NPAGES)].astype(jnp.int32)


def block_levels(stream_key, dims, pieces, low, high):
    gain, own = 1.0, jax.random.fold_in(stream_key, 6)
    for dim, shards_of in pieces:
        draws = jnp.exp(jax.random.uniform(jax.random.fold_in(own, dim), (shards_of,), jnp.float32, low / len(pieces), high / len(pieces)))
        gain = gain * jnp.repeat(draws, dims[dim] // shards_of).reshape([-1 if axis == dim else 1 for axis in range(len(dims))])
    return gain


def normal_values(key, shape, width, limit, pieces=(), kind=jnp.bfloat16):
    level = block_levels(key, shape, pieces, -0.22, 0.18) if pieces else 1.0
    values = jax.random.normal(key, shape, jnp.float32) * width * level
    return jnp.minimum(jnp.maximum(values, -limit), limit).astype(kind)


def setup_inputs(seed: int = 0, part: int = 0) -> dict:
    splits = jax.random.split(jax.random.key(seed), 6)
    part_splits = jax.random.split(jax.random.fold_in(splits[5], part), 6)
    return {
        "q_new": draw_q_new(jax.random.fold_in(jax.random.fold_in(splits[5], part), 71), part),
        "kv_new": draw_kv_new(jax.random.fold_in(jax.random.fold_in(splits[5], part), 71), part),
        "kv_cache": normal_values(part_splits[2], (SLOTS, KVH, PAGE, 2 * HD), 1.0, 4.5, ((0, 4), (1, 4))),
        "page_table": draw_page_table(jax.random.fold_in(jax.random.fold_in(splits[5], part), 71), part),
        "block_offsets": jax.random.permutation(part_splits[4], BLOCKS).astype(jnp.int32),
    }


def reference(q_new, kv_new, kv_cache, page_table, block_offsets):
    group_size = H // KVH
    score_scale = 1.0 / math.sqrt(HD)
    row_ids = jnp.arange(S_NEW, dtype=jnp.int32)
    positions = (block_offsets[row_ids // Q_DEV] * Q_DEV + row_ids % Q_DEV).astype(jnp.int32)
    page_rows = kv_cache[page_table]
    prefix = jnp.transpose(page_rows, (1, 0, 2, 3)).reshape(KVH, NPAGES * PAGE, 2 * HD)
    entries = jnp.concatenate([prefix, jnp.transpose(kv_new, (1, 0, 2))], axis=1)
    key_pos = jnp.concatenate([jnp.full((NPAGES * PAGE,), -1, jnp.int32), positions])
    queries = q_new.reshape(BLOCKS, Q_DEV, KVH, group_size, HD).transpose(2, 0, 1, 3, 4)
    query_pos = positions.reshape(BLOCKS, Q_DEV)

    def one_head(head_pair):
        head_queries, head_entries = head_pair
        key_part = head_entries[:, :HD].astype(jnp.float32)
        value_part = head_entries[:, HD:].astype(jnp.float32)

        def one_block(block_pair):
            block_queries, block_pos = block_pair
            scores = jnp.einsum('qhd,kd->qhk', block_queries.astype(jnp.float32), key_part) * score_scale
            visible = (key_pos[None, :] <= block_pos[:, None])[:, None, :]
            scores = jnp.where(visible, scores, -1e+30)
            row_top = lax.optimization_barrier(jnp.max(scores, axis=2, keepdims=True))
            weights = jnp.where(visible, jnp.exp(scores - row_top), 0.0)
            row_total = lax.optimization_barrier(jnp.sum(weights, axis=2, keepdims=True))
            rounded = lax.optimization_barrier(weights.astype(jnp.bfloat16)).astype(jnp.float32)
            return (jnp.einsum('qhk,kd->qhd', rounded, value_part) / row_total).astype(jnp.bfloat16)
        return lax.map(one_block, (head_queries, query_pos))
    result = lax.map(one_head, (queries, entries))
    return result.transpose(1, 2, 0, 3, 4).reshape(S_NEW, H * HD)
```

```python
import math

import jax
import jax.numpy as jnp
from jax import lax
from jax.sharding import PartitionSpec as P

CAP = 4


def attend(running, queries, keys, values, visible, head_size):
    maxima, totals, summed = running
    score_scale = 1.0 / math.sqrt(head_size)
    scores = (
        jnp.einsum("gqd,gkd->gqk", queries, keys, preferred_element_type=jnp.float32)
        * score_scale
    )
    scores = jnp.where(visible, scores, -1e30)
    row_top = jnp.maximum(maxima, jnp.max(scores, axis=2))
    factor = jnp.exp(maxima - row_top)
    weights = jnp.where(visible, jnp.exp(scores - row_top[..., None]), 0.0)
    totals = totals * factor + jnp.sum(weights, axis=2)
    summed = summed * factor[..., None] + jnp.einsum(
        "gqk,gkd->gqd",
        weights.astype(jnp.bfloat16),
        values,
        preferred_element_type=jnp.float32,
    )
    return (row_top, totals, summed)


def local(q_new, kv_new, kv_cache, page_table, block_offsets):
    q_rows = q_new.shape[0]
    kv_heads = kv_new.shape[1]
    head_size = kv_new.shape[2] // 2
    group_size = q_new.shape[1] // (head_size * kv_heads)
    slots_dev = kv_cache.shape[0]
    page_len = kv_cache.shape[2]
    npages = page_table.shape[0]
    blocks = lax.axis_size("blk")
    myself = lax.axis_index("blk")
    pg = -(-npages // blocks)
    block_ids = jnp.arange(blocks, dtype=jnp.int32)
    my_offset = jnp.sum(jnp.where(block_ids == myself, block_offsets, 0))
    query_pos = jnp.tile(my_offset * q_rows + jnp.arange(q_rows, dtype=jnp.int32), group_size)
    queries = (
        q_new.reshape(q_rows, kv_heads, group_size, head_size)
        .transpose(1, 2, 0, 3)
        .reshape(kv_heads, group_size * q_rows, head_size)
    )
    query_span = group_size * q_rows

    page_owner = page_table // slots_dev
    owned = page_owner == myself
    page_rank = jnp.cumsum(owned.astype(jnp.int32)) - 1
    local_slot = page_table % slots_dev
    counts = jnp.sum((page_owner[None, :] == block_ids[:, None]).astype(jnp.int32), axis=1)
    per_peer = (CAP + blocks - 1) // blocks
    starts = jnp.cumsum(counts) - counts
    my_start = jnp.sum(jnp.where(block_ids == myself, starts, 0))
    peer_slots = jnp.arange(per_peer, dtype=jnp.int32)[None, :]
    wanted = (block_ids[:, None] - my_start) % blocks + peer_slots * blocks
    picked = owned[None, None, :] & (page_rank[None, None, :] == wanted[..., None])
    chosen = jnp.sum(jnp.where(picked, local_slot[None, None, :], 0), axis=2).reshape(-1)
    sent_pages = kv_cache[chosen].reshape(blocks, per_peer, kv_heads, page_len, 2 * head_size)
    sent_pages = sent_pages.transpose(0, 2, 1, 3, 4).reshape(
        blocks, kv_heads, per_peer * page_len, 2 * head_size
    )
    own_rows = jnp.broadcast_to(
        kv_new.transpose(1, 0, 2)[None], (blocks, kv_heads, q_rows, 2 * head_size)
    )
    payload = jnp.concatenate([sent_pages, own_rows], axis=2)
    received = lax.all_to_all(payload, "blk", split_axis=0, concat_axis=0, tiled=True)

    page_part = received[:, :, : per_peer * page_len]
    page_part = page_part.reshape(blocks, kv_heads, per_peer, page_len, 2 * head_size)
    page_part = page_part.transpose(0, 2, 1, 3, 4).reshape(
        blocks * per_peer, kv_heads, page_len, 2 * head_size
    )
    arriving = (myself - starts[:, None]) % blocks + peer_slots * blocks
    present = (arriving < counts[:, None]).reshape(-1)
    order_rank = jnp.cumsum(present.astype(jnp.int32)) - 1
    choose = present[None, :] & (order_rank[None, :] == jnp.arange(pg, dtype=jnp.int32)[:, None])
    positions = jnp.sum(
        jnp.where(choose, jnp.arange(blocks * per_peer, dtype=jnp.int32)[None, :], 0), axis=1
    )
    compact = page_part[positions]
    compact_valid = jnp.arange(pg, dtype=jnp.int32) * blocks + myself < npages
    gathered = lax.all_gather(compact, "blk", axis=0, tiled=True)
    gathered_valid = (
        jnp.arange(pg, dtype=jnp.int32)[None, :] * blocks + block_ids[:, None] < npages
    ).reshape(-1)

    new_rows = received[:, :, per_peer * page_len :]
    new_rows = new_rows.transpose(1, 0, 2, 3).reshape(kv_heads, blocks * q_rows, 2 * head_size)
    own_pages = compact.transpose(1, 0, 2, 3).reshape(kv_heads, pg * page_len, 2 * head_size)
    entries_a = jnp.concatenate([new_rows, own_pages], axis=1)
    row_source = jnp.repeat(block_ids, q_rows)
    key_pos = (
        jnp.sum(jnp.where(row_source[:, None] == block_ids[None, :], block_offsets[None, :], 0), axis=1)
        * q_rows
        + jnp.tile(jnp.arange(q_rows, dtype=jnp.int32), blocks)
    )
    visible_new = key_pos[None, :] <= query_pos[:, None]
    visible_own = jnp.broadcast_to(jnp.repeat(compact_valid, page_len)[None, :], (query_span, pg * page_len))
    visible_a = jnp.concatenate([visible_new, visible_own], axis=1)[None]
    running = (
        jnp.full((kv_heads, query_span), -1e30, jnp.float32),
        jnp.zeros((kv_heads, query_span), jnp.float32),
        jnp.zeros((kv_heads, query_span, head_size), jnp.float32),
    )
    running = attend(
        running, queries, entries_a[..., :head_size], entries_a[..., head_size:], visible_a, head_size
    )

    page_block = jnp.repeat(block_ids, pg)
    use_page = gathered_valid & (page_block != myself)
    entries_b = gathered.transpose(1, 0, 2, 3).reshape(
        kv_heads, blocks * pg * page_len, 2 * head_size
    )
    visible_b = jnp.repeat(use_page, page_len)[None, None, :]
    running = attend(
        running, queries, entries_b[..., :head_size], entries_b[..., head_size:], visible_b, head_size
    )
    maxima, totals, summed = running
    attended = (summed / totals[..., None]).astype(jnp.bfloat16)
    attended = attended.reshape(kv_heads, group_size, q_rows, head_size).transpose(2, 0, 1, 3)
    return attended.reshape(q_rows, kv_heads * group_size * head_size)


def solution(mesh):
    return jax.shard_map(
        local,
        mesh=mesh,
        in_specs=(
            P(("groups", "blk"), "pool"),
            P(("groups", "blk"), "pool", None),
            P(("groups", "blk"), "pool", None, None),
            P("groups"),
            P("groups"),
        ),
        out_specs=P(("groups", "blk"), "pool"),
        check_vma=False,
    )
```

```python
import math

import jax
import jax.numpy as jnp
from jax import lax
from jax.sharding import PartitionSpec as P

CAP = 4


def attend(running, queries, keys, values, visible, head_size):
    maxima, totals, summed = running
    score_scale = 1.0 / math.sqrt(head_size)
    scores = (
        jnp.einsum("gqd,gkd->gqk", queries, keys, preferred_element_type=jnp.float32)
        * score_scale
    )
    scores = jnp.where(visible, scores, -1e30)
    row_top = jnp.maximum(maxima, jnp.max(scores, axis=2))
    factor = jnp.exp(maxima - row_top)
    weights = jnp.where(visible, jnp.exp(scores - row_top[..., None]), 0.0)
    totals = totals * factor + jnp.sum(weights, axis=2)
    summed = summed * factor[..., None] + jnp.einsum(
        "gqk,gkd->gqd",
        weights.astype(jnp.bfloat16),
        values,
        preferred_element_type=jnp.float32,
    )
    return (row_top, totals, summed)


def local(q_new, kv_new, kv_cache, page_table, block_offsets):
    q_rows = q_new.shape[0]
    kv_heads = kv_new.shape[1]
    head_size = kv_new.shape[2] // 2
    group_size = q_new.shape[1] // (head_size * kv_heads)
    slots_dev = kv_cache.shape[0]
    page_len = kv_cache.shape[2]
    npages = page_table.shape[0]
    blocks = lax.axis_size("blk")
    myself = lax.axis_index("blk")
    pg = -(-npages // blocks)
    block_ids = jnp.arange(blocks, dtype=jnp.int32)
    my_offset = jnp.sum(jnp.where(block_ids == myself, block_offsets, 0))
    query_pos = jnp.tile(my_offset * q_rows + jnp.arange(q_rows, dtype=jnp.int32), group_size)
    queries = (
        q_new.reshape(q_rows, kv_heads, group_size, head_size)
        .transpose(1, 2, 0, 3)
        .reshape(kv_heads, group_size * q_rows, head_size)
    )
    query_span = group_size * q_rows

    new_all = lax.all_gather(kv_new.transpose(1, 0, 2), "blk", axis=0)

    page_owner = page_table // slots_dev
    owned = page_owner == myself
    page_rank = jnp.cumsum(owned.astype(jnp.int32)) - 1
    local_slot = page_table % slots_dev
    counts = jnp.sum((page_owner[None, :] == block_ids[:, None]).astype(jnp.int32), axis=1)
    per_peer = (CAP + blocks - 1) // blocks
    starts = jnp.cumsum(counts) - counts
    my_start = jnp.sum(jnp.where(block_ids == myself, starts, 0))
    peer_slots = jnp.arange(per_peer, dtype=jnp.int32)[None, :]
    wanted = (block_ids[:, None] - my_start) % blocks + peer_slots * blocks
    picked = owned[None, None, :] & (page_rank[None, None, :] == wanted[..., None])
    chosen = jnp.sum(jnp.where(picked, local_slot[None, None, :], 0), axis=2).reshape(-1)
    sent_pages = kv_cache[chosen].reshape(blocks, per_peer, kv_heads, page_len, 2 * head_size)
    sent_pages = sent_pages.transpose(0, 2, 1, 3, 4).reshape(
        blocks, kv_heads, per_peer * page_len, 2 * head_size
    )
    received = lax.all_to_all(sent_pages, "blk", split_axis=0, concat_axis=0, tiled=True)

    page_part = received[:, :, : per_peer * page_len]
    page_part = page_part.reshape(blocks, kv_heads, per_peer, page_len, 2 * head_size)
    page_part = page_part.transpose(0, 2, 1, 3, 4).reshape(
        blocks * per_peer, kv_heads, page_len, 2 * head_size
    )
    arriving = (myself - starts[:, None]) % blocks + peer_slots * blocks
    present = (arriving < counts[:, None]).reshape(-1)
    order_rank = jnp.cumsum(present.astype(jnp.int32)) - 1
    choose = present[None, :] & (order_rank[None, :] == jnp.arange(pg, dtype=jnp.int32)[:, None])
    positions = jnp.sum(
        jnp.where(choose, jnp.arange(blocks * per_peer, dtype=jnp.int32)[None, :], 0), axis=1
    )
    compact = page_part[positions]
    compact_valid = jnp.arange(pg, dtype=jnp.int32) * blocks + myself < npages
    gathered = lax.all_gather(compact, "blk", axis=0, tiled=True)
    gathered_valid = (
        jnp.arange(pg, dtype=jnp.int32)[None, :] * blocks + block_ids[:, None] < npages
    ).reshape(-1)

    new_rows = new_all.transpose(1, 0, 2, 3).reshape(kv_heads, blocks * q_rows, 2 * head_size)
    own_pages = compact.transpose(1, 0, 2, 3).reshape(kv_heads, pg * page_len, 2 * head_size)
    entries_a = jnp.concatenate([new_rows, own_pages], axis=1)
    row_source = jnp.repeat(block_ids, q_rows)
    key_pos = (
        jnp.sum(jnp.where(row_source[:, None] == block_ids[None, :], block_offsets[None, :], 0), axis=1)
        * q_rows
        + jnp.tile(jnp.arange(q_rows, dtype=jnp.int32), blocks)
    )
    visible_new = key_pos[None, :] <= query_pos[:, None]
    visible_own = jnp.broadcast_to(jnp.repeat(compact_valid, page_len)[None, :], (query_span, pg * page_len))
    visible_a = jnp.concatenate([visible_new, visible_own], axis=1)[None]
    running = (
        jnp.full((kv_heads, query_span), -1e30, jnp.float32),
        jnp.zeros((kv_heads, query_span), jnp.float32),
        jnp.zeros((kv_heads, query_span, head_size), jnp.float32),
    )
    running = attend(
        running, queries, entries_a[..., :head_size], entries_a[..., head_size:], visible_a, head_size
    )

    page_block = jnp.repeat(block_ids, pg)
    use_page = gathered_valid & (page_block != myself)
    entries_b = gathered.transpose(1, 0, 2, 3).reshape(
        kv_heads, blocks * pg * page_len, 2 * head_size
    )
    visible_b = jnp.repeat(use_page, page_len)[None, None, :]
    running = attend(
        running, queries, entries_b[..., :head_size], entries_b[..., head_size:], visible_b, head_size
    )
    maxima, totals, summed = running
    attended = (summed / totals[..., None]).astype(jnp.bfloat16)
    attended = attended.reshape(kv_heads, group_size, q_rows, head_size).transpose(2, 0, 1, 3)
    return attended.reshape(q_rows, kv_heads * group_size * head_size)


def solution(mesh):
    return jax.shard_map(
        local,
        mesh=mesh,
        in_specs=(
            P(("groups", "blk"), "pool"),
            P(("groups", "blk"), "pool", None),
            P(("groups", "blk"), "pool", None, None),
            P("groups"),
            P("groups"),
        ),
        out_specs=P(("groups", "blk"), "pool"),
        check_vma=False,
    )
```

```python
import functools
import math

import jax
import jax.numpy as jnp
from jax import lax
from jax.experimental import pallas as pl
from jax.experimental.pallas import tpu as pltpu
from jax.sharding import PartitionSpec as P

CAP = 4


def attention_kernel(
    new_mode, page_mode, q_ref, new_ref, page_ref, o_ref, qs_ref, m_ref, l_ref, acc_ref,
    *, group_size, q_rows, head_size,
):
    scale = 1.0 / math.sqrt(head_size)
    for h in range(group_size):
        qs_ref[h * q_rows : (h + 1) * q_rows, :] = q_ref[:, h * head_size : (h + 1) * head_size]
    m_ref[...] = jnp.full(m_ref.shape, -1e30, jnp.float32)
    l_ref[...] = jnp.zeros(l_ref.shape, jnp.float32)
    acc_ref[...] = jnp.zeros(acc_ref.shape, jnp.float32)

    def update(kv, causal):
        keys = kv[:, :head_size]
        values = kv[:, head_size:]
        scores = lax.dot_general(
            qs_ref[...], keys, (((1,), (1,)), ((), ())), preferred_element_type=jnp.float32
        ) * scale
        if causal:
            row = lax.broadcasted_iota(jnp.int32, scores.shape, 0) % q_rows
            col = lax.broadcasted_iota(jnp.int32, scores.shape, 1)
            visible = col <= row
            scores = jnp.where(visible, scores, -1e30)
        m_prev = m_ref[...]
        m_new = jnp.maximum(m_prev, jnp.max(scores, axis=1, keepdims=True))
        alpha = jnp.exp(m_prev - m_new)
        weights = jnp.exp(scores - m_new)
        if causal:
            weights = jnp.where(visible, weights, 0.0)
        l_ref[...] = alpha * l_ref[...] + jnp.sum(weights, axis=1, keepdims=True)
        acc_ref[...] = alpha * acc_ref[...] + lax.dot_general(
            weights.astype(jnp.bfloat16), values, (((1,), (0,)), ((), ())),
            preferred_element_type=jnp.float32,
        )
        m_ref[...] = m_new

    def new_step(c, carry):
        mode = new_mode[c]

        @pl.when(mode == 1)
        def _():
            update(new_ref[c, 0], False)

        @pl.when(mode == 2)
        def _():
            update(new_ref[c, 0], True)

        return carry

    def page_step(c, carry):
        @pl.when(page_mode[c] == 1)
        def _():
            update(page_ref[c, 0], False)

        return carry

    lax.fori_loop(0, new_ref.shape[0], new_step, 0)
    lax.fori_loop(0, page_ref.shape[0], page_step, 0)
    result = (acc_ref[...] / l_ref[...]).astype(o_ref.dtype)
    for h in range(group_size):
        o_ref[:, h * head_size : (h + 1) * head_size] = result[h * q_rows : (h + 1) * q_rows, :]


def attention(new_mode, page_mode, q_new, new_all, pages, group_size, head_size):
    q_rows = q_new.shape[0]
    blocks, kv_heads, new_len, width = new_all.shape
    npage, _, page_len, _ = pages.shape
    rows = group_size * q_rows
    kernel = functools.partial(
        attention_kernel, group_size=group_size, q_rows=q_rows, head_size=head_size
    )
    return pl.pallas_call(
        kernel,
        out_shape=jax.ShapeDtypeStruct(q_new.shape, q_new.dtype),
        grid_spec=pltpu.PrefetchScalarGridSpec(
            num_scalar_prefetch=2,
            grid=(kv_heads,),
            in_specs=[
                pl.BlockSpec((q_rows, group_size * head_size), lambda g, a, b: (0, g)),
                pl.BlockSpec((blocks, 1, new_len, width), lambda g, a, b: (0, g, 0, 0)),
                pl.BlockSpec((npage, 1, page_len, width), lambda g, a, b: (0, g, 0, 0)),
            ],
            out_specs=pl.BlockSpec((q_rows, group_size * head_size), lambda g, a, b: (0, g)),
            scratch_shapes=[
                pltpu.VMEM((rows, head_size), jnp.bfloat16),
                pltpu.VMEM((rows, 1), jnp.float32),
                pltpu.VMEM((rows, 1), jnp.float32),
                pltpu.VMEM((rows, head_size), jnp.float32),
            ],
        ),
    )(new_mode, page_mode, q_new, new_all, pages)


def local(q_new, kv_new, kv_cache, page_table, block_offsets):
    kv_heads = kv_new.shape[1]
    head_size = kv_new.shape[2] // 2
    group_size = q_new.shape[1] // (head_size * kv_heads)
    slots_dev = kv_cache.shape[0]
    npages = page_table.shape[0]
    blocks = lax.axis_size("blk")
    myself = lax.axis_index("blk")
    pg = -(-npages // blocks)
    block_ids = jnp.arange(blocks, dtype=jnp.int32)
    my_offset = jnp.sum(jnp.where(block_ids == myself, block_offsets, 0))

    new_all = lax.all_gather(kv_new.transpose(1, 0, 2), "blk", axis=0)

    page_owner = page_table // slots_dev
    owned = page_owner == myself
    page_rank = jnp.cumsum(owned.astype(jnp.int32)) - 1
    local_slot = page_table % slots_dev
    counts = jnp.sum((page_owner[None, :] == block_ids[:, None]).astype(jnp.int32), axis=1)
    per_peer = (CAP + blocks - 1) // blocks
    starts = jnp.cumsum(counts) - counts
    my_start = jnp.sum(jnp.where(block_ids == myself, starts, 0))
    peer_slots = jnp.arange(per_peer, dtype=jnp.int32)[None, :]
    wanted = (block_ids[:, None] - my_start) % blocks + peer_slots * blocks
    picked = owned[None, None, :] & (page_rank[None, None, :] == wanted[..., None])
    chosen = jnp.sum(jnp.where(picked, local_slot[None, None, :], 0), axis=2).reshape(-1)
    received = lax.all_to_all(kv_cache[chosen], "blk", split_axis=0, concat_axis=0, tiled=True)
    arriving = (myself - starts[:, None]) % blocks + peer_slots * blocks
    present = (arriving < counts[:, None]).reshape(-1)
    order_rank = jnp.cumsum(present.astype(jnp.int32)) - 1
    choose = present[None, :] & (order_rank[None, :] == jnp.arange(pg, dtype=jnp.int32)[:, None])
    positions = jnp.sum(
        jnp.where(choose, jnp.arange(blocks * per_peer, dtype=jnp.int32)[None, :], 0), axis=1
    )
    gathered = lax.all_gather(received[positions], "blk", axis=0, tiled=True)

    new_mode = jnp.where(
        block_offsets < my_offset, 1, jnp.where(block_offsets == my_offset, 2, 0)
    ).astype(jnp.int32)
    page_mode = (
        jnp.arange(pg, dtype=jnp.int32)[None, :] * blocks + block_ids[:, None] < npages
    ).reshape(-1).astype(jnp.int32)
    return attention(new_mode, page_mode, q_new, new_all, gathered, group_size, head_size)


def solution(mesh):
    return jax.shard_map(
        local,
        mesh=mesh,
        in_specs=(
            P(("groups", "blk"), "pool"),
            P(("groups", "blk"), "pool", None),
            P(("groups", "blk"), "pool", None, None),
            P("groups"),
            P("groups"),
        ),
        out_specs=P(("groups", "blk"), "pool"),
        check_vma=False,
    )
```

```python
import functools
import math

import jax
import jax.numpy as jnp
from jax import lax
from jax.experimental import pallas as pl
from jax.experimental.pallas import tpu as pltpu
from jax.sharding import PartitionSpec as P

CAP = 4


def attention_kernel(
    query_start, q_ref, new_ref, page_ref, key_pos_ref, page_ok_ref, o_ref, *, head_size
):
    scale = 1.0 / math.sqrt(head_size)
    queries = q_ref[...]
    new_kv = new_ref[:, 0].reshape(-1, new_ref.shape[-1])
    page_kv = page_ref[:, 0].reshape(-1, page_ref.shape[-1])
    dims = (((1,), (1,)), ((), ()))
    new_scores = lax.dot_general(
        queries, new_kv[:, :head_size], dims, preferred_element_type=jnp.float32
    ) * scale
    page_scores = lax.dot_general(
        queries, page_kv[:, :head_size], dims, preferred_element_type=jnp.float32
    ) * scale
    row_pos = query_start[0] + lax.broadcasted_iota(jnp.int32, new_scores.shape, 0)
    new_visible = key_pos_ref[...] <= row_pos
    page_visible = page_ok_ref[...] > 0
    new_scores = jnp.where(new_visible, new_scores, -1e30)
    page_scores = jnp.where(page_visible, page_scores, -1e30)
    row_top = jnp.maximum(
        jnp.max(new_scores, axis=1, keepdims=True), jnp.max(page_scores, axis=1, keepdims=True)
    )
    new_weights = jnp.where(new_visible, jnp.exp(new_scores - row_top), 0.0)
    page_weights = jnp.where(page_visible, jnp.exp(page_scores - row_top), 0.0)
    row_total = jnp.sum(new_weights, axis=1, keepdims=True) + jnp.sum(
        page_weights, axis=1, keepdims=True
    )
    pv = (((1,), (0,)), ((), ()))
    summed = lax.dot_general(
        new_weights.astype(jnp.bfloat16), new_kv[:, head_size:], pv,
        preferred_element_type=jnp.float32,
    ) + lax.dot_general(
        page_weights.astype(jnp.bfloat16), page_kv[:, head_size:], pv,
        preferred_element_type=jnp.float32,
    )
    o_ref[...] = (summed / row_total).astype(o_ref.dtype)


def attention(query_start, key_pos, page_ok, q_new, new_all, pages, group_size, head_size):
    q_rows = q_new.shape[0]
    blocks, kv_heads, new_len, width = new_all.shape
    npage, _, page_len, _ = pages.shape
    kernel = functools.partial(attention_kernel, head_size=head_size)
    return pl.pallas_call(
        kernel,
        out_shape=jax.ShapeDtypeStruct(q_new.shape, q_new.dtype),
        grid_spec=pltpu.PrefetchScalarGridSpec(
            num_scalar_prefetch=1,
            grid=(kv_heads, group_size),
            in_specs=[
                pl.BlockSpec((q_rows, head_size), lambda g, h, s: (0, g * group_size + h)),
                pl.BlockSpec((blocks, 1, new_len, width), lambda g, h, s: (0, g, 0, 0)),
                pl.BlockSpec((npage, 1, page_len, width), lambda g, h, s: (0, g, 0, 0)),
                pl.BlockSpec((1, blocks * new_len), lambda g, h, s: (0, 0)),
                pl.BlockSpec((1, npage * page_len), lambda g, h, s: (0, 0)),
            ],
            out_specs=pl.BlockSpec((q_rows, head_size), lambda g, h, s: (0, g * group_size + h)),
        ),
    )(query_start, q_new, new_all, pages, key_pos, page_ok)


def local(q_new, kv_new, kv_cache, page_table, block_offsets):
    kv_heads = kv_new.shape[1]
    head_size = kv_new.shape[2] // 2
    group_size = q_new.shape[1] // (head_size * kv_heads)
    slots_dev = kv_cache.shape[0]
    npages = page_table.shape[0]
    blocks = lax.axis_size("blk")
    myself = lax.axis_index("blk")
    pg = -(-npages // blocks)
    block_ids = jnp.arange(blocks, dtype=jnp.int32)
    my_offset = jnp.sum(jnp.where(block_ids == myself, block_offsets, 0))

    new_all = lax.all_gather(kv_new.transpose(1, 0, 2), "blk", axis=0)

    page_owner = page_table // slots_dev
    owned = page_owner == myself
    page_rank = jnp.cumsum(owned.astype(jnp.int32)) - 1
    local_slot = page_table % slots_dev
    counts = jnp.sum((page_owner[None, :] == block_ids[:, None]).astype(jnp.int32), axis=1)
    per_peer = (CAP + blocks - 1) // blocks
    starts = jnp.cumsum(counts) - counts
    my_start = jnp.sum(jnp.where(block_ids == myself, starts, 0))
    peer_slots = jnp.arange(per_peer, dtype=jnp.int32)[None, :]
    wanted = (block_ids[:, None] - my_start) % blocks + peer_slots * blocks
    picked = owned[None, None, :] & (page_rank[None, None, :] == wanted[..., None])
    chosen = jnp.sum(jnp.where(picked, local_slot[None, None, :], 0), axis=2).reshape(-1)
    received = lax.all_to_all(kv_cache[chosen], "blk", split_axis=0, concat_axis=0, tiled=True)
    arriving = (myself - starts[:, None]) % blocks + peer_slots * blocks
    present = (arriving < counts[:, None]).reshape(-1)
    order_rank = jnp.cumsum(present.astype(jnp.int32)) - 1
    choose = present[None, :] & (order_rank[None, :] == jnp.arange(pg, dtype=jnp.int32)[:, None])
    positions = jnp.sum(
        jnp.where(choose, jnp.arange(blocks * per_peer, dtype=jnp.int32)[None, :], 0), axis=1
    )
    gathered = lax.all_gather(received[positions], "blk", axis=0, tiled=True)

    q_rows = q_new.shape[0]
    page_len = kv_cache.shape[2]
    query_start = (my_offset * q_rows).reshape(1).astype(jnp.int32)
    key_pos = (
        jnp.repeat(block_offsets, q_rows) * q_rows
        + jnp.tile(jnp.arange(q_rows, dtype=jnp.int32), blocks)
    ).reshape(1, -1).astype(jnp.int32)
    page_ok = (
        jnp.arange(pg, dtype=jnp.int32)[None, :] * blocks + block_ids[:, None] < npages
    ).reshape(-1)
    page_ok = jnp.repeat(page_ok.astype(jnp.int32), page_len).reshape(1, -1)
    return attention(
        query_start, key_pos, page_ok, q_new, new_all, gathered, group_size, head_size
    )


def solution(mesh):
    return jax.shard_map(
        local,
        mesh=mesh,
        in_specs=(
            P(("groups", "blk"), "pool"),
            P(("groups", "blk"), "pool", None),
            P(("groups", "blk"), "pool", None, None),
            P("groups"),
            P("groups"),
        ),
        out_specs=P(("groups", "blk"), "pool"),
        check_vma=False,
    )
```

```python
import functools
import math

import jax
import jax.numpy as jnp
from jax import lax
from jax.experimental import pallas as pl
from jax.experimental.pallas import tpu as pltpu
from jax.sharding import PartitionSpec as P

CAP = 4


def attention_kernel(
    query_start, q_ref, new_ref, page_ref, key_pos_ref, page_ok_ref, o_ref,
    *, head_size, group_size, mask_pages,
):
    scale = 1.0 / math.sqrt(head_size)
    q_rows = q_ref.shape[0]
    new_kv = new_ref[:, 0].reshape(-1, new_ref.shape[-1])
    page_kv = page_ref[:, 0].reshape(-1, page_ref.shape[-1])
    new_keys = new_kv[:, :head_size]
    new_values = new_kv[:, head_size:]
    page_keys = page_kv[:, :head_size]
    page_values = page_kv[:, head_size:]
    row_pos = query_start[0] + lax.broadcasted_iota(jnp.int32, (q_rows, new_kv.shape[0]), 0)
    new_visible = key_pos_ref[...] <= row_pos
    page_visible = page_ok_ref[...] > 0
    dims = (((1,), (1,)), ((), ()))
    pv = (((1,), (0,)), ((), ()))
    for h in range(group_size):
        queries = q_ref[:, h * head_size : (h + 1) * head_size]
        new_scores = lax.dot_general(
            queries, new_keys, dims, preferred_element_type=jnp.float32
        ) * scale
        page_scores = lax.dot_general(
            queries, page_keys, dims, preferred_element_type=jnp.float32
        ) * scale
        new_scores = jnp.where(new_visible, new_scores, -1e30)
        if mask_pages:
            page_scores = jnp.where(page_visible, page_scores, -1e30)
        row_top = jnp.maximum(
            jnp.max(new_scores, axis=1, keepdims=True),
            jnp.max(page_scores, axis=1, keepdims=True),
        )
        new_weights = jnp.exp(new_scores - row_top)
        page_weights = jnp.exp(page_scores - row_top)
        row_total = jnp.sum(new_weights, axis=1, keepdims=True) + jnp.sum(
            page_weights, axis=1, keepdims=True
        )
        summed = lax.dot_general(
            new_weights.astype(jnp.bfloat16), new_values, pv,
            preferred_element_type=jnp.float32,
        ) + lax.dot_general(
            page_weights.astype(jnp.bfloat16), page_values, pv,
            preferred_element_type=jnp.float32,
        )
        o_ref[:, h * head_size : (h + 1) * head_size] = (summed / row_total).astype(o_ref.dtype)


def attention(query_start, key_pos, page_ok, q_new, new_all, pages, group_size, head_size,
              mask_pages):
    q_rows = q_new.shape[0]
    blocks, kv_heads, new_len, width = new_all.shape
    npage, _, page_len, _ = pages.shape
    kernel = functools.partial(
        attention_kernel, head_size=head_size, group_size=group_size, mask_pages=mask_pages
    )
    span = group_size * head_size
    return pl.pallas_call(
        kernel,
        out_shape=jax.ShapeDtypeStruct(q_new.shape, q_new.dtype),
        grid_spec=pltpu.PrefetchScalarGridSpec(
            num_scalar_prefetch=1,
            grid=(kv_heads,),
            in_specs=[
                pl.BlockSpec((q_rows, span), lambda g, s: (0, g)),
                pl.BlockSpec((blocks, 1, new_len, width), lambda g, s: (0, g, 0, 0)),
                pl.BlockSpec((npage, 1, page_len, width), lambda g, s: (0, g, 0, 0)),
                pl.BlockSpec((1, blocks * new_len), lambda g, s: (0, 0)),
                pl.BlockSpec((1, npage * page_len), lambda g, s: (0, 0)),
            ],
            out_specs=pl.BlockSpec((q_rows, span), lambda g, s: (0, g)),
        ),
    )(query_start, q_new, new_all, pages, key_pos, page_ok)


def local(q_new, kv_new, kv_cache, page_table, block_offsets):
    kv_heads = kv_new.shape[1]
    head_size = kv_new.shape[2] // 2
    group_size = q_new.shape[1] // (head_size * kv_heads)
    slots_dev = kv_cache.shape[0]
    npages = page_table.shape[0]
    blocks = lax.axis_size("blk")
    myself = lax.axis_index("blk")
    pg = -(-npages // blocks)
    block_ids = jnp.arange(blocks, dtype=jnp.int32)
    my_offset = jnp.sum(jnp.where(block_ids == myself, block_offsets, 0))

    new_all = lax.all_gather(kv_new.transpose(1, 0, 2), "blk", axis=0)

    page_owner = page_table // slots_dev
    owned = page_owner == myself
    page_rank = jnp.cumsum(owned.astype(jnp.int32)) - 1
    local_slot = page_table % slots_dev
    counts = jnp.sum((page_owner[None, :] == block_ids[:, None]).astype(jnp.int32), axis=1)
    per_peer = (CAP + blocks - 1) // blocks
    starts = jnp.cumsum(counts) - counts
    my_start = jnp.sum(jnp.where(block_ids == myself, starts, 0))
    peer_slots = jnp.arange(per_peer, dtype=jnp.int32)[None, :]
    wanted = (block_ids[:, None] - my_start) % blocks + peer_slots * blocks
    picked = owned[None, None, :] & (page_rank[None, None, :] == wanted[..., None])
    chosen = jnp.sum(jnp.where(picked, local_slot[None, None, :], 0), axis=2).reshape(-1)
    received = lax.all_to_all(kv_cache[chosen], "blk", split_axis=0, concat_axis=0, tiled=True)
    arriving = (myself - starts[:, None]) % blocks + peer_slots * blocks
    present = (arriving < counts[:, None]).reshape(-1)
    order_rank = jnp.cumsum(present.astype(jnp.int32)) - 1
    choose = present[None, :] & (order_rank[None, :] == jnp.arange(pg, dtype=jnp.int32)[:, None])
    positions = jnp.sum(
        jnp.where(choose, jnp.arange(blocks * per_peer, dtype=jnp.int32)[None, :], 0), axis=1
    )
    gathered = lax.all_gather(received[positions], "blk", axis=0, tiled=True)

    q_rows = q_new.shape[0]
    page_len = kv_cache.shape[2]
    query_start = (my_offset * q_rows).reshape(1).astype(jnp.int32)
    key_pos = (
        jnp.repeat(block_offsets, q_rows) * q_rows
        + jnp.tile(jnp.arange(q_rows, dtype=jnp.int32), blocks)
    ).reshape(1, -1).astype(jnp.int32)
    page_ok = (
        jnp.arange(pg, dtype=jnp.int32)[None, :] * blocks + block_ids[:, None] < npages
    ).reshape(-1)
    page_ok = jnp.repeat(page_ok.astype(jnp.int32), page_len).reshape(1, -1)
    return attention(
        query_start, key_pos, page_ok, q_new, new_all, gathered, group_size, head_size,
        npages % blocks != 0,
    )


def solution(mesh):
    return jax.shard_map(
        local,
        mesh=mesh,
        in_specs=(
            P(("groups", "blk"), "pool"),
            P(("groups", "blk"), "pool", None),
            P(("groups", "blk"), "pool", None, None),
            P("groups"),
            P("groups"),
        ),
        out_specs=P(("groups", "blk"), "pool"),
        check_vma=False,
    )
```

```python
import functools
import math

import jax
import jax.numpy as jnp
from jax import lax
from jax.experimental import pallas as pl
from jax.experimental.pallas import tpu as pltpu
from jax.sharding import PartitionSpec as P

CAP = 4


def new_turn_kernel(
    query_start, q_ref, new_ref, own_ref, key_pos_ref, own_ok_ref, acc_ref, top_ref, total_ref,
    *, head_size, group_size, mask_own,
):
    scale = 1.0 / math.sqrt(head_size)
    q_rows = q_ref.shape[0]
    new_kv = new_ref[:, 0].reshape(-1, new_ref.shape[-1])
    own_kv = own_ref[:, 0].reshape(-1, own_ref.shape[-1])
    row_pos = query_start[0] + lax.broadcasted_iota(jnp.int32, (q_rows, new_kv.shape[0]), 0)
    new_visible = key_pos_ref[...] <= row_pos
    own_visible = own_ok_ref[...] > 0
    dims = (((1,), (1,)), ((), ()))
    pv = (((1,), (0,)), ((), ()))
    for h in range(group_size):
        cols = slice(h * head_size, (h + 1) * head_size)
        queries = q_ref[:, cols]
        new_scores = lax.dot_general(
            queries, new_kv[:, :head_size], dims, preferred_element_type=jnp.float32
        ) * scale
        own_scores = lax.dot_general(
            queries, own_kv[:, :head_size], dims, preferred_element_type=jnp.float32
        ) * scale
        new_scores = jnp.where(new_visible, new_scores, -1e30)
        if mask_own:
            own_scores = jnp.where(own_visible, own_scores, -1e30)
        row_top = jnp.maximum(
            jnp.max(new_scores, axis=1, keepdims=True),
            jnp.max(own_scores, axis=1, keepdims=True),
        )
        new_weights = jnp.exp(new_scores - row_top)
        own_weights = jnp.exp(own_scores - row_top)
        row_total = jnp.sum(new_weights, axis=1, keepdims=True) + jnp.sum(
            own_weights, axis=1, keepdims=True
        )
        acc_ref[:, cols] = lax.dot_general(
            new_weights.astype(jnp.bfloat16), new_kv[:, head_size:], pv,
            preferred_element_type=jnp.float32,
        ) + lax.dot_general(
            own_weights.astype(jnp.bfloat16), own_kv[:, head_size:], pv,
            preferred_element_type=jnp.float32,
        )
        top_ref[:, cols] = jnp.broadcast_to(row_top, (q_rows, head_size))
        total_ref[:, cols] = jnp.broadcast_to(row_total, (q_rows, head_size))


def prefix_kernel(
    q_ref, page_ref, page_ok_ref, acc_ref, top_ref, total_ref, o_ref, *, head_size, group_size
):
    scale = 1.0 / math.sqrt(head_size)
    page_kv = page_ref[:, 0].reshape(-1, page_ref.shape[-1])
    page_visible = page_ok_ref[...] > 0
    dims = (((1,), (1,)), ((), ()))
    pv = (((1,), (0,)), ((), ()))
    for h in range(group_size):
        cols = slice(h * head_size, (h + 1) * head_size)
        scores = lax.dot_general(
            q_ref[:, cols], page_kv[:, :head_size], dims, preferred_element_type=jnp.float32
        ) * scale
        scores = jnp.where(page_visible, scores, -1e30)
        top_prev = top_ref[:, cols][:, :1]
        row_top = jnp.maximum(top_prev, jnp.max(scores, axis=1, keepdims=True))
        factor = jnp.exp(top_prev - row_top)
        weights = jnp.exp(scores - row_top)
        row_total = total_ref[:, cols][:, :1] * factor + jnp.sum(weights, axis=1, keepdims=True)
        summed = acc_ref[:, cols] * factor + lax.dot_general(
            weights.astype(jnp.bfloat16), page_kv[:, head_size:], pv,
            preferred_element_type=jnp.float32,
        )
        o_ref[:, cols] = (summed / row_total).astype(o_ref.dtype)


def new_turn_part(query_start, key_pos, own_ok, q_new, new_all, own, group_size, head_size,
                  mask_own):
    q_rows = q_new.shape[0]
    blocks, kv_heads, new_len, width = new_all.shape
    npage, _, page_len, _ = own.shape
    kernel = functools.partial(
        new_turn_kernel, head_size=head_size, group_size=group_size, mask_own=mask_own
    )
    span = group_size * head_size
    state = jax.ShapeDtypeStruct(q_new.shape, jnp.float32)
    state_spec = pl.BlockSpec((q_rows, span), lambda g, s: (0, g))
    return pl.pallas_call(
        kernel,
        out_shape=(state, state, state),
        grid_spec=pltpu.PrefetchScalarGridSpec(
            num_scalar_prefetch=1,
            grid=(kv_heads,),
            in_specs=[
                pl.BlockSpec((q_rows, span), lambda g, s: (0, g)),
                pl.BlockSpec((blocks, 1, new_len, width), lambda g, s: (0, g, 0, 0)),
                pl.BlockSpec((npage, 1, page_len, width), lambda g, s: (0, g, 0, 0)),
                pl.BlockSpec((1, blocks * new_len), lambda g, s: (0, 0)),
                pl.BlockSpec((1, npage * page_len), lambda g, s: (0, 0)),
            ],
            out_specs=(state_spec, state_spec, state_spec),
        ),
    )(query_start, q_new, new_all, own, key_pos, own_ok)


def prefix_part(page_ok, q_new, pages, acc, top, total, group_size, head_size):
    q_rows = q_new.shape[0]
    npage, kv_heads, page_len, width = pages.shape
    kernel = functools.partial(prefix_kernel, head_size=head_size, group_size=group_size)
    span = group_size * head_size
    block = pl.BlockSpec((q_rows, span), lambda g: (0, g))
    return pl.pallas_call(
        kernel,
        out_shape=jax.ShapeDtypeStruct(q_new.shape, q_new.dtype),
        grid=(kv_heads,),
        in_specs=[
            block,
            pl.BlockSpec((npage, 1, page_len, width), lambda g: (0, g, 0, 0)),
            pl.BlockSpec((1, npage * page_len), lambda g: (0, 0)),
            block,
            block,
            block,
        ],
        out_specs=block,
    )(q_new, pages, page_ok, acc, top, total)


def local(q_new, kv_new, kv_cache, page_table, block_offsets):
    kv_heads = kv_new.shape[1]
    head_size = kv_new.shape[2] // 2
    group_size = q_new.shape[1] // (head_size * kv_heads)
    slots_dev = kv_cache.shape[0]
    npages = page_table.shape[0]
    blocks = lax.axis_size("blk")
    myself = lax.axis_index("blk")
    pg = -(-npages // blocks)
    block_ids = jnp.arange(blocks, dtype=jnp.int32)
    my_offset = jnp.sum(jnp.where(block_ids == myself, block_offsets, 0))

    new_all = lax.all_gather(kv_new.transpose(1, 0, 2), "blk", axis=0)

    page_owner = page_table // slots_dev
    owned = page_owner == myself
    page_rank = jnp.cumsum(owned.astype(jnp.int32)) - 1
    local_slot = page_table % slots_dev
    counts = jnp.sum((page_owner[None, :] == block_ids[:, None]).astype(jnp.int32), axis=1)
    per_peer = (CAP + blocks - 1) // blocks
    starts = jnp.cumsum(counts) - counts
    my_start = jnp.sum(jnp.where(block_ids == myself, starts, 0))
    peer_slots = jnp.arange(per_peer, dtype=jnp.int32)[None, :]
    wanted = (block_ids[:, None] - my_start) % blocks + peer_slots * blocks
    picked = owned[None, None, :] & (page_rank[None, None, :] == wanted[..., None])
    chosen = jnp.sum(jnp.where(picked, local_slot[None, None, :], 0), axis=2).reshape(-1)
    received = lax.all_to_all(kv_cache[chosen], "blk", split_axis=0, concat_axis=0, tiled=True)
    received, new_all = lax.optimization_barrier((received, new_all))
    arriving = (myself - starts[:, None]) % blocks + peer_slots * blocks
    present = (arriving < counts[:, None]).reshape(-1)
    order_rank = jnp.cumsum(present.astype(jnp.int32)) - 1
    choose = present[None, :] & (order_rank[None, :] == jnp.arange(pg, dtype=jnp.int32)[:, None])
    positions = jnp.sum(
        jnp.where(choose, jnp.arange(blocks * per_peer, dtype=jnp.int32)[None, :], 0), axis=1
    )
    own = received[positions]
    gathered = lax.all_gather(own, "blk", axis=0, tiled=True)

    q_rows = q_new.shape[0]
    page_len = kv_cache.shape[2]
    query_start = (my_offset * q_rows).reshape(1).astype(jnp.int32)
    key_pos = (
        jnp.repeat(block_offsets, q_rows) * q_rows
        + jnp.tile(jnp.arange(q_rows, dtype=jnp.int32), blocks)
    ).reshape(1, -1).astype(jnp.int32)
    slot_ids = jnp.arange(pg, dtype=jnp.int32)
    own_ok = slot_ids * blocks + myself < npages
    own_ok = jnp.repeat(own_ok.astype(jnp.int32), page_len).reshape(1, -1)
    page_ok = (
        (slot_ids[None, :] * blocks + block_ids[:, None] < npages)
        & (block_ids[:, None] != myself)
    ).reshape(-1)
    page_ok = jnp.repeat(page_ok.astype(jnp.int32), page_len).reshape(1, -1)
    acc, top, total = new_turn_part(
        query_start, key_pos, own_ok, q_new, new_all, own, group_size, head_size,
        npages % blocks != 0,
    )
    return prefix_part(page_ok, q_new, gathered, acc, top, total, group_size, head_size)


def solution(mesh):
    return jax.shard_map(
        local,
        mesh=mesh,
        in_specs=(
            P(("groups", "blk"), "pool"),
            P(("groups", "blk"), "pool", None),
            P(("groups", "blk"), "pool", None, None),
            P("groups"),
            P("groups"),
        ),
        out_specs=P(("groups", "blk"), "pool"),
        check_vma=False,
    )
```

```python
import functools
import math

import jax
import jax.numpy as jnp
from jax import lax
from jax.experimental import pallas as pl
from jax.experimental.pallas import tpu as pltpu
from jax.sharding import PartitionSpec as P

CAP = 4


def new_turn_kernel(
    query_start, q_ref, new_ref, own_ref, key_pos_ref, own_ok_ref, acc_ref, top_ref, total_ref,
    *, head_size, group_size, mask_own,
):
    scale = 1.0 / math.sqrt(head_size)
    q_rows = q_ref.shape[0]
    new_kv = new_ref[:, 0].reshape(-1, new_ref.shape[-1])
    own_kv = own_ref[:, 0].reshape(-1, own_ref.shape[-1])
    row_pos = query_start[0] + lax.broadcasted_iota(jnp.int32, (q_rows, new_kv.shape[0]), 0)
    new_visible = key_pos_ref[...] <= row_pos
    own_visible = own_ok_ref[...] > 0
    dims = (((1,), (1,)), ((), ()))
    pv = (((1,), (0,)), ((), ()))
    for h in range(group_size):
        cols = slice(h * head_size, (h + 1) * head_size)
        queries = q_ref[:, cols]
        new_scores = lax.dot_general(
            queries, new_kv[:, :head_size], dims, preferred_element_type=jnp.float32
        ) * scale
        own_scores = lax.dot_general(
            queries, own_kv[:, :head_size], dims, preferred_element_type=jnp.float32
        ) * scale
        new_scores = jnp.where(new_visible, new_scores, -1e30)
        if mask_own:
            own_scores = jnp.where(own_visible, own_scores, -1e30)
        row_top = jnp.maximum(
            jnp.max(new_scores, axis=1, keepdims=True),
            jnp.max(own_scores, axis=1, keepdims=True),
        )
        new_weights = jnp.exp(new_scores - row_top)
        own_weights = jnp.exp(own_scores - row_top)
        row_total = jnp.sum(new_weights, axis=1, keepdims=True) + jnp.sum(
            own_weights, axis=1, keepdims=True
        )
        acc_ref[:, cols] = lax.dot_general(
            new_weights.astype(jnp.bfloat16), new_kv[:, head_size:], pv,
            preferred_element_type=jnp.float32,
        ) + lax.dot_general(
            own_weights.astype(jnp.bfloat16), own_kv[:, head_size:], pv,
            preferred_element_type=jnp.float32,
        )
        top_ref[0, :, h : h + 1] = row_top
        total_ref[0, :, h : h + 1] = row_total


def prefix_kernel(
    q_ref, page_ref, page_ok_ref, acc_ref, top_ref, total_ref, o_ref, *, head_size, group_size
):
    scale = 1.0 / math.sqrt(head_size)
    page_kv = page_ref[:, 0].reshape(-1, page_ref.shape[-1])
    page_visible = page_ok_ref[...] > 0
    dims = (((1,), (1,)), ((), ()))
    pv = (((1,), (0,)), ((), ()))
    for h in range(group_size):
        cols = slice(h * head_size, (h + 1) * head_size)
        scores = lax.dot_general(
            q_ref[:, cols], page_kv[:, :head_size], dims, preferred_element_type=jnp.float32
        ) * scale
        scores = jnp.where(page_visible, scores, -1e30)
        top_prev = top_ref[0, :, h : h + 1]
        row_top = jnp.maximum(top_prev, jnp.max(scores, axis=1, keepdims=True))
        factor = jnp.exp(top_prev - row_top)
        weights = jnp.exp(scores - row_top)
        row_total = total_ref[0, :, h : h + 1] * factor + jnp.sum(weights, axis=1, keepdims=True)
        summed = acc_ref[:, cols] * factor + lax.dot_general(
            weights.astype(jnp.bfloat16), page_kv[:, head_size:], pv,
            preferred_element_type=jnp.float32,
        )
        o_ref[:, cols] = (summed / row_total).astype(o_ref.dtype)


def new_turn_part(query_start, key_pos, own_ok, q_new, new_all, own, group_size, head_size,
                  mask_own):
    q_rows = q_new.shape[0]
    blocks, kv_heads, new_len, width = new_all.shape
    npage, _, page_len, _ = own.shape
    kernel = functools.partial(
        new_turn_kernel, head_size=head_size, group_size=group_size, mask_own=mask_own
    )
    span = group_size * head_size
    state = jax.ShapeDtypeStruct(q_new.shape, jnp.float32)
    state_spec = pl.BlockSpec((q_rows, span), lambda g, s: (0, g))
    stat = jax.ShapeDtypeStruct((kv_heads, q_rows, group_size), jnp.float32)
    stat_spec = pl.BlockSpec((1, q_rows, group_size), lambda g, s: (g, 0, 0))
    return pl.pallas_call(
        kernel,
        out_shape=(state, stat, stat),
        grid_spec=pltpu.PrefetchScalarGridSpec(
            num_scalar_prefetch=1,
            grid=(kv_heads,),
            in_specs=[
                pl.BlockSpec((q_rows, span), lambda g, s: (0, g)),
                pl.BlockSpec((blocks, 1, new_len, width), lambda g, s: (0, g, 0, 0)),
                pl.BlockSpec((npage, 1, page_len, width), lambda g, s: (0, g, 0, 0)),
                pl.BlockSpec((1, blocks * new_len), lambda g, s: (0, 0)),
                pl.BlockSpec((1, npage * page_len), lambda g, s: (0, 0)),
            ],
            out_specs=(state_spec, stat_spec, stat_spec),
        ),
    )(query_start, q_new, new_all, own, key_pos, own_ok)


def prefix_part(page_ok, q_new, pages, acc, top, total, group_size, head_size):
    q_rows = q_new.shape[0]
    npage, kv_heads, page_len, width = pages.shape
    kernel = functools.partial(prefix_kernel, head_size=head_size, group_size=group_size)
    span = group_size * head_size
    block = pl.BlockSpec((q_rows, span), lambda g: (0, g))
    stat_spec = pl.BlockSpec((1, q_rows, group_size), lambda g: (g, 0, 0))
    return pl.pallas_call(
        kernel,
        out_shape=jax.ShapeDtypeStruct(q_new.shape, q_new.dtype),
        grid=(kv_heads,),
        in_specs=[
            block,
            pl.BlockSpec((npage, 1, page_len, width), lambda g: (0, g, 0, 0)),
            pl.BlockSpec((1, npage * page_len), lambda g: (0, 0)),
            block,
            stat_spec,
            stat_spec,
        ],
        out_specs=block,
    )(q_new, pages, page_ok, acc, top, total)


def local(q_new, kv_new, kv_cache, page_table, block_offsets):
    kv_heads = kv_new.shape[1]
    head_size = kv_new.shape[2] // 2
    group_size = q_new.shape[1] // (head_size * kv_heads)
    slots_dev = kv_cache.shape[0]
    npages = page_table.shape[0]
    blocks = lax.axis_size("blk")
    myself = lax.axis_index("blk")
    pg = -(-npages // blocks)
    block_ids = jnp.arange(blocks, dtype=jnp.int32)
    my_offset = jnp.sum(jnp.where(block_ids == myself, block_offsets, 0))


    page_owner = page_table // slots_dev
    owned = page_owner == myself
    page_rank = jnp.cumsum(owned.astype(jnp.int32)) - 1
    local_slot = page_table % slots_dev
    counts = jnp.sum((page_owner[None, :] == block_ids[:, None]).astype(jnp.int32), axis=1)
    per_peer = (CAP + blocks - 1) // blocks
    starts = jnp.cumsum(counts) - counts
    my_start = jnp.sum(jnp.where(block_ids == myself, starts, 0))
    peer_slots = jnp.arange(per_peer, dtype=jnp.int32)[None, :]
    wanted = (block_ids[:, None] - my_start) % blocks + peer_slots * blocks
    picked = owned[None, None, :] & (page_rank[None, None, :] == wanted[..., None])
    chosen = jnp.sum(jnp.where(picked, local_slot[None, None, :], 0), axis=2).reshape(-1)
    received = lax.all_to_all(kv_cache[chosen], "blk", split_axis=0, concat_axis=0, tiled=True)
    arriving = (myself - starts[:, None]) % blocks + peer_slots * blocks
    present = (arriving < counts[:, None]).reshape(-1)
    order_rank = jnp.cumsum(present.astype(jnp.int32)) - 1
    choose = present[None, :] & (order_rank[None, :] == jnp.arange(pg, dtype=jnp.int32)[:, None])
    positions = jnp.sum(
        jnp.where(choose, jnp.arange(blocks * per_peer, dtype=jnp.int32)[None, :], 0), axis=1
    )
    own = received[positions]
    gathered = lax.all_gather(own, "blk", axis=0, tiled=True)
    own, new_rows = lax.optimization_barrier((own, kv_new.transpose(1, 0, 2)))
    new_all = lax.all_gather(new_rows, "blk", axis=0)

    q_rows = q_new.shape[0]
    page_len = kv_cache.shape[2]
    query_start = (my_offset * q_rows).reshape(1).astype(jnp.int32)
    key_pos = (
        jnp.repeat(block_offsets, q_rows) * q_rows
        + jnp.tile(jnp.arange(q_rows, dtype=jnp.int32), blocks)
    ).reshape(1, -1).astype(jnp.int32)
    slot_ids = jnp.arange(pg, dtype=jnp.int32)
    own_ok = slot_ids * blocks + myself < npages
    own_ok = jnp.repeat(own_ok.astype(jnp.int32), page_len).reshape(1, -1)
    page_ok = (
        (slot_ids[None, :] * blocks + block_ids[:, None] < npages)
        & (block_ids[:, None] != myself)
    ).reshape(-1)
    page_ok = jnp.repeat(page_ok.astype(jnp.int32), page_len).reshape(1, -1)
    acc, top, total = new_turn_part(
        query_start, key_pos, own_ok, q_new, new_all, own, group_size, head_size,
        npages % blocks != 0,
    )
    return prefix_part(page_ok, q_new, gathered, acc, top, total, group_size, head_size)


def solution(mesh):
    return jax.shard_map(
        local,
        mesh=mesh,
        in_specs=(
            P(("groups", "blk"), "pool"),
            P(("groups", "blk"), "pool", None),
            P(("groups", "blk"), "pool", None, None),
            P("groups"),
            P("groups"),
        ),
        out_specs=P(("groups", "blk"), "pool"),
        check_vma=False,
    )
```

```python
import functools
import math

import jax
import jax.numpy as jnp
from jax import lax
from jax.experimental import pallas as pl
from jax.experimental.pallas import tpu as pltpu
from jax.sharding import PartitionSpec as P

CAP = 4


def new_turn_kernel(
    query_start, q_ref, new_ref, own_ref, key_pos_ref, own_ok_ref, acc_ref, top_ref, total_ref,
    *, head_size, group_size, mask_own,
):
    scale = 1.0 / math.sqrt(head_size)
    q_rows = q_ref.shape[0]
    new_kv = new_ref[:, 0].reshape(-1, new_ref.shape[-1])
    own_kv = own_ref[:, 0].reshape(-1, own_ref.shape[-1])
    row_pos = query_start[0] + lax.broadcasted_iota(jnp.int32, (q_rows, new_kv.shape[0]), 0)
    new_visible = key_pos_ref[...] <= row_pos
    own_visible = own_ok_ref[...] > 0
    dims = (((1,), (1,)), ((), ()))
    pv = (((1,), (0,)), ((), ()))
    for h in range(group_size):
        cols = slice(h * head_size, (h + 1) * head_size)
        queries = q_ref[:, cols]
        new_scores = lax.dot_general(
            queries, new_kv[:, :head_size], dims, preferred_element_type=jnp.float32
        ) * scale
        own_scores = lax.dot_general(
            queries, own_kv[:, :head_size], dims, preferred_element_type=jnp.float32
        ) * scale
        new_scores = jnp.where(new_visible, new_scores, -1e30)
        if mask_own:
            own_scores = jnp.where(own_visible, own_scores, -1e30)
        row_top = jnp.maximum(
            jnp.max(new_scores, axis=1, keepdims=True),
            jnp.max(own_scores, axis=1, keepdims=True),
        )
        new_weights = jnp.exp(new_scores - row_top)
        own_weights = jnp.exp(own_scores - row_top)
        row_total = jnp.sum(new_weights, axis=1, keepdims=True) + jnp.sum(
            own_weights, axis=1, keepdims=True
        )
        acc_ref[:, cols] = lax.dot_general(
            new_weights.astype(jnp.bfloat16), new_kv[:, head_size:], pv,
            preferred_element_type=jnp.float32,
        ) + lax.dot_general(
            own_weights.astype(jnp.bfloat16), own_kv[:, head_size:], pv,
            preferred_element_type=jnp.float32,
        )
        top_ref[0, :, h : h + 1] = row_top
        total_ref[0, :, h : h + 1] = row_total


def prefix_kernel(
    q_ref, page_ref, page_ok_ref, acc_ref, top_ref, total_ref, o_ref, *, head_size, group_size
):
    scale = 1.0 / math.sqrt(head_size)
    page_kv = page_ref[:, 0].reshape(-1, page_ref.shape[-1])
    page_visible = page_ok_ref[...] > 0
    dims = (((1,), (1,)), ((), ()))
    pv = (((1,), (0,)), ((), ()))
    for h in range(group_size):
        cols = slice(h * head_size, (h + 1) * head_size)
        scores = lax.dot_general(
            q_ref[:, cols], page_kv[:, :head_size], dims, preferred_element_type=jnp.float32
        ) * scale
        scores = jnp.where(page_visible, scores, -1e30)
        top_prev = top_ref[0, :, h : h + 1]
        row_top = jnp.maximum(top_prev, jnp.max(scores, axis=1, keepdims=True))
        factor = jnp.exp(top_prev - row_top)
        weights = jnp.exp(scores - row_top)
        row_total = total_ref[0, :, h : h + 1] * factor + jnp.sum(weights, axis=1, keepdims=True)
        summed = acc_ref[:, cols] * factor + lax.dot_general(
            weights.astype(jnp.bfloat16), page_kv[:, head_size:], pv,
            preferred_element_type=jnp.float32,
        )
        o_ref[:, cols] = (summed / row_total).astype(o_ref.dtype)


def new_turn_part(query_start, key_pos, own_ok, q_new, new_all, own, group_size, head_size,
                  mask_own):
    q_rows = q_new.shape[0]
    blocks, kv_heads, new_len, width = new_all.shape
    npage, _, page_len, _ = own.shape
    kernel = functools.partial(
        new_turn_kernel, head_size=head_size, group_size=group_size, mask_own=mask_own
    )
    span = group_size * head_size
    state = jax.ShapeDtypeStruct(q_new.shape, jnp.float32)
    state_spec = pl.BlockSpec((q_rows, span), lambda g, s: (0, g))
    stat = jax.ShapeDtypeStruct((kv_heads, q_rows, group_size), jnp.float32)
    stat_spec = pl.BlockSpec((1, q_rows, group_size), lambda g, s: (g, 0, 0))
    return pl.pallas_call(
        kernel,
        out_shape=(state, stat, stat),
        grid_spec=pltpu.PrefetchScalarGridSpec(
            num_scalar_prefetch=1,
            grid=(kv_heads,),
            in_specs=[
                pl.BlockSpec((q_rows, span), lambda g, s: (0, g)),
                pl.BlockSpec((blocks, 1, new_len, width), lambda g, s: (0, g, 0, 0)),
                pl.BlockSpec((npage, 1, page_len, width), lambda g, s: (0, g, 0, 0)),
                pl.BlockSpec((1, blocks * new_len), lambda g, s: (0, 0)),
                pl.BlockSpec((1, npage * page_len), lambda g, s: (0, 0)),
            ],
            out_specs=(state_spec, stat_spec, stat_spec),
        ),
    )(query_start, q_new, new_all, own, key_pos, own_ok)


def prefix_part(page_ok, q_new, pages, acc, top, total, group_size, head_size):
    q_rows = q_new.shape[0]
    npage, kv_heads, page_len, width = pages.shape
    kernel = functools.partial(prefix_kernel, head_size=head_size, group_size=group_size)
    span = group_size * head_size
    block = pl.BlockSpec((q_rows, span), lambda g: (0, g))
    stat_spec = pl.BlockSpec((1, q_rows, group_size), lambda g: (g, 0, 0))
    return pl.pallas_call(
        kernel,
        out_shape=jax.ShapeDtypeStruct(q_new.shape, q_new.dtype),
        grid=(kv_heads,),
        in_specs=[
            block,
            pl.BlockSpec((npage, 1, page_len, width), lambda g: (0, g, 0, 0)),
            pl.BlockSpec((1, npage * page_len), lambda g: (0, 0)),
            block,
            stat_spec,
            stat_spec,
        ],
        out_specs=block,
    )(q_new, pages, page_ok, acc, top, total)


def send_kernel(table_ref, cache_ref, out_ref, sem, *, blocks, per_peer, slots_dev):
    me = lax.axis_index("blk")
    npages = table_ref.shape[0]

    def count_before(j, acc):
        return acc + (table_ref[j] // slots_dev < me).astype(jnp.int32)

    my_start = lax.fori_loop(0, npages, count_before, jnp.int32(0))

    def issue(j, rank):
        slot = table_ref[j]
        mine = slot // slots_dev == me
        dest = ((rank % blocks + my_start) % blocks) * per_peer + rank // blocks

        @pl.when(mine)
        def _():
            copy = pltpu.make_async_copy(cache_ref.at[slot % slots_dev], out_ref.at[dest], sem.at[0])
            copy.start()
            copy.wait()

        return rank + mine.astype(jnp.int32)

    lax.fori_loop(0, npages, issue, jnp.int32(0))


def compact_kernel(table_ref, recv_ref, out_ref, sem, *, blocks, per_peer, slots_dev):
    me = lax.axis_index("blk")
    npages = table_ref.shape[0]
    pg = out_ref.shape[0]

    def source(j, filled):
        def tally(i, acc):
            owner = table_ref[i] // slots_dev
            return (acc[0] + (owner == j).astype(jnp.int32), acc[1] + (owner < j).astype(jnp.int32))

        count, start = lax.fori_loop(0, npages, tally, (jnp.int32(0), jnp.int32(0)))
        for s in range(per_peer):
            arriving = (me - start) % blocks + s * blocks
            present = (arriving < count) & (filled < pg)

            @pl.when(present)
            def _():
                copy = pltpu.make_async_copy(
                    recv_ref.at[j * per_peer + s], out_ref.at[filled], sem.at[0]
                )
                copy.start()
                copy.wait()

            filled = filled + present.astype(jnp.int32)
        return filled

    lax.fori_loop(0, blocks, source, jnp.int32(0))


def pick_pages(kernel, page_table, source, count, blocks, per_peer, slots_dev):
    body = functools.partial(kernel, blocks=blocks, per_peer=per_peer, slots_dev=slots_dev)
    return pl.pallas_call(
        body,
        out_shape=jax.ShapeDtypeStruct((count,) + source.shape[1:], source.dtype),
        grid_spec=pltpu.PrefetchScalarGridSpec(
            num_scalar_prefetch=1,
            grid=(1,),
            in_specs=[pl.BlockSpec(memory_space=pl.ANY)],
            out_specs=pl.BlockSpec(memory_space=pl.ANY),
            scratch_shapes=[pltpu.SemaphoreType.DMA((1,))],
        ),
    )(page_table, source)


def local(q_new, kv_new, kv_cache, page_table, block_offsets):
    kv_heads = kv_new.shape[1]
    head_size = kv_new.shape[2] // 2
    group_size = q_new.shape[1] // (head_size * kv_heads)
    slots_dev = kv_cache.shape[0]
    npages = page_table.shape[0]
    blocks = lax.axis_size("blk")
    myself = lax.axis_index("blk")
    pg = -(-npages // blocks)
    block_ids = jnp.arange(blocks, dtype=jnp.int32)
    my_offset = jnp.sum(jnp.where(block_ids == myself, block_offsets, 0))


    per_peer = (CAP + blocks - 1) // blocks
    if npages % blocks == 0:
        sent = pick_pages(
            send_kernel, page_table, kv_cache, blocks * per_peer, blocks, per_peer, slots_dev
        )
        received = lax.all_to_all(sent, "blk", split_axis=0, concat_axis=0, tiled=True)
        own = pick_pages(compact_kernel, page_table, received, pg, blocks, per_peer, slots_dev)
    else:
        page_owner = page_table // slots_dev
        owned = page_owner == myself
        page_rank = jnp.cumsum(owned.astype(jnp.int32)) - 1
        local_slot = page_table % slots_dev
        counts = jnp.sum((page_owner[None, :] == block_ids[:, None]).astype(jnp.int32), axis=1)
        starts = jnp.cumsum(counts) - counts
        my_start = jnp.sum(jnp.where(block_ids == myself, starts, 0))
        peer_slots = jnp.arange(per_peer, dtype=jnp.int32)[None, :]
        wanted = (block_ids[:, None] - my_start) % blocks + peer_slots * blocks
        picked = owned[None, None, :] & (page_rank[None, None, :] == wanted[..., None])
        chosen = jnp.sum(jnp.where(picked, local_slot[None, None, :], 0), axis=2).reshape(-1)
        received = lax.all_to_all(
            kv_cache[chosen], "blk", split_axis=0, concat_axis=0, tiled=True
        )
        arriving = (myself - starts[:, None]) % blocks + peer_slots * blocks
        present = (arriving < counts[:, None]).reshape(-1)
        order_rank = jnp.cumsum(present.astype(jnp.int32)) - 1
        choose = present[None, :] & (
            order_rank[None, :] == jnp.arange(pg, dtype=jnp.int32)[:, None]
        )
        positions = jnp.sum(
            jnp.where(choose, jnp.arange(blocks * per_peer, dtype=jnp.int32)[None, :], 0),
            axis=1,
        )
        own = received[positions]
    gathered = lax.all_gather(own, "blk", axis=0, tiled=True)
    own, new_rows = lax.optimization_barrier((own, kv_new.transpose(1, 0, 2)))
    new_all = lax.all_gather(new_rows, "blk", axis=0)

    q_rows = q_new.shape[0]
    page_len = kv_cache.shape[2]
    query_start = (my_offset * q_rows).reshape(1).astype(jnp.int32)
    key_pos = (
        jnp.repeat(block_offsets, q_rows) * q_rows
        + jnp.tile(jnp.arange(q_rows, dtype=jnp.int32), blocks)
    ).reshape(1, -1).astype(jnp.int32)
    slot_ids = jnp.arange(pg, dtype=jnp.int32)
    own_ok = slot_ids * blocks + myself < npages
    own_ok = jnp.repeat(own_ok.astype(jnp.int32), page_len).reshape(1, -1)
    page_ok = (
        (slot_ids[None, :] * blocks + block_ids[:, None] < npages)
        & (block_ids[:, None] != myself)
    ).reshape(-1)
    page_ok = jnp.repeat(page_ok.astype(jnp.int32), page_len).reshape(1, -1)
    acc, top, total = new_turn_part(
        query_start, key_pos, own_ok, q_new, new_all, own, group_size, head_size,
        npages % blocks != 0,
    )
    return prefix_part(page_ok, q_new, gathered, acc, top, total, group_size, head_size)


def solution(mesh):
    return jax.shard_map(
        local,
        mesh=mesh,
        in_specs=(
            P(("groups", "blk"), "pool"),
            P(("groups", "blk"), "pool", None),
            P(("groups", "blk"), "pool", None, None),
            P("groups"),
            P("groups"),
        ),
        out_specs=P(("groups", "blk"), "pool"),
        check_vma=False,
    )
```

```python
import functools
import math

import jax
import jax.numpy as jnp
from jax import lax
from jax.experimental import pallas as pl
from jax.experimental.pallas import tpu as pltpu
from jax.sharding import PartitionSpec as P

CAP = 4


def attention_kernel(
    query_start, q_ref, new_ref, page_ref, key_pos_ref, page_ok_ref, o_ref,
    *, head_size, group_size, mask_pages,
):
    scale = 1.0 / math.sqrt(head_size)
    q_rows = q_ref.shape[0]
    new_kv = new_ref[:, 0].reshape(-1, new_ref.shape[-1])
    page_kv = page_ref[:, 0].reshape(-1, page_ref.shape[-1])
    new_keys = new_kv[:, :head_size]
    new_values = new_kv[:, head_size:]
    page_keys = page_kv[:, :head_size]
    page_values = page_kv[:, head_size:]
    row_pos = query_start[0] + lax.broadcasted_iota(jnp.int32, (q_rows, new_kv.shape[0]), 0)
    new_visible = key_pos_ref[...] <= row_pos
    page_visible = page_ok_ref[...] > 0
    dims = (((1,), (1,)), ((), ()))
    pv = (((1,), (0,)), ((), ()))
    for h in range(group_size):
        queries = q_ref[:, h * head_size : (h + 1) * head_size]
        new_scores = lax.dot_general(
            queries, new_keys, dims, preferred_element_type=jnp.float32
        ) * scale
        page_scores = lax.dot_general(
            queries, page_keys, dims, preferred_element_type=jnp.float32
        ) * scale
        new_scores = jnp.where(new_visible, new_scores, -1e30)
        if mask_pages:
            page_scores = jnp.where(page_visible, page_scores, -1e30)
        row_top = jnp.maximum(
            jnp.max(new_scores, axis=1, keepdims=True),
            jnp.max(page_scores, axis=1, keepdims=True),
        )
        new_weights = jnp.exp(new_scores - row_top)
        page_weights = jnp.exp(page_scores - row_top)
        row_total = jnp.sum(new_weights, axis=1, keepdims=True) + jnp.sum(
            page_weights, axis=1, keepdims=True
        )
        summed = lax.dot_general(
            new_weights.astype(jnp.bfloat16), new_values, pv,
            preferred_element_type=jnp.float32,
        ) + lax.dot_general(
            page_weights.astype(jnp.bfloat16), page_values, pv,
            preferred_element_type=jnp.float32,
        )
        o_ref[:, h * head_size : (h + 1) * head_size] = (summed / row_total).astype(o_ref.dtype)


def attention(query_start, key_pos, page_ok, q_new, new_all, pages, group_size, head_size,
              mask_pages):
    q_rows = q_new.shape[0]
    blocks, kv_heads, new_len, width = new_all.shape
    npage, _, page_len, _ = pages.shape
    kernel = functools.partial(
        attention_kernel, head_size=head_size, group_size=group_size, mask_pages=mask_pages
    )
    span = group_size * head_size
    return pl.pallas_call(
        kernel,
        out_shape=jax.ShapeDtypeStruct(q_new.shape, q_new.dtype),
        grid_spec=pltpu.PrefetchScalarGridSpec(
            num_scalar_prefetch=1,
            grid=(kv_heads,),
            in_specs=[
                pl.BlockSpec((q_rows, span), lambda g, s: (0, g)),
                pl.BlockSpec((blocks, 1, new_len, width), lambda g, s: (0, g, 0, 0)),
                pl.BlockSpec((npage, 1, page_len, width), lambda g, s: (0, g, 0, 0)),
                pl.BlockSpec((1, blocks * new_len), lambda g, s: (0, 0)),
                pl.BlockSpec((1, npage * page_len), lambda g, s: (0, 0)),
            ],
            out_specs=pl.BlockSpec((q_rows, span), lambda g, s: (0, g)),
        ),
    )(query_start, q_new, new_all, pages, key_pos, page_ok)


def local(q_new, kv_new, kv_cache, page_table, block_offsets):
    kv_heads = kv_new.shape[1]
    head_size = kv_new.shape[2] // 2
    group_size = q_new.shape[1] // (head_size * kv_heads)
    slots_dev = kv_cache.shape[0]
    npages = page_table.shape[0]
    blocks = lax.axis_size("blk")
    myself = lax.axis_index("blk")
    pg = -(-npages // blocks)
    block_ids = jnp.arange(blocks, dtype=jnp.int32)
    my_offset = jnp.sum(jnp.where(block_ids == myself, block_offsets, 0))

    new_all = lax.all_gather(kv_new.transpose(1, 0, 2), "blk", axis=0)

    page_owner = page_table // slots_dev
    owned = page_owner == myself
    page_rank = jnp.cumsum(owned.astype(jnp.int32)) - 1
    local_slot = page_table % slots_dev
    counts = jnp.sum((page_owner[None, :] == block_ids[:, None]).astype(jnp.int32), axis=1)
    per_peer = (CAP + blocks - 1) // blocks
    starts = jnp.cumsum(counts) - counts
    my_start = jnp.sum(jnp.where(block_ids == myself, starts, 0))
    peer_slots = jnp.arange(per_peer, dtype=jnp.int32)[None, :]
    wanted = (block_ids[:, None] - my_start) % blocks + peer_slots * blocks
    picked = owned[None, None, :] & (page_rank[None, None, :] == wanted[..., None])
    chosen = jnp.sum(jnp.where(picked, local_slot[None, None, :], 0), axis=2).reshape(-1)
    by_shift = chosen.reshape(blocks, per_peer)[(myself + block_ids) % blocks].reshape(-1)
    sent = kv_cache[by_shift].reshape((blocks, per_peer) + kv_cache.shape[1:])
    arrived = [sent[0]]
    for k in range(1, blocks):
        arrived.append(
            lax.ppermute(sent[k], "blk", [(i, (i + k) % blocks) for i in range(blocks)])
        )
    received = jnp.stack(arrived).reshape((blocks * per_peer,) + kv_cache.shape[1:])
    arriving = (myself - starts[:, None]) % blocks + peer_slots * blocks
    present = (arriving < counts[:, None])[(myself - block_ids) % blocks].reshape(-1)
    order_rank = jnp.cumsum(present.astype(jnp.int32)) - 1
    choose = present[None, :] & (order_rank[None, :] == jnp.arange(pg, dtype=jnp.int32)[:, None])
    positions = jnp.sum(
        jnp.where(choose, jnp.arange(blocks * per_peer, dtype=jnp.int32)[None, :], 0), axis=1
    )
    gathered = lax.all_gather(received[positions], "blk", axis=0, tiled=True)

    q_rows = q_new.shape[0]
    page_len = kv_cache.shape[2]
    query_start = (my_offset * q_rows).reshape(1).astype(jnp.int32)
    key_pos = (
        jnp.repeat(block_offsets, q_rows) * q_rows
        + jnp.tile(jnp.arange(q_rows, dtype=jnp.int32), blocks)
    ).reshape(1, -1).astype(jnp.int32)
    page_ok = (
        jnp.arange(pg, dtype=jnp.int32)[None, :] * blocks + block_ids[:, None] < npages
    ).reshape(-1)
    page_ok = jnp.repeat(page_ok.astype(jnp.int32), page_len).reshape(1, -1)
    return attention(
        query_start, key_pos, page_ok, q_new, new_all, gathered, group_size, head_size,
        npages % blocks != 0,
    )


def solution(mesh):
    return jax.shard_map(
        local,
        mesh=mesh,
        in_specs=(
            P(("groups", "blk"), "pool"),
            P(("groups", "blk"), "pool", None),
            P(("groups", "blk"), "pool", None, None),
            P("groups"),
            P("groups"),
        ),
        out_specs=P(("groups", "blk"), "pool"),
        check_vma=False,
    )
```

```python
import functools
import math

import jax
import jax.numpy as jnp
from jax import lax
from jax.experimental import pallas as pl
from jax.experimental.pallas import tpu as pltpu
from jax.sharding import PartitionSpec as P

CAP = 4


def attention_kernel(
    query_start, q_ref, new_ref, page_ref, key_pos_ref, page_ok_ref, o_ref,
    *, head_size, group_size, mask_pages,
):
    scale = 1.0 / math.sqrt(head_size)
    q_rows = q_ref.shape[0]
    new_kv = new_ref[:, 0].reshape(-1, new_ref.shape[-1])
    page_kv = page_ref[:, 0].reshape(-1, page_ref.shape[-1])
    new_keys = new_kv[:, :head_size]
    new_values = new_kv[:, head_size:]
    page_keys = page_kv[:, :head_size]
    page_values = page_kv[:, head_size:]
    row_pos = query_start[0] + lax.broadcasted_iota(jnp.int32, (q_rows, new_kv.shape[0]), 0)
    new_visible = key_pos_ref[...] <= row_pos
    page_visible = page_ok_ref[...] > 0
    dims = (((1,), (1,)), ((), ()))
    pv = (((1,), (0,)), ((), ()))
    for h in range(group_size):
        queries = q_ref[:, h * head_size : (h + 1) * head_size]
        new_scores = lax.dot_general(
            queries, new_keys, dims, preferred_element_type=jnp.float32
        ) * scale
        page_scores = lax.dot_general(
            queries, page_keys, dims, preferred_element_type=jnp.float32
        ) * scale
        new_scores = jnp.where(new_visible, new_scores, -1e30)
        if mask_pages:
            page_scores = jnp.where(page_visible, page_scores, -1e30)
        row_top = jnp.maximum(
            jnp.max(new_scores, axis=1, keepdims=True),
            jnp.max(page_scores, axis=1, keepdims=True),
        )
        new_weights = jnp.exp(new_scores - row_top)
        page_weights = jnp.exp(page_scores - row_top)
        row_total = jnp.sum(new_weights, axis=1, keepdims=True) + jnp.sum(
            page_weights, axis=1, keepdims=True
        )
        summed = lax.dot_general(
            new_weights.astype(jnp.bfloat16), new_values, pv,
            preferred_element_type=jnp.float32,
        ) + lax.dot_general(
            page_weights.astype(jnp.bfloat16), page_values, pv,
            preferred_element_type=jnp.float32,
        )
        o_ref[:, h * head_size : (h + 1) * head_size] = (summed / row_total).astype(o_ref.dtype)


def attention(query_start, key_pos, page_ok, q_new, new_all, pages, group_size, head_size,
              mask_pages):
    q_rows = q_new.shape[0]
    blocks, kv_heads, new_len, width = new_all.shape
    npage, _, page_len, _ = pages.shape
    kernel = functools.partial(
        attention_kernel, head_size=head_size, group_size=group_size, mask_pages=mask_pages
    )
    span = group_size * head_size
    return pl.pallas_call(
        kernel,
        out_shape=jax.ShapeDtypeStruct(q_new.shape, q_new.dtype),
        grid_spec=pltpu.PrefetchScalarGridSpec(
            num_scalar_prefetch=1,
            grid=(kv_heads,),
            in_specs=[
                pl.BlockSpec((q_rows, span), lambda g, s: (0, g)),
                pl.BlockSpec((blocks, 1, new_len, width), lambda g, s: (0, g, 0, 0)),
                pl.BlockSpec((npage, 1, page_len, width), lambda g, s: (0, g, 0, 0)),
                pl.BlockSpec((1, blocks * new_len), lambda g, s: (0, 0)),
                pl.BlockSpec((1, npage * page_len), lambda g, s: (0, 0)),
            ],
            out_specs=pl.BlockSpec((q_rows, span), lambda g, s: (0, g)),
        ),
    )(query_start, q_new, new_all, pages, key_pos, page_ok)


def local(q_new, kv_new, kv_cache, page_table, block_offsets):
    kv_heads = kv_new.shape[1]
    head_size = kv_new.shape[2] // 2
    group_size = q_new.shape[1] // (head_size * kv_heads)
    slots_dev = kv_cache.shape[0]
    npages = page_table.shape[0]
    blocks = lax.axis_size("blk")
    myself = lax.axis_index("blk")
    pg = -(-npages // blocks)
    block_ids = jnp.arange(blocks, dtype=jnp.int32)
    my_offset = jnp.sum(jnp.where(block_ids == myself, block_offsets, 0))

    own_rows = kv_new.transpose(1, 0, 2)
    new_all = [own_rows]
    for k in range(1, blocks):
        new_all.append(
            lax.ppermute(own_rows, "blk", [(i, (i + k) % blocks) for i in range(blocks)])
        )
    new_all = jnp.stack(new_all)
    shifted_offsets = block_offsets[(myself - block_ids) % blocks]

    page_owner = page_table // slots_dev
    owned = page_owner == myself
    page_rank = jnp.cumsum(owned.astype(jnp.int32)) - 1
    local_slot = page_table % slots_dev
    counts = jnp.sum((page_owner[None, :] == block_ids[:, None]).astype(jnp.int32), axis=1)
    per_peer = (CAP + blocks - 1) // blocks
    starts = jnp.cumsum(counts) - counts
    my_start = jnp.sum(jnp.where(block_ids == myself, starts, 0))
    peer_slots = jnp.arange(per_peer, dtype=jnp.int32)[None, :]
    wanted = (block_ids[:, None] - my_start) % blocks + peer_slots * blocks
    picked = owned[None, None, :] & (page_rank[None, None, :] == wanted[..., None])
    chosen = jnp.sum(jnp.where(picked, local_slot[None, None, :], 0), axis=2).reshape(-1)
    by_shift = chosen.reshape(blocks, per_peer)[(myself + block_ids) % blocks].reshape(-1)
    sent = kv_cache[by_shift].reshape((blocks, per_peer) + kv_cache.shape[1:])
    sent, new_all = lax.optimization_barrier((sent, new_all))
    arrived = [sent[0]]
    for k in range(1, blocks):
        arrived.append(
            lax.ppermute(sent[k], "blk", [(i, (i + k) % blocks) for i in range(blocks)])
        )
    received = jnp.stack(arrived).reshape((blocks * per_peer,) + kv_cache.shape[1:])
    arriving = (myself - starts[:, None]) % blocks + peer_slots * blocks
    present = (arriving < counts[:, None])[(myself - block_ids) % blocks].reshape(-1)
    order_rank = jnp.cumsum(present.astype(jnp.int32)) - 1
    choose = present[None, :] & (order_rank[None, :] == jnp.arange(pg, dtype=jnp.int32)[:, None])
    positions = jnp.sum(
        jnp.where(choose, jnp.arange(blocks * per_peer, dtype=jnp.int32)[None, :], 0), axis=1
    )
    gathered = lax.all_gather(received[positions], "blk", axis=0, tiled=True)

    q_rows = q_new.shape[0]
    page_len = kv_cache.shape[2]
    query_start = (my_offset * q_rows).reshape(1).astype(jnp.int32)
    key_pos = (
        jnp.repeat(shifted_offsets, q_rows) * q_rows
        + jnp.tile(jnp.arange(q_rows, dtype=jnp.int32), blocks)
    ).reshape(1, -1).astype(jnp.int32)
    page_ok = (
        jnp.arange(pg, dtype=jnp.int32)[None, :] * blocks + block_ids[:, None] < npages
    ).reshape(-1)
    page_ok = jnp.repeat(page_ok.astype(jnp.int32), page_len).reshape(1, -1)
    return attention(
        query_start, key_pos, page_ok, q_new, new_all, gathered, group_size, head_size,
        npages % blocks != 0,
    )


def solution(mesh):
    return jax.shard_map(
        local,
        mesh=mesh,
        in_specs=(
            P(("groups", "blk"), "pool"),
            P(("groups", "blk"), "pool", None),
            P(("groups", "blk"), "pool", None, None),
            P("groups"),
            P("groups"),
        ),
        out_specs=P(("groups", "blk"), "pool"),
        check_vma=False,
    )
```

```python
import functools
import math

import jax
import jax.numpy as jnp
from jax import lax
from jax.experimental import pallas as pl
from jax.experimental.pallas import tpu as pltpu
from jax.sharding import PartitionSpec as P

CAP = 4


def attention_kernel(
    query_start, q_ref, new_ref, page_ref, key_pos_ref, page_ok_ref, o_ref,
    *, head_size, group_size, mask_pages,
):
    scale = 1.0 / math.sqrt(head_size)
    q_rows = q_ref.shape[0]
    new_kv = new_ref[:, 0].reshape(-1, new_ref.shape[-1])
    page_kv = page_ref[:, 0].reshape(-1, page_ref.shape[-1])
    new_keys = new_kv[:, :head_size]
    new_values = new_kv[:, head_size:]
    page_keys = page_kv[:, :head_size]
    page_values = page_kv[:, head_size:]
    row_pos = query_start[0] + lax.broadcasted_iota(jnp.int32, (q_rows, new_kv.shape[0]), 0)
    new_visible = key_pos_ref[...] <= row_pos
    page_visible = page_ok_ref[...] > 0
    dims = (((1,), (1,)), ((), ()))
    pv = (((1,), (0,)), ((), ()))
    for h in range(group_size):
        queries = q_ref[:, h * head_size : (h + 1) * head_size]
        new_scores = lax.dot_general(
            queries, new_keys, dims, preferred_element_type=jnp.float32
        ) * scale
        page_scores = lax.dot_general(
            queries, page_keys, dims, preferred_element_type=jnp.float32
        ) * scale
        new_scores = jnp.where(new_visible, new_scores, -1e30)
        if mask_pages:
            page_scores = jnp.where(page_visible, page_scores, -1e30)
        row_top = jnp.maximum(
            jnp.max(new_scores, axis=1, keepdims=True),
            jnp.max(page_scores, axis=1, keepdims=True),
        )
        new_weights = jnp.exp(new_scores - row_top)
        page_weights = jnp.exp(page_scores - row_top)
        row_total = jnp.sum(new_weights, axis=1, keepdims=True) + jnp.sum(
            page_weights, axis=1, keepdims=True
        )
        summed = lax.dot_general(
            new_weights.astype(jnp.bfloat16), new_values, pv,
            preferred_element_type=jnp.float32,
        ) + lax.dot_general(
            page_weights.astype(jnp.bfloat16), page_values, pv,
            preferred_element_type=jnp.float32,
        )
        o_ref[:, h * head_size : (h + 1) * head_size] = (summed / row_total).astype(o_ref.dtype)


def attention(query_start, key_pos, page_ok, q_new, new_all, pages, group_size, head_size,
              mask_pages):
    q_rows = q_new.shape[0]
    blocks, kv_heads, new_len, width = new_all.shape
    npage, _, page_len, _ = pages.shape
    kernel = functools.partial(
        attention_kernel, head_size=head_size, group_size=group_size, mask_pages=mask_pages
    )
    span = group_size * head_size
    return pl.pallas_call(
        kernel,
        out_shape=jax.ShapeDtypeStruct(q_new.shape, q_new.dtype),
        grid_spec=pltpu.PrefetchScalarGridSpec(
            num_scalar_prefetch=1,
            grid=(kv_heads,),
            in_specs=[
                pl.BlockSpec((q_rows, span), lambda g, s: (0, g)),
                pl.BlockSpec((blocks, 1, new_len, width), lambda g, s: (0, g, 0, 0)),
                pl.BlockSpec((npage, 1, page_len, width), lambda g, s: (0, g, 0, 0)),
                pl.BlockSpec((1, blocks * new_len), lambda g, s: (0, 0)),
                pl.BlockSpec((1, npage * page_len), lambda g, s: (0, 0)),
            ],
            out_specs=pl.BlockSpec((q_rows, span), lambda g, s: (0, g)),
        ),
    )(query_start, q_new, new_all, pages, key_pos, page_ok)


def local(q_new, kv_new, kv_cache, page_table, block_offsets):
    kv_heads = kv_new.shape[1]
    head_size = kv_new.shape[2] // 2
    group_size = q_new.shape[1] // (head_size * kv_heads)
    slots_dev = kv_cache.shape[0]
    npages = page_table.shape[0]
    blocks = lax.axis_size("blk")
    myself = lax.axis_index("blk")
    pg = -(-npages // blocks)
    block_ids = jnp.arange(blocks, dtype=jnp.int32)
    my_offset = jnp.sum(jnp.where(block_ids == myself, block_offsets, 0))

    own_rows = kv_new.transpose(1, 0, 2)
    new_all = [own_rows]
    for k in range(1, blocks):
        new_all.append(
            lax.ppermute(own_rows, "blk", [(i, (i + k) % blocks) for i in range(blocks)])
        )
    new_all = jnp.stack(new_all)
    shifted_offsets = block_offsets[(myself - block_ids) % blocks]

    page_owner = page_table // slots_dev
    owned = page_owner == myself
    page_rank = jnp.cumsum(owned.astype(jnp.int32)) - 1
    local_slot = page_table % slots_dev
    counts = jnp.sum((page_owner[None, :] == block_ids[:, None]).astype(jnp.int32), axis=1)
    per_peer = (CAP + blocks - 1) // blocks
    starts = jnp.cumsum(counts) - counts
    my_start = jnp.sum(jnp.where(block_ids == myself, starts, 0))
    peer_slots = jnp.arange(per_peer, dtype=jnp.int32)[None, :]
    wanted = (block_ids[:, None] - my_start) % blocks + peer_slots * blocks
    picked = owned[None, None, :] & (page_rank[None, None, :] == wanted[..., None])
    chosen = jnp.sum(jnp.where(picked, local_slot[None, None, :], 0), axis=2).reshape(-1)
    by_shift = chosen.reshape(blocks, per_peer)[(myself + block_ids) % blocks].reshape(-1)
    sent = kv_cache[by_shift].reshape((blocks, per_peer) + kv_cache.shape[1:])
    sent, new_all = lax.optimization_barrier((sent, new_all))
    arrived = [sent[0]]
    for k in range(1, blocks):
        arrived.append(
            lax.ppermute(sent[k], "blk", [(i, (i + k) % blocks) for i in range(blocks)])
        )
    received = jnp.stack(arrived).reshape((blocks * per_peer,) + kv_cache.shape[1:])
    arriving = (myself - starts[:, None]) % blocks + peer_slots * blocks
    present = (arriving < counts[:, None])[(myself - block_ids) % blocks].reshape(-1)
    order_rank = jnp.cumsum(present.astype(jnp.int32)) - 1
    choose = present[None, :] & (order_rank[None, :] == jnp.arange(pg, dtype=jnp.int32)[:, None])
    positions = jnp.sum(
        jnp.where(choose, jnp.arange(blocks * per_peer, dtype=jnp.int32)[None, :], 0), axis=1
    )
    own = received[positions]
    gathered = [own]
    for k in range(1, blocks):
        gathered.append(
            lax.ppermute(own, "blk", [(i, (i + k) % blocks) for i in range(blocks)])
        )
    gathered = jnp.concatenate(gathered)

    q_rows = q_new.shape[0]
    page_len = kv_cache.shape[2]
    query_start = (my_offset * q_rows).reshape(1).astype(jnp.int32)
    key_pos = (
        jnp.repeat(shifted_offsets, q_rows) * q_rows
        + jnp.tile(jnp.arange(q_rows, dtype=jnp.int32), blocks)
    ).reshape(1, -1).astype(jnp.int32)
    page_ok = (
        jnp.arange(pg, dtype=jnp.int32)[None, :] * blocks + ((myself - block_ids) % blocks)[:, None]
        < npages
    ).reshape(-1)
    page_ok = jnp.repeat(page_ok.astype(jnp.int32), page_len).reshape(1, -1)
    return attention(
        query_start, key_pos, page_ok, q_new, new_all, gathered, group_size, head_size,
        npages % blocks != 0,
    )


def solution(mesh):
    return jax.shard_map(
        local,
        mesh=mesh,
        in_specs=(
            P(("groups", "blk"), "pool"),
            P(("groups", "blk"), "pool", None),
            P(("groups", "blk"), "pool", None, None),
            P("groups"),
            P("groups"),
        ),
        out_specs=P(("groups", "blk"), "pool"),
        check_vma=False,
    )
```

```python
import functools
import math

import jax
import jax.numpy as jnp
from jax import lax
from jax.experimental import pallas as pl
from jax.experimental.pallas import tpu as pltpu
from jax.sharding import PartitionSpec as P

CAP = 4


def attention_kernel(
    query_start, q_ref, new_ref, page_ref, key_pos_ref, page_ok_ref, o_ref,
    *, head_size, group_size, mask_pages,
):
    scale = 1.0 / math.sqrt(head_size)
    q_rows = q_ref.shape[0]
    new_kv = new_ref[:, 0].reshape(-1, new_ref.shape[-1])
    page_kv = page_ref[:, 0].reshape(-1, page_ref.shape[-1])
    new_keys = new_kv[:, :head_size]
    new_values = new_kv[:, head_size:]
    page_keys = page_kv[:, :head_size]
    page_values = page_kv[:, head_size:]
    row_pos = query_start[0] + lax.broadcasted_iota(jnp.int32, (q_rows, new_kv.shape[0]), 0)
    new_visible = key_pos_ref[...] <= row_pos
    page_visible = page_ok_ref[...] > 0
    dims = (((1,), (1,)), ((), ()))
    pv = (((1,), (0,)), ((), ()))
    stack = 2 if group_size % 2 == 0 else 1
    new_visible = jnp.concatenate([new_visible] * stack, axis=0)
    for c in range(group_size // stack):
        heads = range(c * stack, (c + 1) * stack)
        queries = jnp.concatenate(
            [q_ref[:, h * head_size : (h + 1) * head_size] for h in heads], axis=0
        )
        new_scores = lax.dot_general(
            queries, new_keys, dims, preferred_element_type=jnp.float32
        ) * scale
        page_scores = lax.dot_general(
            queries, page_keys, dims, preferred_element_type=jnp.float32
        ) * scale
        new_scores = jnp.where(new_visible, new_scores, -1e30)
        if mask_pages:
            page_scores = jnp.where(page_visible, page_scores, -1e30)
        row_top = jnp.maximum(
            jnp.max(new_scores, axis=1, keepdims=True),
            jnp.max(page_scores, axis=1, keepdims=True),
        )
        new_weights = jnp.exp(new_scores - row_top)
        page_weights = jnp.exp(page_scores - row_top)
        row_total = jnp.sum(new_weights, axis=1, keepdims=True) + jnp.sum(
            page_weights, axis=1, keepdims=True
        )
        summed = lax.dot_general(
            new_weights.astype(jnp.bfloat16), new_values, pv,
            preferred_element_type=jnp.float32,
        ) + lax.dot_general(
            page_weights.astype(jnp.bfloat16), page_values, pv,
            preferred_element_type=jnp.float32,
        )
        result = (summed / row_total).astype(o_ref.dtype)
        for j, h in enumerate(heads):
            o_ref[:, h * head_size : (h + 1) * head_size] = result[j * q_rows : (j + 1) * q_rows]


def attention(query_start, key_pos, page_ok, q_new, new_all, pages, group_size, head_size,
              mask_pages):
    q_rows = q_new.shape[0]
    blocks, kv_heads, new_len, width = new_all.shape
    npage, _, page_len, _ = pages.shape
    kernel = functools.partial(
        attention_kernel, head_size=head_size, group_size=group_size, mask_pages=mask_pages
    )
    span = group_size * head_size
    return pl.pallas_call(
        kernel,
        out_shape=jax.ShapeDtypeStruct(q_new.shape, q_new.dtype),
        grid_spec=pltpu.PrefetchScalarGridSpec(
            num_scalar_prefetch=1,
            grid=(kv_heads,),
            in_specs=[
                pl.BlockSpec((q_rows, span), lambda g, s: (0, g)),
                pl.BlockSpec((blocks, 1, new_len, width), lambda g, s: (0, g, 0, 0)),
                pl.BlockSpec((npage, 1, page_len, width), lambda g, s: (0, g, 0, 0)),
                pl.BlockSpec((1, blocks * new_len), lambda g, s: (0, 0)),
                pl.BlockSpec((1, npage * page_len), lambda g, s: (0, 0)),
            ],
            out_specs=pl.BlockSpec((q_rows, span), lambda g, s: (0, g)),
        ),
    )(query_start, q_new, new_all, pages, key_pos, page_ok)


def local(q_new, kv_new, kv_cache, page_table, block_offsets):
    kv_heads = kv_new.shape[1]
    head_size = kv_new.shape[2] // 2
    group_size = q_new.shape[1] // (head_size * kv_heads)
    slots_dev = kv_cache.shape[0]
    npages = page_table.shape[0]
    blocks = lax.axis_size("blk")
    myself = lax.axis_index("blk")
    pg = -(-npages // blocks)
    block_ids = jnp.arange(blocks, dtype=jnp.int32)
    my_offset = jnp.sum(jnp.where(block_ids == myself, block_offsets, 0))

    own_rows = kv_new.transpose(1, 0, 2)
    new_all = [own_rows]
    for k in range(1, blocks):
        new_all.append(
            lax.ppermute(own_rows, "blk", [(i, (i + k) % blocks) for i in range(blocks)])
        )
    new_all = jnp.stack(new_all)
    shifted_offsets = block_offsets[(myself - block_ids) % blocks]

    page_owner = page_table // slots_dev
    owned = page_owner == myself
    page_rank = jnp.cumsum(owned.astype(jnp.int32)) - 1
    local_slot = page_table % slots_dev
    counts = jnp.sum((page_owner[None, :] == block_ids[:, None]).astype(jnp.int32), axis=1)
    per_peer = (CAP + blocks - 1) // blocks
    starts = jnp.cumsum(counts) - counts
    my_start = jnp.sum(jnp.where(block_ids == myself, starts, 0))
    peer_slots = jnp.arange(per_peer, dtype=jnp.int32)[None, :]
    wanted = (block_ids[:, None] - my_start) % blocks + peer_slots * blocks
    picked = owned[None, None, :] & (page_rank[None, None, :] == wanted[..., None])
    chosen = jnp.sum(jnp.where(picked, local_slot[None, None, :], 0), axis=2).reshape(-1)
    by_shift = chosen.reshape(blocks, per_peer)[(myself + block_ids) % blocks].reshape(-1)
    sent = kv_cache[by_shift].reshape((blocks, per_peer) + kv_cache.shape[1:])
    sent, new_all = lax.optimization_barrier((sent, new_all))
    arrived = [sent[0]]
    for k in range(1, blocks):
        arrived.append(
            lax.ppermute(sent[k], "blk", [(i, (i + k) % blocks) for i in range(blocks)])
        )
    received = jnp.stack(arrived).reshape((blocks * per_peer,) + kv_cache.shape[1:])
    arriving = (myself - starts[:, None]) % blocks + peer_slots * blocks
    present = (arriving < counts[:, None])[(myself - block_ids) % blocks].reshape(-1)
    order_rank = jnp.cumsum(present.astype(jnp.int32)) - 1
    choose = present[None, :] & (order_rank[None, :] == jnp.arange(pg, dtype=jnp.int32)[:, None])
    positions = jnp.sum(
        jnp.where(choose, jnp.arange(blocks * per_peer, dtype=jnp.int32)[None, :], 0), axis=1
    )
    own = received[positions]
    gathered = [own]
    for k in range(1, blocks):
        gathered.append(
            lax.ppermute(own, "blk", [(i, (i + k) % blocks) for i in range(blocks)])
        )
    gathered = jnp.concatenate(gathered)

    q_rows = q_new.shape[0]
    page_len = kv_cache.shape[2]
    query_start = (my_offset * q_rows).reshape(1).astype(jnp.int32)
    key_pos = (
        jnp.repeat(shifted_offsets, q_rows) * q_rows
        + jnp.tile(jnp.arange(q_rows, dtype=jnp.int32), blocks)
    ).reshape(1, -1).astype(jnp.int32)
    page_ok = (
        jnp.arange(pg, dtype=jnp.int32)[None, :] * blocks + ((myself - block_ids) % blocks)[:, None]
        < npages
    ).reshape(-1)
    page_ok = jnp.repeat(page_ok.astype(jnp.int32), page_len).reshape(1, -1)
    return attention(
        query_start, key_pos, page_ok, q_new, new_all, gathered, group_size, head_size,
        npages % blocks != 0,
    )


def solution(mesh):
    return jax.shard_map(
        local,
        mesh=mesh,
        in_specs=(
            P(("groups", "blk"), "pool"),
            P(("groups", "blk"), "pool", None),
            P(("groups", "blk"), "pool", None, None),
            P("groups"),
            P("groups"),
        ),
        out_specs=P(("groups", "blk"), "pool"),
        check_vma=False,
    )
```

```python
import functools
import math

import jax
import jax.numpy as jnp
from jax import lax
from jax.experimental import pallas as pl
from jax.experimental.pallas import tpu as pltpu
from jax.sharding import PartitionSpec as P

CAP = 4


def attention_kernel(query_start, q_ref, *refs, head_size, group_size, mask_pages, chunks):
    new_refs = refs[:chunks]
    page_refs = refs[chunks : 2 * chunks]
    key_pos_ref, page_ok_ref, o_ref = refs[2 * chunks :]
    scale = 1.0 / math.sqrt(head_size)
    q_rows = q_ref.shape[0]
    new_kv = jnp.concatenate([r[0] for r in new_refs], axis=0)
    page_kv = jnp.concatenate(
        [r[:, 0].reshape(-1, r.shape[-1]) for r in page_refs], axis=0
    )
    new_keys = new_kv[:, :head_size]
    new_values = new_kv[:, head_size:]
    page_keys = page_kv[:, :head_size]
    page_values = page_kv[:, head_size:]
    row_pos = query_start[0] + lax.broadcasted_iota(jnp.int32, (q_rows, new_kv.shape[0]), 0)
    new_visible = key_pos_ref[...] <= row_pos
    page_visible = page_ok_ref[...] > 0
    dims = (((1,), (1,)), ((), ()))
    pv = (((1,), (0,)), ((), ()))
    stack = math.gcd(group_size, 4)
    new_visible = jnp.concatenate([new_visible] * stack, axis=0)
    for c in range(group_size // stack):
        heads = range(c * stack, (c + 1) * stack)
        queries = jnp.concatenate(
            [q_ref[:, h * head_size : (h + 1) * head_size] for h in heads], axis=0
        )
        new_scores = lax.dot_general(
            queries, new_keys, dims, preferred_element_type=jnp.float32
        ) * scale
        page_scores = lax.dot_general(
            queries, page_keys, dims, preferred_element_type=jnp.float32
        ) * scale
        new_scores = jnp.where(new_visible, new_scores, -1e30)
        if mask_pages:
            page_scores = jnp.where(page_visible, page_scores, -1e30)
        row_top = jnp.maximum(
            jnp.max(new_scores, axis=1, keepdims=True),
            jnp.max(page_scores, axis=1, keepdims=True),
        )
        new_weights = jnp.exp(new_scores - row_top)
        page_weights = jnp.exp(page_scores - row_top)
        row_total = jnp.sum(new_weights, axis=1, keepdims=True) + jnp.sum(
            page_weights, axis=1, keepdims=True
        )
        summed = lax.dot_general(
            new_weights.astype(jnp.bfloat16), new_values, pv,
            preferred_element_type=jnp.float32,
        ) + lax.dot_general(
            page_weights.astype(jnp.bfloat16), page_values, pv,
            preferred_element_type=jnp.float32,
        )
        result = (summed / row_total).astype(o_ref.dtype)
        for j, h in enumerate(heads):
            o_ref[:, h * head_size : (h + 1) * head_size] = result[j * q_rows : (j + 1) * q_rows]


def attention(query_start, key_pos, page_ok, q_new, new_list, page_list, group_size, head_size,
              mask_pages):
    q_rows = q_new.shape[0]
    blocks = len(new_list)
    kv_heads, new_len, width = new_list[0].shape
    pg, _, page_len, _ = page_list[0].shape
    npage = blocks * pg
    kernel = functools.partial(
        attention_kernel, head_size=head_size, group_size=group_size, mask_pages=mask_pages,
        chunks=blocks,
    )
    span = group_size * head_size
    return pl.pallas_call(
        kernel,
        out_shape=jax.ShapeDtypeStruct(q_new.shape, q_new.dtype),
        grid_spec=pltpu.PrefetchScalarGridSpec(
            num_scalar_prefetch=1,
            grid=(kv_heads,),
            in_specs=[
                pl.BlockSpec((q_rows, span), lambda g, s: (0, g)),
                *[pl.BlockSpec((1, new_len, width), lambda g, s: (g, 0, 0))] * blocks,
                *[pl.BlockSpec((pg, 1, page_len, width), lambda g, s: (0, g, 0, 0))] * blocks,
                pl.BlockSpec((1, blocks * new_len), lambda g, s: (0, 0)),
                pl.BlockSpec((1, npage * page_len), lambda g, s: (0, 0)),
            ],
            out_specs=pl.BlockSpec((q_rows, span), lambda g, s: (0, g)),
        ),
    )(query_start, q_new, *new_list, *page_list, key_pos, page_ok)


def local(q_new, kv_new, kv_cache, page_table, block_offsets):
    kv_heads = kv_new.shape[1]
    head_size = kv_new.shape[2] // 2
    group_size = q_new.shape[1] // (head_size * kv_heads)
    slots_dev = kv_cache.shape[0]
    npages = page_table.shape[0]
    blocks = lax.axis_size("blk")
    myself = lax.axis_index("blk")
    pg = -(-npages // blocks)
    block_ids = jnp.arange(blocks, dtype=jnp.int32)
    my_offset = jnp.sum(jnp.where(block_ids == myself, block_offsets, 0))

    own_rows = kv_new.transpose(1, 0, 2)
    new_all = [own_rows]
    for k in range(1, blocks):
        new_all.append(
            lax.ppermute(own_rows, "blk", [(i, (i + k) % blocks) for i in range(blocks)])
        )
    shifted_offsets = block_offsets[(myself - block_ids) % blocks]

    page_owner = page_table // slots_dev
    owned = page_owner == myself
    page_rank = jnp.cumsum(owned.astype(jnp.int32)) - 1
    local_slot = page_table % slots_dev
    counts = jnp.sum((page_owner[None, :] == block_ids[:, None]).astype(jnp.int32), axis=1)
    per_peer = (CAP + blocks - 1) // blocks
    starts = jnp.cumsum(counts) - counts
    my_start = jnp.sum(jnp.where(block_ids == myself, starts, 0))
    peer_slots = jnp.arange(per_peer, dtype=jnp.int32)[None, :]
    wanted = (block_ids[:, None] - my_start) % blocks + peer_slots * blocks
    picked = owned[None, None, :] & (page_rank[None, None, :] == wanted[..., None])
    chosen = jnp.sum(jnp.where(picked, local_slot[None, None, :], 0), axis=2).reshape(-1)
    by_shift = chosen.reshape(blocks, per_peer)[(myself + block_ids) % blocks].reshape(-1)
    sent = kv_cache[by_shift].reshape((blocks, per_peer) + kv_cache.shape[1:])
    sent, new_all = lax.optimization_barrier((sent, new_all))
    new_all = list(new_all)
    arrived = [sent[0]]
    for k in range(1, blocks):
        arrived.append(
            lax.ppermute(sent[k], "blk", [(i, (i + k) % blocks) for i in range(blocks)])
        )
    received = jnp.stack(arrived).reshape((blocks * per_peer,) + kv_cache.shape[1:])
    arriving = (myself - starts[:, None]) % blocks + peer_slots * blocks
    present = (arriving < counts[:, None])[(myself - block_ids) % blocks].reshape(-1)
    order_rank = jnp.cumsum(present.astype(jnp.int32)) - 1
    choose = present[None, :] & (order_rank[None, :] == jnp.arange(pg, dtype=jnp.int32)[:, None])
    positions = jnp.sum(
        jnp.where(choose, jnp.arange(blocks * per_peer, dtype=jnp.int32)[None, :], 0), axis=1
    )
    own = received[positions]
    gathered = [own]
    for k in range(1, blocks):
        gathered.append(
            lax.ppermute(own, "blk", [(i, (i + k) % blocks) for i in range(blocks)])
        )

    q_rows = q_new.shape[0]
    page_len = kv_cache.shape[2]
    query_start = (my_offset * q_rows).reshape(1).astype(jnp.int32)
    key_pos = (
        jnp.repeat(shifted_offsets, q_rows) * q_rows
        + jnp.tile(jnp.arange(q_rows, dtype=jnp.int32), blocks)
    ).reshape(1, -1).astype(jnp.int32)
    page_ok = (
        jnp.arange(pg, dtype=jnp.int32)[None, :] * blocks + ((myself - block_ids) % blocks)[:, None]
        < npages
    ).reshape(-1)
    page_ok = jnp.repeat(page_ok.astype(jnp.int32), page_len).reshape(1, -1)
    return attention(
        query_start, key_pos, page_ok, q_new, new_all, gathered, group_size, head_size,
        npages % blocks != 0,
    )


def solution(mesh):
    return jax.shard_map(
        local,
        mesh=mesh,
        in_specs=(
            P(("groups", "blk"), "pool"),
            P(("groups", "blk"), "pool", None),
            P(("groups", "blk"), "pool", None, None),
            P("groups"),
            P("groups"),
        ),
        out_specs=P(("groups", "blk"), "pool"),
        check_vma=False,
    )
```

```python
import functools
import math

import jax
import jax.numpy as jnp
from jax import lax
from jax.experimental import pallas as pl
from jax.experimental.pallas import tpu as pltpu
from jax.sharding import PartitionSpec as P

CAP = 4


def attention_kernel(
    query_start, q_ref, new_ref, page_ref, key_pos_ref, page_ok_ref, acc_ref, top_ref, total_ref,
    *, head_size, group_size, mask_pages,
):
    scale = 1.0 / math.sqrt(head_size)
    q_rows = q_ref.shape[0]
    new_kv = new_ref[:, 0].reshape(-1, new_ref.shape[-1])
    page_kv = page_ref[:, 0].reshape(-1, page_ref.shape[-1])
    new_keys = new_kv[:, :head_size]
    new_values = new_kv[:, head_size:]
    page_keys = page_kv[:, :head_size]
    page_values = page_kv[:, head_size:]
    row_pos = query_start[0] + lax.broadcasted_iota(jnp.int32, (q_rows, new_kv.shape[0]), 0)
    new_visible = key_pos_ref[...] <= row_pos
    page_visible = page_ok_ref[...] > 0
    dims = (((1,), (1,)), ((), ()))
    pv = (((1,), (0,)), ((), ()))
    stack = 2 if group_size % 2 == 0 else 1
    new_visible = jnp.concatenate([new_visible] * stack, axis=0)
    for c in range(group_size // stack):
        heads = range(c * stack, (c + 1) * stack)
        queries = jnp.concatenate(
            [q_ref[:, h * head_size : (h + 1) * head_size] for h in heads], axis=0
        )
        new_scores = lax.dot_general(
            queries, new_keys, dims, preferred_element_type=jnp.float32
        ) * scale
        page_scores = lax.dot_general(
            queries, page_keys, dims, preferred_element_type=jnp.float32
        ) * scale
        new_scores = jnp.where(new_visible, new_scores, -1e30)
        if mask_pages:
            page_scores = jnp.where(page_visible, page_scores, -1e30)
        row_top = jnp.maximum(
            jnp.max(new_scores, axis=1, keepdims=True),
            jnp.max(page_scores, axis=1, keepdims=True),
        )
        new_weights = jnp.exp(new_scores - row_top)
        page_weights = jnp.exp(page_scores - row_top)
        row_total = jnp.sum(new_weights, axis=1, keepdims=True) + jnp.sum(
            page_weights, axis=1, keepdims=True
        )
        summed = lax.dot_general(
            new_weights.astype(jnp.bfloat16), new_values, pv,
            preferred_element_type=jnp.float32,
        ) + lax.dot_general(
            page_weights.astype(jnp.bfloat16), page_values, pv,
            preferred_element_type=jnp.float32,
        )
        for j, h in enumerate(heads):
            rows = slice(j * q_rows, (j + 1) * q_rows)
            acc_ref[:, h * head_size : (h + 1) * head_size] = summed[rows]
            top_ref[0, :, h : h + 1] = row_top[rows]
            total_ref[0, :, h : h + 1] = row_total[rows]


def prefix_kernel(
    q_ref, page_ref, page_ok_ref, acc_ref, top_ref, total_ref, o_ref,
    *, head_size, group_size, mask_pages,
):
    scale = 1.0 / math.sqrt(head_size)
    q_rows = q_ref.shape[0]
    page_kv = page_ref[:, 0].reshape(-1, page_ref.shape[-1])
    page_keys = page_kv[:, :head_size]
    page_values = page_kv[:, head_size:]
    page_visible = page_ok_ref[...] > 0
    dims = (((1,), (1,)), ((), ()))
    pv = (((1,), (0,)), ((), ()))
    stack = 2 if group_size % 2 == 0 else 1
    for c in range(group_size // stack):
        heads = range(c * stack, (c + 1) * stack)
        queries = jnp.concatenate(
            [q_ref[:, h * head_size : (h + 1) * head_size] for h in heads], axis=0
        )
        top_prev = jnp.concatenate([top_ref[0, :, h : h + 1] for h in heads], axis=0)
        total_prev = jnp.concatenate([total_ref[0, :, h : h + 1] for h in heads], axis=0)
        acc_prev = jnp.concatenate(
            [acc_ref[:, h * head_size : (h + 1) * head_size] for h in heads], axis=0
        )
        scores = lax.dot_general(
            queries, page_keys, dims, preferred_element_type=jnp.float32
        ) * scale
        if mask_pages:
            scores = jnp.where(page_visible, scores, -1e30)
        row_top = jnp.maximum(top_prev, jnp.max(scores, axis=1, keepdims=True))
        factor = jnp.exp(top_prev - row_top)
        weights = jnp.exp(scores - row_top)
        row_total = total_prev * factor + jnp.sum(weights, axis=1, keepdims=True)
        summed = acc_prev * factor + lax.dot_general(
            weights.astype(jnp.bfloat16), page_values, pv, preferred_element_type=jnp.float32
        )
        result = (summed / row_total).astype(o_ref.dtype)
        for j, h in enumerate(heads):
            o_ref[:, h * head_size : (h + 1) * head_size] = result[j * q_rows : (j + 1) * q_rows]


def prefix_part(page_ok, q_new, pages, acc, top, total, group_size, head_size, mask_pages):
    q_rows = q_new.shape[0]
    npage, kv_heads, page_len, width = pages.shape
    kernel = functools.partial(
        prefix_kernel, head_size=head_size, group_size=group_size, mask_pages=mask_pages
    )
    span = group_size * head_size
    block = pl.BlockSpec((q_rows, span), lambda g: (0, g))
    stat_spec = pl.BlockSpec((1, q_rows, group_size), lambda g: (g, 0, 0))
    return pl.pallas_call(
        kernel,
        out_shape=jax.ShapeDtypeStruct(q_new.shape, q_new.dtype),
        grid=(kv_heads,),
        in_specs=[
            block,
            pl.BlockSpec((npage, 1, page_len, width), lambda g: (0, g, 0, 0)),
            pl.BlockSpec((1, npage * page_len), lambda g: (0, 0)),
            block,
            stat_spec,
            stat_spec,
        ],
        out_specs=block,
    )(q_new, pages, page_ok, acc, top, total)


def attention(query_start, key_pos, page_ok, q_new, new_all, pages, group_size, head_size,
              mask_pages):
    q_rows = q_new.shape[0]
    blocks, kv_heads, new_len, width = new_all.shape
    npage, _, page_len, _ = pages.shape
    kernel = functools.partial(
        attention_kernel, head_size=head_size, group_size=group_size, mask_pages=mask_pages
    )
    span = group_size * head_size
    stat = jax.ShapeDtypeStruct((kv_heads, q_rows, group_size), jnp.float32)
    stat_spec = pl.BlockSpec((1, q_rows, group_size), lambda g, s: (g, 0, 0))
    return pl.pallas_call(
        kernel,
        out_shape=(jax.ShapeDtypeStruct(q_new.shape, jnp.float32), stat, stat),
        grid_spec=pltpu.PrefetchScalarGridSpec(
            num_scalar_prefetch=1,
            grid=(kv_heads,),
            in_specs=[
                pl.BlockSpec((q_rows, span), lambda g, s: (0, g)),
                pl.BlockSpec((blocks, 1, new_len, width), lambda g, s: (0, g, 0, 0)),
                pl.BlockSpec((npage, 1, page_len, width), lambda g, s: (0, g, 0, 0)),
                pl.BlockSpec((1, blocks * new_len), lambda g, s: (0, 0)),
                pl.BlockSpec((1, npage * page_len), lambda g, s: (0, 0)),
            ],
            out_specs=(pl.BlockSpec((q_rows, span), lambda g, s: (0, g)), stat_spec, stat_spec),
        ),
    )(query_start, q_new, new_all, pages, key_pos, page_ok)


def local(q_new, kv_new, kv_cache, page_table, block_offsets):
    kv_heads = kv_new.shape[1]
    head_size = kv_new.shape[2] // 2
    group_size = q_new.shape[1] // (head_size * kv_heads)
    slots_dev = kv_cache.shape[0]
    npages = page_table.shape[0]
    blocks = lax.axis_size("blk")
    myself = lax.axis_index("blk")
    pg = -(-npages // blocks)
    block_ids = jnp.arange(blocks, dtype=jnp.int32)
    my_offset = jnp.sum(jnp.where(block_ids == myself, block_offsets, 0))

    own_rows = kv_new.transpose(1, 0, 2)
    new_all = [own_rows]
    for k in range(1, blocks):
        new_all.append(
            lax.ppermute(own_rows, "blk", [(i, (i + k) % blocks) for i in range(blocks)])
        )
    shifted_offsets = block_offsets[(myself - block_ids) % blocks]

    page_owner = page_table // slots_dev
    owned = page_owner == myself
    page_rank = jnp.cumsum(owned.astype(jnp.int32)) - 1
    local_slot = page_table % slots_dev
    counts = jnp.sum((page_owner[None, :] == block_ids[:, None]).astype(jnp.int32), axis=1)
    per_peer = (CAP + blocks - 1) // blocks
    starts = jnp.cumsum(counts) - counts
    my_start = jnp.sum(jnp.where(block_ids == myself, starts, 0))
    peer_slots = jnp.arange(per_peer, dtype=jnp.int32)[None, :]
    wanted = (block_ids[:, None] - my_start) % blocks + peer_slots * blocks
    picked = owned[None, None, :] & (page_rank[None, None, :] == wanted[..., None])
    chosen = jnp.sum(jnp.where(picked, local_slot[None, None, :], 0), axis=2).reshape(-1)
    by_shift = chosen.reshape(blocks, per_peer)[(myself + block_ids) % blocks].reshape(-1)
    sent = kv_cache[by_shift].reshape((blocks, per_peer) + kv_cache.shape[1:])
    sent, new_all = lax.optimization_barrier((sent, new_all))
    new_all = jnp.stack(new_all)
    arrived = [sent[0]]
    for k in range(1, blocks):
        arrived.append(
            lax.ppermute(sent[k], "blk", [(i, (i + k) % blocks) for i in range(blocks)])
        )
    received = jnp.stack(arrived).reshape((blocks * per_peer,) + kv_cache.shape[1:])
    arriving = (myself - starts[:, None]) % blocks + peer_slots * blocks
    present = (arriving < counts[:, None])[(myself - block_ids) % blocks].reshape(-1)
    order_rank = jnp.cumsum(present.astype(jnp.int32)) - 1
    choose = present[None, :] & (order_rank[None, :] == jnp.arange(pg, dtype=jnp.int32)[:, None])
    positions = jnp.sum(
        jnp.where(choose, jnp.arange(blocks * per_peer, dtype=jnp.int32)[None, :], 0), axis=1
    )
    own = received[positions]
    gathered = [own]
    for k in range(1, blocks):
        gathered.append(
            lax.ppermute(own, "blk", [(i, (i + k) % blocks) for i in range(blocks)])
        )
    others = jnp.concatenate(gathered[1:])

    q_rows = q_new.shape[0]
    page_len = kv_cache.shape[2]
    query_start = (my_offset * q_rows).reshape(1).astype(jnp.int32)
    key_pos = (
        jnp.repeat(shifted_offsets, q_rows) * q_rows
        + jnp.tile(jnp.arange(q_rows, dtype=jnp.int32), blocks)
    ).reshape(1, -1).astype(jnp.int32)
    slot_ids = jnp.arange(pg, dtype=jnp.int32)
    page_ok = slot_ids[None, :] * blocks + ((myself - block_ids) % blocks)[:, None] < npages
    page_ok = jnp.repeat(page_ok.astype(jnp.int32).reshape(-1), page_len).reshape(1, -1)
    own_ok = page_ok[:, : pg * page_len]
    others_ok = page_ok[:, pg * page_len :]
    ragged = npages % blocks != 0
    acc, top, total = attention(
        query_start, key_pos, own_ok, q_new, new_all, own, group_size, head_size, ragged
    )
    return prefix_part(others_ok, q_new, others, acc, top, total, group_size, head_size, ragged)


def solution(mesh):
    return jax.shard_map(
        local,
        mesh=mesh,
        in_specs=(
            P(("groups", "blk"), "pool"),
            P(("groups", "blk"), "pool", None),
            P(("groups", "blk"), "pool", None, None),
            P("groups"),
            P("groups"),
        ),
        out_specs=P(("groups", "blk"), "pool"),
        check_vma=False,
    )
```

```python
import functools
import math

import jax
import jax.numpy as jnp
from jax import lax
from jax.experimental import pallas as pl
from jax.experimental.pallas import tpu as pltpu
from jax.sharding import PartitionSpec as P

CAP = 4


def attention_kernel(
    query_start, q_ref, new_ref, page_ref, key_pos_ref, page_ok_ref, acc_ref, top_ref, total_ref,
    *, head_size, group_size, mask_pages,
):
    scale = 1.0 / math.sqrt(head_size)
    q_rows = q_ref.shape[0]
    new_kv = new_ref[:, 0].reshape(-1, new_ref.shape[-1])
    page_kv = page_ref[:, 0].reshape(-1, page_ref.shape[-1])
    new_keys = new_kv[:, :head_size]
    new_values = new_kv[:, head_size:]
    page_keys = page_kv[:, :head_size]
    page_values = page_kv[:, head_size:]
    row_pos = query_start[0] + lax.broadcasted_iota(jnp.int32, (q_rows, new_kv.shape[0]), 0)
    new_visible = key_pos_ref[...] <= row_pos
    page_visible = page_ok_ref[...] > 0
    dims = (((1,), (1,)), ((), ()))
    pv = (((1,), (0,)), ((), ()))
    stack = 2 if group_size % 2 == 0 else 1
    new_visible = jnp.concatenate([new_visible] * stack, axis=0)
    for c in range(group_size // stack):
        heads = range(c * stack, (c + 1) * stack)
        queries = jnp.concatenate(
            [q_ref[:, h * head_size : (h + 1) * head_size] for h in heads], axis=0
        )
        new_scores = lax.dot_general(
            queries, new_keys, dims, preferred_element_type=jnp.float32
        ) * scale
        page_scores = lax.dot_general(
            queries, page_keys, dims, preferred_element_type=jnp.float32
        ) * scale
        new_scores = jnp.where(new_visible, new_scores, -1e30)
        if mask_pages:
            page_scores = jnp.where(page_visible, page_scores, -1e30)
        row_top = jnp.maximum(
            jnp.max(new_scores, axis=1, keepdims=True),
            jnp.max(page_scores, axis=1, keepdims=True),
        )
        new_weights = jnp.exp(new_scores - row_top)
        page_weights = jnp.exp(page_scores - row_top)
        row_total = jnp.sum(new_weights, axis=1, keepdims=True) + jnp.sum(
            page_weights, axis=1, keepdims=True
        )
        summed = lax.dot_general(
            new_weights.astype(jnp.bfloat16), new_values, pv,
            preferred_element_type=jnp.float32,
        ) + lax.dot_general(
            page_weights.astype(jnp.bfloat16), page_values, pv,
            preferred_element_type=jnp.float32,
        )
        for j, h in enumerate(heads):
            rows = slice(j * q_rows, (j + 1) * q_rows)
            acc_ref[:, h * head_size : (h + 1) * head_size] = summed[rows]
            top_ref[0, :, h : h + 1] = row_top[rows]
            total_ref[0, :, h : h + 1] = row_total[rows]


def prefix_kernel(
    q_ref, page_ref, page_ok_ref, acc_ref, top_ref, total_ref, *out_refs,
    head_size, group_size, mask_pages, final,
):
    scale = 1.0 / math.sqrt(head_size)
    q_rows = q_ref.shape[0]
    page_kv = page_ref[:, 0].reshape(-1, page_ref.shape[-1])
    page_keys = page_kv[:, :head_size]
    page_values = page_kv[:, head_size:]
    page_visible = page_ok_ref[...] > 0
    dims = (((1,), (1,)), ((), ()))
    pv = (((1,), (0,)), ((), ()))
    stack = 2 if group_size % 2 == 0 else 1
    for c in range(group_size // stack):
        heads = range(c * stack, (c + 1) * stack)
        queries = jnp.concatenate(
            [q_ref[:, h * head_size : (h + 1) * head_size] for h in heads], axis=0
        )
        top_prev = jnp.concatenate([top_ref[0, :, h : h + 1] for h in heads], axis=0)
        total_prev = jnp.concatenate([total_ref[0, :, h : h + 1] for h in heads], axis=0)
        acc_prev = jnp.concatenate(
            [acc_ref[:, h * head_size : (h + 1) * head_size] for h in heads], axis=0
        )
        scores = lax.dot_general(
            queries, page_keys, dims, preferred_element_type=jnp.float32
        ) * scale
        if mask_pages:
            scores = jnp.where(page_visible, scores, -1e30)
        row_top = jnp.maximum(top_prev, jnp.max(scores, axis=1, keepdims=True))
        factor = jnp.exp(top_prev - row_top)
        weights = jnp.exp(scores - row_top)
        row_total = total_prev * factor + jnp.sum(weights, axis=1, keepdims=True)
        summed = acc_prev * factor + lax.dot_general(
            weights.astype(jnp.bfloat16), page_values, pv, preferred_element_type=jnp.float32
        )
        for j, h in enumerate(heads):
            rows = slice(j * q_rows, (j + 1) * q_rows)
            cols = slice(h * head_size, (h + 1) * head_size)
            if final:
                out_refs[0][:, cols] = (summed[rows] / row_total[rows]).astype(out_refs[0].dtype)
            else:
                out_refs[0][:, cols] = summed[rows]
                out_refs[1][0, :, h : h + 1] = row_top[rows]
                out_refs[2][0, :, h : h + 1] = row_total[rows]


def prefix_part(page_ok, q_new, pages, acc, top, total, group_size, head_size, mask_pages,
                final=True):
    q_rows = q_new.shape[0]
    npage, kv_heads, page_len, width = pages.shape
    kernel = functools.partial(
        prefix_kernel, head_size=head_size, group_size=group_size, mask_pages=mask_pages,
        final=final,
    )
    span = group_size * head_size
    block = pl.BlockSpec((q_rows, span), lambda g: (0, g))
    stat_spec = pl.BlockSpec((1, q_rows, group_size), lambda g: (g, 0, 0))
    if final:
        out_shape = jax.ShapeDtypeStruct(q_new.shape, q_new.dtype)
        out_specs = block
    else:
        stat = jax.ShapeDtypeStruct(top.shape, jnp.float32)
        out_shape = (jax.ShapeDtypeStruct(q_new.shape, jnp.float32), stat, stat)
        out_specs = (block, stat_spec, stat_spec)
    rows = q_new.shape[0] * q_new.shape[1] // head_size
    keys = npage * page_len
    cost = pl.CostEstimate(
        flops=4 * rows * keys * head_size,
        transcendentals=rows * keys,
        bytes_accessed=q_new.size * 2 + pages.size * 2 + acc.size * 8,
    )
    return pl.pallas_call(
        kernel,
        out_shape=out_shape,
        cost_estimate=cost,
        grid=(kv_heads,),
        in_specs=[
            block,
            pl.BlockSpec((npage, 1, page_len, width), lambda g: (0, g, 0, 0)),
            pl.BlockSpec((1, npage * page_len), lambda g: (0, 0)),
            block,
            stat_spec,
            stat_spec,
        ],
        out_specs=out_specs,
    )(q_new, pages, page_ok, acc, top, total)


def attention(query_start, key_pos, page_ok, q_new, new_all, pages, group_size, head_size,
              mask_pages):
    q_rows = q_new.shape[0]
    blocks, kv_heads, new_len, width = new_all.shape
    npage, _, page_len, _ = pages.shape
    kernel = functools.partial(
        attention_kernel, head_size=head_size, group_size=group_size, mask_pages=mask_pages
    )
    span = group_size * head_size
    stat = jax.ShapeDtypeStruct((kv_heads, q_rows, group_size), jnp.float32)
    stat_spec = pl.BlockSpec((1, q_rows, group_size), lambda g, s: (g, 0, 0))
    return pl.pallas_call(
        kernel,
        out_shape=(jax.ShapeDtypeStruct(q_new.shape, jnp.float32), stat, stat),
        grid_spec=pltpu.PrefetchScalarGridSpec(
            num_scalar_prefetch=1,
            grid=(kv_heads,),
            in_specs=[
                pl.BlockSpec((q_rows, span), lambda g, s: (0, g)),
                pl.BlockSpec((blocks, 1, new_len, width), lambda g, s: (0, g, 0, 0)),
                pl.BlockSpec((npage, 1, page_len, width), lambda g, s: (0, g, 0, 0)),
                pl.BlockSpec((1, blocks * new_len), lambda g, s: (0, 0)),
                pl.BlockSpec((1, npage * page_len), lambda g, s: (0, 0)),
            ],
            out_specs=(pl.BlockSpec((q_rows, span), lambda g, s: (0, g)), stat_spec, stat_spec),
        ),
    )(query_start, q_new, new_all, pages, key_pos, page_ok)


def local(q_new, kv_new, kv_cache, page_table, block_offsets):
    kv_heads = kv_new.shape[1]
    head_size = kv_new.shape[2] // 2
    group_size = q_new.shape[1] // (head_size * kv_heads)
    slots_dev = kv_cache.shape[0]
    npages = page_table.shape[0]
    blocks = lax.axis_size("blk")
    myself = lax.axis_index("blk")
    pg = -(-npages // blocks)
    block_ids = jnp.arange(blocks, dtype=jnp.int32)
    my_offset = jnp.sum(jnp.where(block_ids == myself, block_offsets, 0))

    own_rows = kv_new.transpose(1, 0, 2)
    new_all = [own_rows]
    for k in range(1, blocks):
        new_all.append(
            lax.ppermute(own_rows, "blk", [(i, (i + k) % blocks) for i in range(blocks)])
        )
    shifted_offsets = block_offsets[(myself - block_ids) % blocks]

    page_owner = page_table // slots_dev
    owned = page_owner == myself
    page_rank = jnp.cumsum(owned.astype(jnp.int32)) - 1
    local_slot = page_table % slots_dev
    counts = jnp.sum((page_owner[None, :] == block_ids[:, None]).astype(jnp.int32), axis=1)
    per_peer = (CAP + blocks - 1) // blocks
    starts = jnp.cumsum(counts) - counts
    my_start = jnp.sum(jnp.where(block_ids == myself, starts, 0))
    peer_slots = jnp.arange(per_peer, dtype=jnp.int32)[None, :]
    wanted = (block_ids[:, None] - my_start) % blocks + peer_slots * blocks
    picked = owned[None, None, :] & (page_rank[None, None, :] == wanted[..., None])
    chosen = jnp.sum(jnp.where(picked, local_slot[None, None, :], 0), axis=2).reshape(-1)
    by_shift = chosen.reshape(blocks, per_peer)[(myself + block_ids) % blocks].reshape(-1)
    sent = kv_cache[by_shift].reshape((blocks, per_peer) + kv_cache.shape[1:])
    sent, new_all = lax.optimization_barrier((sent, new_all))
    new_all = jnp.stack(new_all)
    arrived = [sent[0]]
    for k in range(1, blocks):
        arrived.append(
            lax.ppermute(sent[k], "blk", [(i, (i + k) % blocks) for i in range(blocks)])
        )
    received = jnp.stack(arrived).reshape((blocks * per_peer,) + kv_cache.shape[1:])
    arriving = (myself - starts[:, None]) % blocks + peer_slots * blocks
    present = (arriving < counts[:, None])[(myself - block_ids) % blocks].reshape(-1)
    order_rank = jnp.cumsum(present.astype(jnp.int32)) - 1
    choose = present[None, :] & (order_rank[None, :] == jnp.arange(pg, dtype=jnp.int32)[:, None])
    positions = jnp.sum(
        jnp.where(choose, jnp.arange(blocks * per_peer, dtype=jnp.int32)[None, :], 0), axis=1
    )
    own = received[positions]
    gathered = [own]
    for k in range(1, blocks):
        gathered.append(
            lax.ppermute(own, "blk", [(i, (i + k) % blocks) for i in range(blocks)])
        )
    later = blocks > 2

    q_rows = q_new.shape[0]
    page_len = kv_cache.shape[2]
    query_start = (my_offset * q_rows).reshape(1).astype(jnp.int32)
    key_pos = (
        jnp.repeat(shifted_offsets, q_rows) * q_rows
        + jnp.tile(jnp.arange(q_rows, dtype=jnp.int32), blocks)
    ).reshape(1, -1).astype(jnp.int32)
    slot_ids = jnp.arange(pg, dtype=jnp.int32)
    page_ok = slot_ids[None, :] * blocks + ((myself - block_ids) % blocks)[:, None] < npages
    page_ok = jnp.repeat(page_ok.astype(jnp.int32).reshape(-1), page_len).reshape(1, -1)
    own_ok = page_ok[:, : pg * page_len]
    first_ok = page_ok[:, pg * page_len : 2 * pg * page_len]
    later_ok = page_ok[:, 2 * pg * page_len :]
    ragged = npages % blocks != 0
    acc, top, total = attention(
        query_start, key_pos, own_ok, q_new, new_all, own, group_size, head_size, ragged
    )
    if not later:
        return prefix_part(
            first_ok, q_new, gathered[1], acc, top, total, group_size, head_size, ragged
        )
    acc, top, total = prefix_part(
        first_ok, q_new, gathered[1], acc, top, total, group_size, head_size, ragged, False
    )
    acc, top, total, farther = lax.optimization_barrier((acc, top, total, gathered[2:]))
    later = jnp.concatenate(farther)
    return prefix_part(later_ok, q_new, later, acc, top, total, group_size, head_size, ragged)


def solution(mesh):
    return jax.shard_map(
        local,
        mesh=mesh,
        in_specs=(
            P(("groups", "blk"), "pool"),
            P(("groups", "blk"), "pool", None),
            P(("groups", "blk"), "pool", None, None),
            P("groups"),
            P("groups"),
        ),
        out_specs=P(("groups", "blk"), "pool"),
        check_vma=False,
    )
```

```python
import functools
import math

import jax
import jax.numpy as jnp
from jax import lax
from jax.experimental import pallas as pl
from jax.experimental.pallas import tpu as pltpu
from jax.sharding import PartitionSpec as P

CAP = 4


def attention_kernel(
    query_start, q_ref, new_ref, page_ref, key_pos_ref, page_ok_ref, acc_ref, top_ref, total_ref,
    *, head_size, group_size, mask_pages,
):
    scale = 1.0 / math.sqrt(head_size)
    q_rows = q_ref.shape[0]
    new_kv = new_ref[:, 0].reshape(-1, new_ref.shape[-1])
    page_kv = page_ref[:, 0].reshape(-1, page_ref.shape[-1])
    new_keys = new_kv[:, :head_size]
    new_values = new_kv[:, head_size:]
    page_keys = page_kv[:, :head_size]
    page_values = page_kv[:, head_size:]
    row_pos = query_start[0] + lax.broadcasted_iota(jnp.int32, (q_rows, new_kv.shape[0]), 0)
    new_visible = key_pos_ref[...] <= row_pos
    page_visible = page_ok_ref[...] > 0
    dims = (((1,), (1,)), ((), ()))
    pv = (((1,), (0,)), ((), ()))
    stack = 2 if group_size % 2 == 0 else 1
    new_visible = jnp.concatenate([new_visible] * stack, axis=0)
    for c in range(group_size // stack):
        heads = range(c * stack, (c + 1) * stack)
        queries = jnp.concatenate(
            [q_ref[:, h * head_size : (h + 1) * head_size] for h in heads], axis=0
        )
        new_scores = lax.dot_general(
            queries, new_keys, dims, preferred_element_type=jnp.float32
        ) * scale
        page_scores = lax.dot_general(
            queries, page_keys, dims, preferred_element_type=jnp.float32
        ) * scale
        new_scores = jnp.where(new_visible, new_scores, -1e30)
        if mask_pages:
            page_scores = jnp.where(page_visible, page_scores, -1e30)
        row_top = jnp.maximum(
            jnp.max(new_scores, axis=1, keepdims=True),
            jnp.max(page_scores, axis=1, keepdims=True),
        )
        new_weights = jnp.exp(new_scores - row_top)
        page_weights = jnp.exp(page_scores - row_top)
        row_total = jnp.sum(new_weights, axis=1, keepdims=True) + jnp.sum(
            page_weights, axis=1, keepdims=True
        )
        summed = lax.dot_general(
            new_weights.astype(jnp.bfloat16), new_values, pv,
            preferred_element_type=jnp.float32,
        ) + lax.dot_general(
            page_weights.astype(jnp.bfloat16), page_values, pv,
            preferred_element_type=jnp.float32,
        )
        for j, h in enumerate(heads):
            rows = slice(j * q_rows, (j + 1) * q_rows)
            acc_ref[:, h * head_size : (h + 1) * head_size] = summed[rows]
            top_ref[0, :, h : h + 1] = row_top[rows]
            total_ref[0, :, h : h + 1] = row_total[rows]


def prefix_kernel(
    q_ref, page_ref, page_ok_ref, acc_ref, top_ref, total_ref, *out_refs,
    head_size, group_size, mask_pages, final,
):
    scale = 1.0 / math.sqrt(head_size)
    q_rows = q_ref.shape[0]
    page_kv = page_ref[:, 0].reshape(-1, page_ref.shape[-1])
    page_keys = page_kv[:, :head_size]
    page_values = page_kv[:, head_size:]
    page_visible = page_ok_ref[...] > 0
    dims = (((1,), (1,)), ((), ()))
    pv = (((1,), (0,)), ((), ()))
    stack = 2 if group_size % 2 == 0 else 1
    for c in range(group_size // stack):
        heads = range(c * stack, (c + 1) * stack)
        queries = jnp.concatenate(
            [q_ref[:, h * head_size : (h + 1) * head_size] for h in heads], axis=0
        )
        top_prev = jnp.concatenate([top_ref[0, :, h : h + 1] for h in heads], axis=0)
        total_prev = jnp.concatenate([total_ref[0, :, h : h + 1] for h in heads], axis=0)
        acc_prev = jnp.concatenate(
            [acc_ref[:, h * head_size : (h + 1) * head_size] for h in heads], axis=0
        )
        scores = lax.dot_general(
            queries, page_keys, dims, preferred_element_type=jnp.float32
        ) * scale
        if mask_pages:
            scores = jnp.where(page_visible, scores, -1e30)
        row_top = jnp.maximum(top_prev, jnp.max(scores, axis=1, keepdims=True))
        factor = jnp.exp(top_prev - row_top)
        weights = jnp.exp(scores - row_top)
        row_total = total_prev * factor + jnp.sum(weights, axis=1, keepdims=True)
        summed = acc_prev * factor + lax.dot_general(
            weights.astype(jnp.bfloat16), page_values, pv, preferred_element_type=jnp.float32
        )
        for j, h in enumerate(heads):
            rows = slice(j * q_rows, (j + 1) * q_rows)
            cols = slice(h * head_size, (h + 1) * head_size)
            if final:
                out_refs[0][:, cols] = (summed[rows] / row_total[rows]).astype(out_refs[0].dtype)
            else:
                out_refs[0][:, cols] = summed[rows]
                out_refs[1][0, :, h : h + 1] = row_top[rows]
                out_refs[2][0, :, h : h + 1] = row_total[rows]


def prefix_part(page_ok, q_new, pages, acc, top, total, group_size, head_size, mask_pages,
                final=True):
    q_rows = q_new.shape[0]
    npage, kv_heads, page_len, width = pages.shape
    kernel = functools.partial(
        prefix_kernel, head_size=head_size, group_size=group_size, mask_pages=mask_pages,
        final=final,
    )
    span = group_size * head_size
    block = pl.BlockSpec((q_rows, span), lambda g: (0, g))
    stat_spec = pl.BlockSpec((1, q_rows, group_size), lambda g: (g, 0, 0))
    if final:
        out_shape = jax.ShapeDtypeStruct(q_new.shape, q_new.dtype)
        out_specs = block
    else:
        stat = jax.ShapeDtypeStruct(top.shape, jnp.float32)
        out_shape = (jax.ShapeDtypeStruct(q_new.shape, jnp.float32), stat, stat)
        out_specs = (block, stat_spec, stat_spec)
    rows = q_new.shape[0] * q_new.shape[1] // head_size
    keys = npage * page_len
    cost = pl.CostEstimate(
        flops=4 * rows * keys * head_size,
        transcendentals=rows * keys,
        bytes_accessed=q_new.size * 2 + pages.size * 2 + acc.size * 8,
    )
    return pl.pallas_call(
        kernel,
        out_shape=out_shape,
        cost_estimate=cost,
        grid=(kv_heads,),
        in_specs=[
            block,
            pl.BlockSpec((npage, 1, page_len, width), lambda g: (0, g, 0, 0)),
            pl.BlockSpec((1, npage * page_len), lambda g: (0, 0)),
            block,
            stat_spec,
            stat_spec,
        ],
        out_specs=out_specs,
    )(q_new, pages, page_ok, acc, top, total)


def attention(query_start, key_pos, page_ok, q_new, new_all, pages, group_size, head_size,
              mask_pages):
    q_rows = q_new.shape[0]
    blocks, kv_heads, new_len, width = new_all.shape
    npage, _, page_len, _ = pages.shape
    kernel = functools.partial(
        attention_kernel, head_size=head_size, group_size=group_size, mask_pages=mask_pages
    )
    span = group_size * head_size
    stat = jax.ShapeDtypeStruct((kv_heads, q_rows, group_size), jnp.float32)
    stat_spec = pl.BlockSpec((1, q_rows, group_size), lambda g, s: (g, 0, 0))
    return pl.pallas_call(
        kernel,
        out_shape=(jax.ShapeDtypeStruct(q_new.shape, jnp.float32), stat, stat),
        grid_spec=pltpu.PrefetchScalarGridSpec(
            num_scalar_prefetch=1,
            grid=(kv_heads,),
            in_specs=[
                pl.BlockSpec((q_rows, span), lambda g, s: (0, g)),
                pl.BlockSpec((blocks, 1, new_len, width), lambda g, s: (0, g, 0, 0)),
                pl.BlockSpec((npage, 1, page_len, width), lambda g, s: (0, g, 0, 0)),
                pl.BlockSpec((1, blocks * new_len), lambda g, s: (0, 0)),
                pl.BlockSpec((1, npage * page_len), lambda g, s: (0, 0)),
            ],
            out_specs=(pl.BlockSpec((q_rows, span), lambda g, s: (0, g)), stat_spec, stat_spec),
        ),
    )(query_start, q_new, new_all, pages, key_pos, page_ok)


def local(q_new, kv_new, kv_cache, page_table, block_offsets):
    kv_heads = kv_new.shape[1]
    head_size = kv_new.shape[2] // 2
    group_size = q_new.shape[1] // (head_size * kv_heads)
    slots_dev = kv_cache.shape[0]
    npages = page_table.shape[0]
    blocks = lax.axis_size("blk")
    myself = lax.axis_index("blk")
    pg = -(-npages // blocks)
    block_ids = jnp.arange(blocks, dtype=jnp.int32)
    my_offset = jnp.sum(jnp.where(block_ids == myself, block_offsets, 0))

    own_rows = kv_new.transpose(1, 0, 2)
    new_all = [own_rows]
    for k in range(1, blocks):
        new_all.append(
            lax.ppermute(own_rows, "blk", [(i, (i + k) % blocks) for i in range(blocks)])
        )
    shifted_offsets = block_offsets[(myself - block_ids) % blocks]

    page_owner = page_table // slots_dev
    owned = page_owner == myself
    local_slot = page_table % slots_dev
    per_peer = (CAP + blocks - 1) // blocks
    page_ids = jnp.arange(npages, dtype=jnp.int32)
    page_rank = jnp.sum(
        ((page_ids[None, :] < page_ids[:, None]) & owned[None, :]).astype(jnp.int32), axis=1
    )
    my_start = jnp.sum((page_owner < myself).astype(jnp.int32))
    peer_slots = jnp.arange(per_peer, dtype=jnp.int32)[None, :]
    wanted = (myself + block_ids[:, None] - my_start) % blocks + peer_slots * blocks
    picked = owned[None, None, :] & (page_rank[None, None, :] == wanted[..., None])
    by_shift = jnp.sum(jnp.where(picked, local_slot[None, None, :], 0), axis=2).reshape(-1)
    sent = jnp.stack(
        [lax.dynamic_index_in_dim(kv_cache, by_shift[i], keepdims=False)
         for i in range(blocks * per_peer)]
    ).reshape((blocks, per_peer) + kv_cache.shape[1:])
    sent, new_all = lax.optimization_barrier((sent, new_all))
    new_all = jnp.stack(new_all)
    arrived = [sent[0]]
    for k in range(1, blocks):
        arrived.append(
            lax.ppermute(sent[k], "blk", [(i, (i + k) % blocks) for i in range(blocks)])
        )
    received = jnp.stack(arrived).reshape((blocks * per_peer,) + kv_cache.shape[1:])
    source = (myself - block_ids) % blocks
    counts = jnp.sum((page_owner[None, :] == source[:, None]).astype(jnp.int32), axis=1)
    starts = jnp.sum((page_owner[None, :] < source[:, None]).astype(jnp.int32), axis=1)
    arriving = (myself - starts[:, None]) % blocks + peer_slots * blocks
    present = (arriving < counts[:, None]).reshape(-1)
    chunk_ids = jnp.arange(blocks * per_peer, dtype=jnp.int32)
    order_rank = jnp.sum(
        ((chunk_ids[None, :] < chunk_ids[:, None]) & present[None, :]).astype(jnp.int32), axis=1
    )
    choose = present[None, :] & (order_rank[None, :] == jnp.arange(pg, dtype=jnp.int32)[:, None])
    positions = jnp.sum(jnp.where(choose, chunk_ids[None, :], 0), axis=1)
    own = jnp.stack(
        [lax.dynamic_index_in_dim(received, positions[i], keepdims=False) for i in range(pg)]
    )
    gathered = [own]
    for k in range(1, blocks):
        gathered.append(
            lax.ppermute(own, "blk", [(i, (i + k) % blocks) for i in range(blocks)])
        )
    later = blocks > 2

    q_rows = q_new.shape[0]
    page_len = kv_cache.shape[2]
    query_start = (my_offset * q_rows).reshape(1).astype(jnp.int32)
    key_pos = (
        jnp.repeat(shifted_offsets, q_rows) * q_rows
        + jnp.tile(jnp.arange(q_rows, dtype=jnp.int32), blocks)
    ).reshape(1, -1).astype(jnp.int32)
    slot_ids = jnp.arange(pg, dtype=jnp.int32)
    page_ok = slot_ids[None, :] * blocks + ((myself - block_ids) % blocks)[:, None] < npages
    page_ok = jnp.repeat(page_ok.astype(jnp.int32).reshape(-1), page_len).reshape(1, -1)
    own_ok = page_ok[:, : pg * page_len]
    first_ok = page_ok[:, pg * page_len : 2 * pg * page_len]
    later_ok = page_ok[:, 2 * pg * page_len :]
    ragged = npages % blocks != 0
    acc, top, total = attention(
        query_start, key_pos, own_ok, q_new, new_all, own, group_size, head_size, ragged
    )
    if not later:
        return prefix_part(
            first_ok, q_new, gathered[1], acc, top, total, group_size, head_size, ragged
        )
    acc, top, total = prefix_part(
        first_ok, q_new, gathered[1], acc, top, total, group_size, head_size, ragged, False
    )
    acc, top, total, farther = lax.optimization_barrier((acc, top, total, gathered[2:]))
    later = jnp.concatenate(farther)
    return prefix_part(later_ok, q_new, later, acc, top, total, group_size, head_size, ragged)


def solution(mesh):
    return jax.shard_map(
        local,
        mesh=mesh,
        in_specs=(
            P(("groups", "blk"), "pool"),
            P(("groups", "blk"), "pool", None),
            P(("groups", "blk"), "pool", None, None),
            P("groups"),
            P("groups"),
        ),
        out_specs=P(("groups", "blk"), "pool"),
        check_vma=False,
    )
```

```python
import functools
import math

import jax
import jax.numpy as jnp
from jax import lax
from jax.experimental import pallas as pl
from jax.experimental.pallas import tpu as pltpu
from jax.sharding import PartitionSpec as P

CAP = 4


def attention_kernel(
    query_start, q_ref, new_ref, page_ref, key_pos_ref, page_ok_ref, acc_ref, top_ref, total_ref,
    *, head_size, group_size, mask_pages,
):
    scale = 1.0 / math.sqrt(head_size)
    q_rows = q_ref.shape[0]
    new_kv = new_ref[:, 0].reshape(-1, new_ref.shape[-1])
    page_kv = page_ref[:, 0].reshape(-1, page_ref.shape[-1])
    new_keys = new_kv[:, :head_size]
    new_values = new_kv[:, head_size:]
    page_keys = page_kv[:, :head_size]
    page_values = page_kv[:, head_size:]
    row_pos = query_start[0] + lax.broadcasted_iota(jnp.int32, (q_rows, new_kv.shape[0]), 0)
    new_visible = key_pos_ref[...] <= row_pos
    page_visible = page_ok_ref[...] > 0
    dims = (((1,), (1,)), ((), ()))
    pv = (((1,), (0,)), ((), ()))
    stack = 2 if group_size % 2 == 0 else 1
    new_visible = jnp.concatenate([new_visible] * stack, axis=0)
    for c in range(group_size // stack):
        heads = range(c * stack, (c + 1) * stack)
        queries = jnp.concatenate(
            [q_ref[:, h * head_size : (h + 1) * head_size] for h in heads], axis=0
        )
        new_scores = lax.dot_general(
            queries, new_keys, dims, preferred_element_type=jnp.float32
        ) * scale
        page_scores = lax.dot_general(
            queries, page_keys, dims, preferred_element_type=jnp.float32
        ) * scale
        new_scores = jnp.where(new_visible, new_scores, -1e30)
        if mask_pages:
            page_scores = jnp.where(page_visible, page_scores, -1e30)
        row_top = jnp.maximum(
            jnp.max(new_scores, axis=1, keepdims=True),
            jnp.max(page_scores, axis=1, keepdims=True),
        )
        new_weights = jnp.exp(new_scores - row_top)
        page_weights = jnp.exp(page_scores - row_top)
        row_total = jnp.sum(new_weights, axis=1, keepdims=True) + jnp.sum(
            page_weights, axis=1, keepdims=True
        )
        summed = lax.dot_general(
            new_weights.astype(jnp.bfloat16), new_values, pv,
            preferred_element_type=jnp.float32,
        ) + lax.dot_general(
            page_weights.astype(jnp.bfloat16), page_values, pv,
            preferred_element_type=jnp.float32,
        )
        for j, h in enumerate(heads):
            rows = slice(j * q_rows, (j + 1) * q_rows)
            acc_ref[:, h * head_size : (h + 1) * head_size] = summed[rows]
            top_ref[0, :, h : h + 1] = row_top[rows]
            total_ref[0, :, h : h + 1] = row_total[rows]


def prefix_kernel(
    q_ref, page_ref, page_ok_ref, acc_ref, top_ref, total_ref, *out_refs,
    head_size, group_size, mask_pages, final,
):
    scale = 1.0 / math.sqrt(head_size)
    q_rows = q_ref.shape[0]
    page_kv = page_ref[:, 0].reshape(-1, page_ref.shape[-1])
    page_keys = page_kv[:, :head_size]
    page_values = page_kv[:, head_size:]
    page_visible = page_ok_ref[...] > 0
    dims = (((1,), (1,)), ((), ()))
    pv = (((1,), (0,)), ((), ()))
    stack = math.gcd(group_size, 4)
    for c in range(group_size // stack):
        heads = range(c * stack, (c + 1) * stack)
        queries = jnp.concatenate(
            [q_ref[:, h * head_size : (h + 1) * head_size] for h in heads], axis=0
        )
        top_prev = jnp.concatenate([top_ref[0, :, h : h + 1] for h in heads], axis=0)
        total_prev = jnp.concatenate([total_ref[0, :, h : h + 1] for h in heads], axis=0)
        acc_prev = jnp.concatenate(
            [acc_ref[:, h * head_size : (h + 1) * head_size] for h in heads], axis=0
        )
        scores = lax.dot_general(
            queries, page_keys, dims, preferred_element_type=jnp.float32
        ) * scale
        if mask_pages:
            scores = jnp.where(page_visible, scores, -1e30)
        row_top = jnp.maximum(top_prev, jnp.max(scores, axis=1, keepdims=True))
        factor = jnp.exp(top_prev - row_top)
        weights = jnp.exp(scores - row_top)
        row_total = total_prev * factor + jnp.sum(weights, axis=1, keepdims=True)
        summed = acc_prev * factor + lax.dot_general(
            weights.astype(jnp.bfloat16), page_values, pv, preferred_element_type=jnp.float32
        )
        for j, h in enumerate(heads):
            rows = slice(j * q_rows, (j + 1) * q_rows)
            cols = slice(h * head_size, (h + 1) * head_size)
            if final:
                out_refs[0][:, cols] = (summed[rows] / row_total[rows]).astype(out_refs[0].dtype)
            else:
                out_refs[0][:, cols] = summed[rows]
                out_refs[1][0, :, h : h + 1] = row_top[rows]
                out_refs[2][0, :, h : h + 1] = row_total[rows]


def prefix_part(page_ok, q_new, pages, acc, top, total, group_size, head_size, mask_pages,
                final=True):
    q_rows = q_new.shape[0]
    npage, kv_heads, page_len, width = pages.shape
    kernel = functools.partial(
        prefix_kernel, head_size=head_size, group_size=group_size, mask_pages=mask_pages,
        final=final,
    )
    span = group_size * head_size
    block = pl.BlockSpec((q_rows, span), lambda g: (0, g))
    stat_spec = pl.BlockSpec((1, q_rows, group_size), lambda g: (g, 0, 0))
    if final:
        out_shape = jax.ShapeDtypeStruct(q_new.shape, q_new.dtype)
        out_specs = block
    else:
        stat = jax.ShapeDtypeStruct(top.shape, jnp.float32)
        out_shape = (jax.ShapeDtypeStruct(q_new.shape, jnp.float32), stat, stat)
        out_specs = (block, stat_spec, stat_spec)
    rows = q_new.shape[0] * q_new.shape[1] // head_size
    keys = npage * page_len
    cost = pl.CostEstimate(
        flops=4 * rows * keys * head_size,
        transcendentals=rows * keys,
        bytes_accessed=q_new.size * 2 + pages.size * 2 + acc.size * 8,
    )
    return pl.pallas_call(
        kernel,
        out_shape=out_shape,
        cost_estimate=cost,
        grid=(kv_heads,),
        in_specs=[
            block,
            pl.BlockSpec((npage, 1, page_len, width), lambda g: (0, g, 0, 0)),
            pl.BlockSpec((1, npage * page_len), lambda g: (0, 0)),
            block,
            stat_spec,
            stat_spec,
        ],
        out_specs=out_specs,
    )(q_new, pages, page_ok, acc, top, total)


def attention(query_start, key_pos, page_ok, q_new, new_all, pages, group_size, head_size,
              mask_pages):
    q_rows = q_new.shape[0]
    blocks, kv_heads, new_len, width = new_all.shape
    npage, _, page_len, _ = pages.shape
    kernel = functools.partial(
        attention_kernel, head_size=head_size, group_size=group_size, mask_pages=mask_pages
    )
    span = group_size * head_size
    stat = jax.ShapeDtypeStruct((kv_heads, q_rows, group_size), jnp.float32)
    stat_spec = pl.BlockSpec((1, q_rows, group_size), lambda g, s: (g, 0, 0))
    return pl.pallas_call(
        kernel,
        out_shape=(jax.ShapeDtypeStruct(q_new.shape, jnp.float32), stat, stat),
        grid_spec=pltpu.PrefetchScalarGridSpec(
            num_scalar_prefetch=1,
            grid=(kv_heads,),
            in_specs=[
                pl.BlockSpec((q_rows, span), lambda g, s: (0, g)),
                pl.BlockSpec((blocks, 1, new_len, width), lambda g, s: (0, g, 0, 0)),
                pl.BlockSpec((npage, 1, page_len, width), lambda g, s: (0, g, 0, 0)),
                pl.BlockSpec((1, blocks * new_len), lambda g, s: (0, 0)),
                pl.BlockSpec((1, npage * page_len), lambda g, s: (0, 0)),
            ],
            out_specs=(pl.BlockSpec((q_rows, span), lambda g, s: (0, g)), stat_spec, stat_spec),
        ),
    )(query_start, q_new, new_all, pages, key_pos, page_ok)


def local(q_new, kv_new, kv_cache, page_table, block_offsets):
    kv_heads = kv_new.shape[1]
    head_size = kv_new.shape[2] // 2
    group_size = q_new.shape[1] // (head_size * kv_heads)
    slots_dev = kv_cache.shape[0]
    npages = page_table.shape[0]
    blocks = lax.axis_size("blk")
    myself = lax.axis_index("blk")
    pg = -(-npages // blocks)
    block_ids = jnp.arange(blocks, dtype=jnp.int32)
    my_offset = jnp.sum(jnp.where(block_ids == myself, block_offsets, 0))

    own_rows = kv_new.transpose(1, 0, 2)
    new_all = [own_rows]
    for k in range(1, blocks):
        new_all.append(
            lax.ppermute(own_rows, "blk", [(i, (i + k) % blocks) for i in range(blocks)])
        )
    shifted_offsets = block_offsets[(myself - block_ids) % blocks]

    page_owner = page_table // slots_dev
    owned = page_owner == myself
    page_rank = jnp.cumsum(owned.astype(jnp.int32)) - 1
    local_slot = page_table % slots_dev
    counts = jnp.sum((page_owner[None, :] == block_ids[:, None]).astype(jnp.int32), axis=1)
    per_peer = (CAP + blocks - 1) // blocks
    starts = jnp.cumsum(counts) - counts
    my_start = jnp.sum(jnp.where(block_ids == myself, starts, 0))
    peer_slots = jnp.arange(per_peer, dtype=jnp.int32)[None, :]
    wanted = (block_ids[:, None] - my_start) % blocks + peer_slots * blocks
    picked = owned[None, None, :] & (page_rank[None, None, :] == wanted[..., None])
    chosen = jnp.sum(jnp.where(picked, local_slot[None, None, :], 0), axis=2).reshape(-1)
    by_shift = chosen.reshape(blocks, per_peer)[(myself + block_ids) % blocks].reshape(-1)
    sent = kv_cache[by_shift].reshape((blocks, per_peer) + kv_cache.shape[1:])
    sent, new_all = lax.optimization_barrier((sent, new_all))
    new_all = jnp.stack(new_all)
    arrived = [sent[0]]
    for k in range(1, blocks):
        arrived.append(
            lax.ppermute(sent[k], "blk", [(i, (i + k) % blocks) for i in range(blocks)])
        )
    received = jnp.stack(arrived).reshape((blocks * per_peer,) + kv_cache.shape[1:])
    arriving = (myself - starts[:, None]) % blocks + peer_slots * blocks
    present = (arriving < counts[:, None])[(myself - block_ids) % blocks].reshape(-1)
    order_rank = jnp.cumsum(present.astype(jnp.int32)) - 1
    choose = present[None, :] & (order_rank[None, :] == jnp.arange(pg, dtype=jnp.int32)[:, None])
    positions = jnp.sum(
        jnp.where(choose, jnp.arange(blocks * per_peer, dtype=jnp.int32)[None, :], 0), axis=1
    )
    own = received[positions]
    gathered = [own]
    for k in range(1, blocks):
        gathered.append(
            lax.ppermute(own, "blk", [(i, (i + k) % blocks) for i in range(blocks)])
        )
    later = blocks > 2

    q_rows = q_new.shape[0]
    page_len = kv_cache.shape[2]
    query_start = (my_offset * q_rows).reshape(1).astype(jnp.int32)
    key_pos = (
        jnp.repeat(shifted_offsets, q_rows) * q_rows
        + jnp.tile(jnp.arange(q_rows, dtype=jnp.int32), blocks)
    ).reshape(1, -1).astype(jnp.int32)
    slot_ids = jnp.arange(pg, dtype=jnp.int32)
    page_ok = slot_ids[None, :] * blocks + ((myself - block_ids) % blocks)[:, None] < npages
    page_ok = jnp.repeat(page_ok.astype(jnp.int32).reshape(-1), page_len).reshape(1, -1)
    own_ok = page_ok[:, : pg * page_len]
    first_ok = page_ok[:, pg * page_len : 2 * pg * page_len]
    later_ok = page_ok[:, 2 * pg * page_len :]
    ragged = npages % blocks != 0
    acc, top, total = attention(
        query_start, key_pos, own_ok, q_new, new_all, own, group_size, head_size, ragged
    )
    if not later:
        return prefix_part(
            first_ok, q_new, gathered[1], acc, top, total, group_size, head_size, ragged
        )
    acc, top, total = prefix_part(
        first_ok, q_new, gathered[1], acc, top, total, group_size, head_size, ragged, False
    )
    acc, top, total, farther = lax.optimization_barrier((acc, top, total, gathered[2:]))
    later = jnp.concatenate(farther)
    return prefix_part(later_ok, q_new, later, acc, top, total, group_size, head_size, ragged)


def solution(mesh):
    return jax.shard_map(
        local,
        mesh=mesh,
        in_specs=(
            P(("groups", "blk"), "pool"),
            P(("groups", "blk"), "pool", None),
            P(("groups", "blk"), "pool", None, None),
            P("groups"),
            P("groups"),
        ),
        out_specs=P(("groups", "blk"), "pool"),
        check_vma=False,
    )
```

```python
import functools
import math

import jax
import jax.numpy as jnp
from jax import lax
from jax.experimental import pallas as pl
from jax.experimental.pallas import tpu as pltpu
from jax.sharding import PartitionSpec as P

CAP = 4


def attention_kernel(
    query_start, q_ref, new_ref, page_ref, key_pos_ref, page_ok_ref, acc_ref, top_ref, total_ref,
    *, head_size, group_size, mask_pages,
):
    scale = 1.0 / math.sqrt(head_size)
    q_rows = q_ref.shape[0]
    new_kv = new_ref[:, 0].reshape(-1, new_ref.shape[-1])
    page_kv = page_ref[:, 0].reshape(-1, page_ref.shape[-1])
    new_keys = new_kv[:, :head_size]
    new_values = new_kv[:, head_size:]
    page_keys = page_kv[:, :head_size]
    page_values = page_kv[:, head_size:]
    row_pos = query_start[0] + lax.broadcasted_iota(jnp.int32, (q_rows, new_kv.shape[0]), 0)
    new_visible = key_pos_ref[...] <= row_pos
    page_visible = page_ok_ref[...] > 0
    dims = (((1,), (1,)), ((), ()))
    pv = (((1,), (0,)), ((), ()))
    stack = 2 if group_size % 2 == 0 else 1
    new_visible = jnp.concatenate([new_visible] * stack, axis=0)
    for c in range(group_size // stack):
        heads = range(c * stack, (c + 1) * stack)
        queries = jnp.concatenate(
            [q_ref[:, h * head_size : (h + 1) * head_size] for h in heads], axis=0
        )
        new_scores = lax.dot_general(
            queries, new_keys, dims, preferred_element_type=jnp.float32
        ) * scale
        page_scores = lax.dot_general(
            queries, page_keys, dims, preferred_element_type=jnp.float32
        ) * scale
        new_scores = jnp.where(new_visible, new_scores, -1e30)
        if mask_pages:
            page_scores = jnp.where(page_visible, page_scores, -1e30)
        row_top = jnp.maximum(
            jnp.max(new_scores, axis=1, keepdims=True),
            jnp.max(page_scores, axis=1, keepdims=True),
        )
        new_weights = jnp.exp(new_scores - row_top)
        page_weights = jnp.exp(page_scores - row_top)
        row_total = jnp.sum(new_weights, axis=1, keepdims=True) + jnp.sum(
            page_weights, axis=1, keepdims=True
        )
        summed = lax.dot_general(
            new_weights.astype(jnp.bfloat16), new_values, pv,
            preferred_element_type=jnp.float32,
        ) + lax.dot_general(
            page_weights.astype(jnp.bfloat16), page_values, pv,
            preferred_element_type=jnp.float32,
        )
        for j, h in enumerate(heads):
            rows = slice(j * q_rows, (j + 1) * q_rows)
            acc_ref[:, h * head_size : (h + 1) * head_size] = summed[rows]
            top_ref[0, :, h : h + 1] = row_top[rows]
            total_ref[0, :, h : h + 1] = row_total[rows]


def prefix_kernel(
    q_ref, page_ref, page_ok_ref, acc_ref, top_ref, total_ref, *out_refs,
    head_size, group_size, mask_pages, final,
):
    scale = 1.0 / math.sqrt(head_size)
    q_rows = q_ref.shape[0]
    page_kv = page_ref[:, 0].reshape(-1, page_ref.shape[-1])
    page_keys = page_kv[:, :head_size]
    page_values = page_kv[:, head_size:]
    page_visible = page_ok_ref[...] > 0
    dims = (((1,), (1,)), ((), ()))
    pv = (((1,), (0,)), ((), ()))
    stack = 2 if group_size % 2 == 0 else 1
    for c in range(group_size // stack):
        heads = range(c * stack, (c + 1) * stack)
        queries = jnp.concatenate(
            [q_ref[:, h * head_size : (h + 1) * head_size] for h in heads], axis=0
        )
        top_prev = jnp.concatenate([top_ref[0, :, h : h + 1] for h in heads], axis=0)
        total_prev = jnp.concatenate([total_ref[0, :, h : h + 1] for h in heads], axis=0)
        acc_prev = jnp.concatenate(
            [acc_ref[:, h * head_size : (h + 1) * head_size] for h in heads], axis=0
        )
        scores = lax.dot_general(
            queries, page_keys, dims, preferred_element_type=jnp.float32
        ) * scale
        if mask_pages:
            scores = jnp.where(page_visible, scores, -1e30)
        row_top = jnp.maximum(top_prev, jnp.max(scores, axis=1, keepdims=True))
        factor = jnp.exp(top_prev - row_top)
        weights = jnp.exp(scores - row_top)
        row_total = total_prev * factor + jnp.sum(weights, axis=1, keepdims=True)
        summed = acc_prev * factor + lax.dot_general(
            weights.astype(jnp.bfloat16), page_values, pv, preferred_element_type=jnp.float32
        )
        for j, h in enumerate(heads):
            rows = slice(j * q_rows, (j + 1) * q_rows)
            cols = slice(h * head_size, (h + 1) * head_size)
            if final:
                out_refs[0][:, cols] = (summed[rows] / row_total[rows]).astype(out_refs[0].dtype)
            else:
                out_refs[0][:, cols] = summed[rows]
                out_refs[1][0, :, h : h + 1] = row_top[rows]
                out_refs[2][0, :, h : h + 1] = row_total[rows]


def prefix_part(page_ok, q_new, pages, acc, top, total, group_size, head_size, mask_pages,
                final=True):
    q_rows = q_new.shape[0]
    npage, kv_heads, page_len, width = pages.shape
    kernel = functools.partial(
        prefix_kernel, head_size=head_size, group_size=group_size, mask_pages=mask_pages,
        final=final,
    )
    span = group_size * head_size
    block = pl.BlockSpec((q_rows, span), lambda g: (0, g))
    stat_spec = pl.BlockSpec((1, q_rows, group_size), lambda g: (g, 0, 0))
    if final:
        out_shape = jax.ShapeDtypeStruct(q_new.shape, q_new.dtype)
        out_specs = block
    else:
        stat = jax.ShapeDtypeStruct(top.shape, jnp.float32)
        out_shape = (jax.ShapeDtypeStruct(q_new.shape, jnp.float32), stat, stat)
        out_specs = (block, stat_spec, stat_spec)
    rows = q_new.shape[0] * q_new.shape[1] // head_size
    keys = npage * page_len
    cost = pl.CostEstimate(
        flops=4 * rows * keys * head_size,
        transcendentals=rows * keys,
        bytes_accessed=q_new.size * 2 + pages.size * 2 + acc.size * 8,
    )
    return pl.pallas_call(
        kernel,
        out_shape=out_shape,
        cost_estimate=cost,
        grid=(kv_heads,),
        in_specs=[
            block,
            pl.BlockSpec((npage, 1, page_len, width), lambda g: (0, g, 0, 0)),
            pl.BlockSpec((1, npage * page_len), lambda g: (0, 0)),
            block,
            stat_spec,
            stat_spec,
        ],
        out_specs=out_specs,
    )(q_new, pages, page_ok, acc, top, total)


def attention(query_start, key_pos, page_ok, q_new, new_all, pages, group_size, head_size,
              mask_pages):
    q_rows = q_new.shape[0]
    blocks, kv_heads, new_len, width = new_all.shape
    npage, _, page_len, _ = pages.shape
    kernel = functools.partial(
        attention_kernel, head_size=head_size, group_size=group_size, mask_pages=mask_pages
    )
    span = group_size * head_size
    stat = jax.ShapeDtypeStruct((kv_heads, q_rows, group_size), jnp.float32)
    stat_spec = pl.BlockSpec((1, q_rows, group_size), lambda g, s: (g, 0, 0))
    return pl.pallas_call(
        kernel,
        out_shape=(jax.ShapeDtypeStruct(q_new.shape, jnp.float32), stat, stat),
        grid_spec=pltpu.PrefetchScalarGridSpec(
            num_scalar_prefetch=1,
            grid=(kv_heads,),
            in_specs=[
                pl.BlockSpec((q_rows, span), lambda g, s: (0, g)),
                pl.BlockSpec((blocks, 1, new_len, width), lambda g, s: (0, g, 0, 0)),
                pl.BlockSpec((npage, 1, page_len, width), lambda g, s: (0, g, 0, 0)),
                pl.BlockSpec((1, blocks * new_len), lambda g, s: (0, 0)),
                pl.BlockSpec((1, npage * page_len), lambda g, s: (0, 0)),
            ],
            out_specs=(pl.BlockSpec((q_rows, span), lambda g, s: (0, g)), stat_spec, stat_spec),
        ),
    )(query_start, q_new, new_all, pages, key_pos, page_ok)


def local(q_new, kv_new, kv_cache, page_table, block_offsets):
    kv_heads = kv_new.shape[1]
    head_size = kv_new.shape[2] // 2
    group_size = q_new.shape[1] // (head_size * kv_heads)
    slots_dev = kv_cache.shape[0]
    npages = page_table.shape[0]
    blocks = lax.axis_size("blk")
    myself = lax.axis_index("blk")
    pg = -(-npages // blocks)
    block_ids = jnp.arange(blocks, dtype=jnp.int32)
    my_offset = jnp.sum(jnp.where(block_ids == myself, block_offsets, 0))

    own_rows = kv_new.transpose(1, 0, 2)
    new_all = [own_rows]
    for k in range(1, blocks):
        new_all.append(
            lax.ppermute(own_rows, "blk", [(i, (i + k) % blocks) for i in range(blocks)])
        )
    shifted_offsets = block_offsets[(myself - block_ids) % blocks]

    page_owner = page_table // slots_dev
    owned = page_owner == myself
    page_rank = jnp.cumsum(owned.astype(jnp.int32)) - 1
    local_slot = page_table % slots_dev
    counts = jnp.sum((page_owner[None, :] == block_ids[:, None]).astype(jnp.int32), axis=1)
    per_peer = (CAP + blocks - 1) // blocks
    starts = jnp.cumsum(counts) - counts
    my_start = jnp.sum(jnp.where(block_ids == myself, starts, 0))
    peer_slots = jnp.arange(per_peer, dtype=jnp.int32)[None, :]
    wanted = (block_ids[:, None] - my_start) % blocks + peer_slots * blocks
    picked = owned[None, None, :] & (page_rank[None, None, :] == wanted[..., None])
    chosen = jnp.sum(jnp.where(picked, local_slot[None, None, :], 0), axis=2).reshape(-1)
    by_shift = chosen.reshape(blocks, per_peer)[(myself + block_ids) % blocks].reshape(-1)
    sent = [
        lax.dynamic_slice_in_dim(kv_cache, by_shift[k * per_peer], per_peer)
        if per_peer == 1 else kv_cache[by_shift[k * per_peer : (k + 1) * per_peer]]
        for k in range(blocks)
    ]
    sent, new_all = lax.optimization_barrier((sent, new_all))
    new_all = jnp.stack(new_all)
    arrived = [sent[0]]
    for k in range(1, blocks):
        arrived.append(
            lax.ppermute(sent[k], "blk", [(i, (i + k) % blocks) for i in range(blocks)])
        )
    received = jnp.stack(arrived).reshape((blocks * per_peer,) + kv_cache.shape[1:])
    arriving = (myself - starts[:, None]) % blocks + peer_slots * blocks
    present = (arriving < counts[:, None])[(myself - block_ids) % blocks].reshape(-1)
    order_rank = jnp.cumsum(present.astype(jnp.int32)) - 1
    choose = present[None, :] & (order_rank[None, :] == jnp.arange(pg, dtype=jnp.int32)[:, None])
    positions = jnp.sum(
        jnp.where(choose, jnp.arange(blocks * per_peer, dtype=jnp.int32)[None, :], 0), axis=1
    )
    own = received[positions]
    gathered = [own]
    for k in range(1, blocks):
        gathered.append(
            lax.ppermute(own, "blk", [(i, (i + k) % blocks) for i in range(blocks)])
        )
    later = blocks > 2

    q_rows = q_new.shape[0]
    page_len = kv_cache.shape[2]
    query_start = (my_offset * q_rows).reshape(1).astype(jnp.int32)
    key_pos = (
        jnp.repeat(shifted_offsets, q_rows) * q_rows
        + jnp.tile(jnp.arange(q_rows, dtype=jnp.int32), blocks)
    ).reshape(1, -1).astype(jnp.int32)
    slot_ids = jnp.arange(pg, dtype=jnp.int32)
    page_ok = slot_ids[None, :] * blocks + ((myself - block_ids) % blocks)[:, None] < npages
    page_ok = jnp.repeat(page_ok.astype(jnp.int32).reshape(-1), page_len).reshape(1, -1)
    own_ok = page_ok[:, : pg * page_len]
    first_ok = page_ok[:, pg * page_len : 2 * pg * page_len]
    later_ok = page_ok[:, 2 * pg * page_len :]
    ragged = npages % blocks != 0
    acc, top, total = attention(
        query_start, key_pos, own_ok, q_new, new_all, own, group_size, head_size, ragged
    )
    if not later:
        return prefix_part(
            first_ok, q_new, gathered[1], acc, top, total, group_size, head_size, ragged
        )
    acc, top, total = prefix_part(
        first_ok, q_new, gathered[1], acc, top, total, group_size, head_size, ragged, False
    )
    acc, top, total, farther = lax.optimization_barrier((acc, top, total, gathered[2:]))
    later = jnp.concatenate(farther)
    return prefix_part(later_ok, q_new, later, acc, top, total, group_size, head_size, ragged)


def solution(mesh):
    return jax.shard_map(
        local,
        mesh=mesh,
        in_specs=(
            P(("groups", "blk"), "pool"),
            P(("groups", "blk"), "pool", None),
            P(("groups", "blk"), "pool", None, None),
            P("groups"),
            P("groups"),
        ),
        out_specs=P(("groups", "blk"), "pool"),
        check_vma=False,
    )
```

```python
import functools
import math

import jax
import jax.numpy as jnp
from jax import lax
from jax.experimental import pallas as pl
from jax.experimental.pallas import tpu as pltpu
from jax.sharding import PartitionSpec as P

CAP = 4


def attention_kernel(
    query_start, q_ref, new_ref, page_ref, key_pos_ref, page_ok_ref, acc_ref, top_ref, total_ref,
    *, head_size, group_size, mask_pages,
):
    scale = 1.0 / math.sqrt(head_size)
    q_rows = q_ref.shape[0]
    new_kv = new_ref[:, 0].reshape(-1, new_ref.shape[-1])
    page_kv = page_ref[:, 0].reshape(-1, page_ref.shape[-1])
    new_keys = new_kv[:, :head_size]
    new_values = new_kv[:, head_size:]
    page_keys = page_kv[:, :head_size]
    page_values = page_kv[:, head_size:]
    row_pos = query_start[0] + lax.broadcasted_iota(jnp.int32, (q_rows, new_kv.shape[0]), 0)
    new_visible = key_pos_ref[...] <= row_pos
    page_visible = page_ok_ref[...] > 0
    dims = (((1,), (1,)), ((), ()))
    pv = (((1,), (0,)), ((), ()))
    stack = 2 if group_size % 2 == 0 else 1
    new_visible = jnp.concatenate([new_visible] * stack, axis=0)
    for c in range(group_size // stack):
        heads = range(c * stack, (c + 1) * stack)
        queries = jnp.concatenate(
            [q_ref[:, h * head_size : (h + 1) * head_size] for h in heads], axis=0
        )
        new_scores = lax.dot_general(
            queries, new_keys, dims, preferred_element_type=jnp.float32
        ) * scale
        page_scores = lax.dot_general(
            queries, page_keys, dims, preferred_element_type=jnp.float32
        ) * scale
        new_scores = jnp.where(new_visible, new_scores, -1e30)
        if mask_pages:
            page_scores = jnp.where(page_visible, page_scores, -1e30)
        row_top = jnp.maximum(
            jnp.max(new_scores, axis=1, keepdims=True),
            jnp.max(page_scores, axis=1, keepdims=True),
        )
        new_weights = jnp.exp(new_scores - row_top)
        page_weights = jnp.exp(page_scores - row_top)
        row_total = jnp.sum(new_weights, axis=1, keepdims=True) + jnp.sum(
            page_weights, axis=1, keepdims=True
        )
        summed = lax.dot_general(
            new_weights.astype(jnp.bfloat16), new_values, pv,
            preferred_element_type=jnp.float32,
        ) + lax.dot_general(
            page_weights.astype(jnp.bfloat16), page_values, pv,
            preferred_element_type=jnp.float32,
        )
        for j, h in enumerate(heads):
            rows = slice(j * q_rows, (j + 1) * q_rows)
            acc_ref[:, h * head_size : (h + 1) * head_size] = summed[rows]
            top_ref[0, :, h : h + 1] = row_top[rows]
            total_ref[0, :, h : h + 1] = row_total[rows]


def prefix_kernel(
    q_ref, *refs, head_size, group_size, mask_pages, final, parts,
):
    page_refs = refs[:parts]
    page_ok_ref, acc_ref, top_ref, total_ref = refs[parts : parts + 4]
    out_refs = refs[parts + 4 :]
    scale = 1.0 / math.sqrt(head_size)
    q_rows = q_ref.shape[0]
    page_kv = jnp.concatenate(
        [r[:, 0].reshape(-1, r.shape[-1]) for r in page_refs], axis=0
    )
    page_keys = page_kv[:, :head_size]
    page_values = page_kv[:, head_size:]
    page_visible = page_ok_ref[...] > 0
    dims = (((1,), (1,)), ((), ()))
    pv = (((1,), (0,)), ((), ()))
    stack = 2 if group_size % 2 == 0 else 1
    for c in range(group_size // stack):
        heads = range(c * stack, (c + 1) * stack)
        queries = jnp.concatenate(
            [q_ref[:, h * head_size : (h + 1) * head_size] for h in heads], axis=0
        )
        top_prev = jnp.concatenate([top_ref[0, :, h : h + 1] for h in heads], axis=0)
        total_prev = jnp.concatenate([total_ref[0, :, h : h + 1] for h in heads], axis=0)
        acc_prev = jnp.concatenate(
            [acc_ref[:, h * head_size : (h + 1) * head_size] for h in heads], axis=0
        )
        scores = lax.dot_general(
            queries, page_keys, dims, preferred_element_type=jnp.float32
        ) * scale
        if mask_pages:
            scores = jnp.where(page_visible, scores, -1e30)
        row_top = jnp.maximum(top_prev, jnp.max(scores, axis=1, keepdims=True))
        factor = jnp.exp(top_prev - row_top)
        weights = jnp.exp(scores - row_top)
        row_total = total_prev * factor + jnp.sum(weights, axis=1, keepdims=True)
        summed = acc_prev * factor + lax.dot_general(
            weights.astype(jnp.bfloat16), page_values, pv, preferred_element_type=jnp.float32
        )
        for j, h in enumerate(heads):
            rows = slice(j * q_rows, (j + 1) * q_rows)
            cols = slice(h * head_size, (h + 1) * head_size)
            if final:
                out_refs[0][:, cols] = (summed[rows] / row_total[rows]).astype(out_refs[0].dtype)
            else:
                out_refs[0][:, cols] = summed[rows]
                out_refs[1][0, :, h : h + 1] = row_top[rows]
                out_refs[2][0, :, h : h + 1] = row_total[rows]


def prefix_part(page_ok, q_new, page_list, acc, top, total, group_size, head_size, mask_pages,
                final=True):
    q_rows = q_new.shape[0]
    part_pages, kv_heads, page_len, width = page_list[0].shape
    npage = part_pages * len(page_list)
    kernel = functools.partial(
        prefix_kernel, head_size=head_size, group_size=group_size, mask_pages=mask_pages,
        final=final, parts=len(page_list),
    )
    span = group_size * head_size
    block = pl.BlockSpec((q_rows, span), lambda g: (0, g))
    stat_spec = pl.BlockSpec((1, q_rows, group_size), lambda g: (g, 0, 0))
    if final:
        out_shape = jax.ShapeDtypeStruct(q_new.shape, q_new.dtype)
        out_specs = block
    else:
        stat = jax.ShapeDtypeStruct(top.shape, jnp.float32)
        out_shape = (jax.ShapeDtypeStruct(q_new.shape, jnp.float32), stat, stat)
        out_specs = (block, stat_spec, stat_spec)
    rows = q_new.shape[0] * q_new.shape[1] // head_size
    keys = npage * page_len
    cost = pl.CostEstimate(
        flops=4 * rows * keys * head_size,
        transcendentals=rows * keys,
        bytes_accessed=q_new.size * 2 + npage * kv_heads * page_len * width * 2 + acc.size * 8,
    )
    return pl.pallas_call(
        kernel,
        out_shape=out_shape,
        cost_estimate=cost,
        grid=(kv_heads,),
        in_specs=[
            block,
            *[pl.BlockSpec((part_pages, 1, page_len, width), lambda g: (0, g, 0, 0))]
            * len(page_list),
            pl.BlockSpec((1, npage * page_len), lambda g: (0, 0)),
            block,
            stat_spec,
            stat_spec,
        ],
        out_specs=out_specs,
    )(q_new, *page_list, page_ok, acc, top, total)


def attention(query_start, key_pos, page_ok, q_new, new_all, pages, group_size, head_size,
              mask_pages):
    q_rows = q_new.shape[0]
    blocks, kv_heads, new_len, width = new_all.shape
    npage, _, page_len, _ = pages.shape
    kernel = functools.partial(
        attention_kernel, head_size=head_size, group_size=group_size, mask_pages=mask_pages
    )
    span = group_size * head_size
    stat = jax.ShapeDtypeStruct((kv_heads, q_rows, group_size), jnp.float32)
    stat_spec = pl.BlockSpec((1, q_rows, group_size), lambda g, s: (g, 0, 0))
    return pl.pallas_call(
        kernel,
        out_shape=(jax.ShapeDtypeStruct(q_new.shape, jnp.float32), stat, stat),
        grid_spec=pltpu.PrefetchScalarGridSpec(
            num_scalar_prefetch=1,
            grid=(kv_heads,),
            in_specs=[
                pl.BlockSpec((q_rows, span), lambda g, s: (0, g)),
                pl.BlockSpec((blocks, 1, new_len, width), lambda g, s: (0, g, 0, 0)),
                pl.BlockSpec((npage, 1, page_len, width), lambda g, s: (0, g, 0, 0)),
                pl.BlockSpec((1, blocks * new_len), lambda g, s: (0, 0)),
                pl.BlockSpec((1, npage * page_len), lambda g, s: (0, 0)),
            ],
            out_specs=(pl.BlockSpec((q_rows, span), lambda g, s: (0, g)), stat_spec, stat_spec),
        ),
    )(query_start, q_new, new_all, pages, key_pos, page_ok)


def local(q_new, kv_new, kv_cache, page_table, block_offsets):
    kv_heads = kv_new.shape[1]
    head_size = kv_new.shape[2] // 2
    group_size = q_new.shape[1] // (head_size * kv_heads)
    slots_dev = kv_cache.shape[0]
    npages = page_table.shape[0]
    blocks = lax.axis_size("blk")
    myself = lax.axis_index("blk")
    pg = -(-npages // blocks)
    block_ids = jnp.arange(blocks, dtype=jnp.int32)
    my_offset = jnp.sum(jnp.where(block_ids == myself, block_offsets, 0))

    own_rows = kv_new.transpose(1, 0, 2)
    new_all = [own_rows]
    for k in range(1, blocks):
        new_all.append(
            lax.ppermute(own_rows, "blk", [(i, (i + k) % blocks) for i in range(blocks)])
        )
    shifted_offsets = block_offsets[(myself - block_ids) % blocks]

    page_owner = page_table // slots_dev
    owned = page_owner == myself
    page_rank = jnp.cumsum(owned.astype(jnp.int32)) - 1
    local_slot = page_table % slots_dev
    counts = jnp.sum((page_owner[None, :] == block_ids[:, None]).astype(jnp.int32), axis=1)
    per_peer = (CAP + blocks - 1) // blocks
    starts = jnp.cumsum(counts) - counts
    my_start = jnp.sum(jnp.where(block_ids == myself, starts, 0))
    peer_slots = jnp.arange(per_peer, dtype=jnp.int32)[None, :]
    wanted = (block_ids[:, None] - my_start) % blocks + peer_slots * blocks
    picked = owned[None, None, :] & (page_rank[None, None, :] == wanted[..., None])
    chosen = jnp.sum(jnp.where(picked, local_slot[None, None, :], 0), axis=2).reshape(-1)
    by_shift = chosen.reshape(blocks, per_peer)[(myself + block_ids) % blocks].reshape(-1)
    sent = kv_cache[by_shift].reshape((blocks, per_peer) + kv_cache.shape[1:])
    sent, new_all = lax.optimization_barrier((sent, new_all))
    new_all = jnp.stack(new_all)
    arrived = [sent[0]]
    for k in range(1, blocks):
        arrived.append(
            lax.ppermute(sent[k], "blk", [(i, (i + k) % blocks) for i in range(blocks)])
        )
    received = jnp.stack(arrived).reshape((blocks * per_peer,) + kv_cache.shape[1:])
    arriving = (myself - starts[:, None]) % blocks + peer_slots * blocks
    present = (arriving < counts[:, None])[(myself - block_ids) % blocks].reshape(-1)
    order_rank = jnp.cumsum(present.astype(jnp.int32)) - 1
    choose = present[None, :] & (order_rank[None, :] == jnp.arange(pg, dtype=jnp.int32)[:, None])
    positions = jnp.sum(
        jnp.where(choose, jnp.arange(blocks * per_peer, dtype=jnp.int32)[None, :], 0), axis=1
    )
    own = received[positions]
    gathered = [own]
    for k in range(1, blocks):
        gathered.append(
            lax.ppermute(own, "blk", [(i, (i + k) % blocks) for i in range(blocks)])
        )
    later = blocks > 2

    q_rows = q_new.shape[0]
    page_len = kv_cache.shape[2]
    query_start = (my_offset * q_rows).reshape(1).astype(jnp.int32)
    key_pos = (
        jnp.repeat(shifted_offsets, q_rows) * q_rows
        + jnp.tile(jnp.arange(q_rows, dtype=jnp.int32), blocks)
    ).reshape(1, -1).astype(jnp.int32)
    slot_ids = jnp.arange(pg, dtype=jnp.int32)
    page_ok = slot_ids[None, :] * blocks + ((myself - block_ids) % blocks)[:, None] < npages
    page_ok = jnp.repeat(page_ok.astype(jnp.int32).reshape(-1), page_len).reshape(1, -1)
    own_ok = page_ok[:, : pg * page_len]
    first_ok = page_ok[:, pg * page_len : 2 * pg * page_len]
    later_ok = page_ok[:, 2 * pg * page_len :]
    ragged = npages % blocks != 0
    acc, top, total = attention(
        query_start, key_pos, own_ok, q_new, new_all, own, group_size, head_size, ragged
    )
    if not later:
        return prefix_part(
            first_ok, q_new, [gathered[1]], acc, top, total, group_size, head_size, ragged
        )
    acc, top, total = prefix_part(
        first_ok, q_new, [gathered[1]], acc, top, total, group_size, head_size, ragged, False
    )
    acc, top, total, farther = lax.optimization_barrier((acc, top, total, gathered[2:]))
    return prefix_part(later_ok, q_new, list(farther), acc, top, total, group_size, head_size, ragged)


def solution(mesh):
    return jax.shard_map(
        local,
        mesh=mesh,
        in_specs=(
            P(("groups", "blk"), "pool"),
            P(("groups", "blk"), "pool", None),
            P(("groups", "blk"), "pool", None, None),
            P("groups"),
            P("groups"),
        ),
        out_specs=P(("groups", "blk"), "pool"),
        check_vma=False,
    )
```

```python
import functools
import math

import jax
import jax.numpy as jnp
from jax import lax
from jax.experimental import pallas as pl
from jax.experimental.pallas import tpu as pltpu
from jax.sharding import PartitionSpec as P

CAP = 4


def attention_kernel(
    query_start, q_ref, new_ref, page_ref, key_pos_ref, page_ok_ref, acc_ref, top_ref, total_ref,
    *, head_size, group_size, mask_pages,
):
    scale = 1.0 / math.sqrt(head_size)
    q_rows = q_ref.shape[0]
    new_kv = new_ref[:, 0].reshape(-1, new_ref.shape[-1])
    page_kv = page_ref[:, 0].reshape(-1, page_ref.shape[-1])
    new_keys = new_kv[:, :head_size]
    new_values = new_kv[:, head_size:]
    page_keys = page_kv[:, :head_size]
    page_values = page_kv[:, head_size:]
    row_pos = query_start[0] + lax.broadcasted_iota(jnp.int32, (q_rows, new_kv.shape[0]), 0)
    new_visible = key_pos_ref[...] <= row_pos
    page_visible = page_ok_ref[...] > 0
    dims = (((1,), (1,)), ((), ()))
    pv = (((1,), (0,)), ((), ()))
    stack = 2 if group_size % 2 == 0 else 1
    new_visible = jnp.concatenate([new_visible] * stack, axis=0)
    for c in range(group_size // stack):
        heads = range(c * stack, (c + 1) * stack)
        queries = jnp.concatenate(
            [q_ref[:, h * head_size : (h + 1) * head_size] for h in heads], axis=0
        )
        new_scores = lax.dot_general(
            queries, new_keys, dims, preferred_element_type=jnp.float32
        ) * scale
        page_scores = lax.dot_general(
            queries, page_keys, dims, preferred_element_type=jnp.float32
        ) * scale
        new_scores = jnp.where(new_visible, new_scores, -1e30)
        if mask_pages:
            page_scores = jnp.where(page_visible, page_scores, -1e30)
        row_top = jnp.maximum(
            jnp.max(new_scores, axis=1, keepdims=True),
            jnp.max(page_scores, axis=1, keepdims=True),
        )
        new_weights = jnp.exp(new_scores - row_top)
        page_weights = jnp.exp(page_scores - row_top)
        row_total = jnp.sum(new_weights, axis=1, keepdims=True) + jnp.sum(
            page_weights, axis=1, keepdims=True
        )
        summed = lax.dot_general(
            new_weights.astype(jnp.bfloat16), new_values, pv,
            preferred_element_type=jnp.float32,
        ) + lax.dot_general(
            page_weights.astype(jnp.bfloat16), page_values, pv,
            preferred_element_type=jnp.float32,
        )
        for j, h in enumerate(heads):
            rows = slice(j * q_rows, (j + 1) * q_rows)
            acc_ref[:, h * head_size : (h + 1) * head_size] = summed[rows]
            top_ref[0, :, h : h + 1] = row_top[rows]
            total_ref[0, :, h : h + 1] = row_total[rows]


def prefix_kernel(
    q_ref, *refs, head_size, group_size, mask_pages, final, parts,
):
    page_refs = refs[:parts]
    page_ok_ref, acc_ref, top_ref, total_ref = refs[parts : parts + 4]
    out_refs = refs[parts + 4 :]
    scale = 1.0 / math.sqrt(head_size)
    q_rows = q_ref.shape[0]
    page_kv = jnp.concatenate(
        [r[:, 0].reshape(-1, r.shape[-1]) for r in page_refs], axis=0
    )
    page_keys = page_kv[:, :head_size]
    page_values = page_kv[:, head_size:]
    page_visible = page_ok_ref[...] > 0
    dims = (((1,), (1,)), ((), ()))
    pv = (((1,), (0,)), ((), ()))
    stack = 2 if group_size % 2 == 0 else 1
    for c in range(group_size // stack):
        heads = range(c * stack, (c + 1) * stack)
        queries = jnp.concatenate(
            [q_ref[:, h * head_size : (h + 1) * head_size] for h in heads], axis=0
        )
        top_prev = jnp.concatenate([top_ref[0, :, h : h + 1] for h in heads], axis=0)
        total_prev = jnp.concatenate([total_ref[0, :, h : h + 1] for h in heads], axis=0)
        acc_prev = jnp.concatenate(
            [acc_ref[:, h * head_size : (h + 1) * head_size] for h in heads], axis=0
        )
        scores = lax.dot_general(
            queries, page_keys, dims, preferred_element_type=jnp.float32
        ) * scale
        if mask_pages:
            scores = jnp.where(page_visible, scores, -1e30)
        row_top = jnp.maximum(top_prev, jnp.max(scores, axis=1, keepdims=True))
        factor = jnp.exp(top_prev - row_top)
        weights = jnp.exp(scores - row_top)
        row_total = total_prev * factor + jnp.sum(weights, axis=1, keepdims=True)
        summed = acc_prev * factor + lax.dot_general(
            weights.astype(jnp.bfloat16), page_values, pv, preferred_element_type=jnp.float32
        )
        for j, h in enumerate(heads):
            rows = slice(j * q_rows, (j + 1) * q_rows)
            cols = slice(h * head_size, (h + 1) * head_size)
            if final:
                out_refs[0][:, cols] = (summed[rows] / row_total[rows]).astype(out_refs[0].dtype)
            else:
                out_refs[0][:, cols] = summed[rows]
                out_refs[1][0, :, h : h + 1] = row_top[rows]
                out_refs[2][0, :, h : h + 1] = row_total[rows]


def prefix_part(page_ok, q_new, page_list, acc, top, total, group_size, head_size, mask_pages,
                final=True):
    q_rows = q_new.shape[0]
    part_pages, kv_heads, page_len, width = page_list[0].shape
    npage = part_pages * len(page_list)
    kernel = functools.partial(
        prefix_kernel, head_size=head_size, group_size=group_size, mask_pages=mask_pages,
        final=final, parts=len(page_list),
    )
    span = group_size * head_size
    block = pl.BlockSpec((q_rows, span), lambda g: (0, g))
    stat_spec = pl.BlockSpec((1, q_rows, group_size), lambda g: (g, 0, 0))
    if final:
        out_shape = jax.ShapeDtypeStruct(q_new.shape, q_new.dtype)
        out_specs = block
    else:
        stat = jax.ShapeDtypeStruct(top.shape, jnp.float32)
        out_shape = (jax.ShapeDtypeStruct(q_new.shape, jnp.float32), stat, stat)
        out_specs = (block, stat_spec, stat_spec)
    rows = q_new.shape[0] * q_new.shape[1] // head_size
    keys = npage * page_len
    cost = pl.CostEstimate(
        flops=4 * rows * keys * head_size,
        transcendentals=rows * keys,
        bytes_accessed=q_new.size * 2 + npage * kv_heads * page_len * width * 2 + acc.size * 8,
    )
    return pl.pallas_call(
        kernel,
        out_shape=out_shape,
        cost_estimate=cost,
        grid=(kv_heads,),
        in_specs=[
            block,
            *[pl.BlockSpec((part_pages, 1, page_len, width), lambda g: (0, g, 0, 0))]
            * len(page_list),
            pl.BlockSpec((1, npage * page_len), lambda g: (0, 0)),
            block,
            stat_spec,
            stat_spec,
        ],
        out_specs=out_specs,
    )(q_new, *page_list, page_ok, acc, top, total)


def attention(query_start, key_pos, page_ok, q_new, new_all, pages, group_size, head_size,
              mask_pages):
    q_rows = q_new.shape[0]
    blocks, kv_heads, new_len, width = new_all.shape
    npage, _, page_len, _ = pages.shape
    kernel = functools.partial(
        attention_kernel, head_size=head_size, group_size=group_size, mask_pages=mask_pages
    )
    span = group_size * head_size
    stat = jax.ShapeDtypeStruct((kv_heads, q_rows, group_size), jnp.float32)
    stat_spec = pl.BlockSpec((1, q_rows, group_size), lambda g, s: (g, 0, 0))
    return pl.pallas_call(
        kernel,
        out_shape=(jax.ShapeDtypeStruct(q_new.shape, jnp.float32), stat, stat),
        grid_spec=pltpu.PrefetchScalarGridSpec(
            num_scalar_prefetch=1,
            grid=(kv_heads,),
            in_specs=[
                pl.BlockSpec((q_rows, span), lambda g, s: (0, g)),
                pl.BlockSpec((blocks, 1, new_len, width), lambda g, s: (0, g, 0, 0)),
                pl.BlockSpec((npage, 1, page_len, width), lambda g, s: (0, g, 0, 0)),
                pl.BlockSpec((1, blocks * new_len), lambda g, s: (0, 0)),
                pl.BlockSpec((1, npage * page_len), lambda g, s: (0, 0)),
            ],
            out_specs=(pl.BlockSpec((q_rows, span), lambda g, s: (0, g)), stat_spec, stat_spec),
        ),
    )(query_start, q_new, new_all, pages, key_pos, page_ok)


def local(q_new, kv_new, kv_cache, page_table, block_offsets):
    kv_heads = kv_new.shape[1]
    head_size = kv_new.shape[2] // 2
    group_size = q_new.shape[1] // (head_size * kv_heads)
    slots_dev = kv_cache.shape[0]
    npages = page_table.shape[0]
    blocks = lax.axis_size("blk")
    myself = lax.axis_index("blk")
    pg = -(-npages // blocks)
    block_ids = jnp.arange(blocks, dtype=jnp.int32)
    my_offset = jnp.sum(jnp.where(block_ids == myself, block_offsets, 0))

    own_rows = kv_new.transpose(1, 0, 2)
    new_all = [own_rows]
    for k in range(1, blocks):
        new_all.append(
            lax.ppermute(own_rows, "blk", [(i, (i + k) % blocks) for i in range(blocks)])
        )
    shifted_offsets = block_offsets[(myself - block_ids) % blocks]

    page_owner = page_table // slots_dev
    owned = page_owner == myself
    page_rank = jnp.cumsum(owned.astype(jnp.int32)) - 1
    local_slot = page_table % slots_dev
    counts = jnp.sum((page_owner[None, :] == block_ids[:, None]).astype(jnp.int32), axis=1)
    per_peer = (CAP + blocks - 1) // blocks
    starts = jnp.cumsum(counts) - counts
    my_start = jnp.sum(jnp.where(block_ids == myself, starts, 0))
    peer_slots = jnp.arange(per_peer, dtype=jnp.int32)[None, :]
    wanted = (block_ids[:, None] - my_start) % blocks + peer_slots * blocks
    picked = owned[None, None, :] & (page_rank[None, None, :] == wanted[..., None])
    chosen = jnp.sum(jnp.where(picked, local_slot[None, None, :], 0), axis=2).reshape(-1)
    by_shift = chosen.reshape(blocks, per_peer)[(myself + block_ids) % blocks].reshape(-1)
    sent = kv_cache[by_shift].reshape((blocks, per_peer) + kv_cache.shape[1:])
    sent, new_all = lax.optimization_barrier((sent, new_all))
    new_all = jnp.stack(new_all)
    arrived = [sent[0]]
    for k in range(1, blocks):
        arrived.append(
            lax.ppermute(sent[k], "blk", [(i, (i + k) % blocks) for i in range(blocks)])
        )
    received = jnp.stack(arrived).reshape((blocks * per_peer,) + kv_cache.shape[1:])
    arriving = (myself - starts[:, None]) % blocks + peer_slots * blocks
    present = (arriving < counts[:, None])[(myself - block_ids) % blocks].reshape(-1)
    order_rank = jnp.cumsum(present.astype(jnp.int32)) - 1
    choose = present[None, :] & (order_rank[None, :] == jnp.arange(pg, dtype=jnp.int32)[:, None])
    positions = jnp.sum(
        jnp.where(choose, jnp.arange(blocks * per_peer, dtype=jnp.int32)[None, :], 0), axis=1
    )
    own = received[positions]
    gathered = [own]
    for k in range(1, blocks):
        gathered.append(
            lax.ppermute(own, "blk", [(i, (i + k) % blocks) for i in range(blocks)])
        )
    later = blocks > 2

    q_rows = q_new.shape[0]
    page_len = kv_cache.shape[2]
    query_start = (my_offset * q_rows).reshape(1).astype(jnp.int32)
    key_pos = (
        jnp.repeat(shifted_offsets, q_rows) * q_rows
        + jnp.tile(jnp.arange(q_rows, dtype=jnp.int32), blocks)
    ).reshape(1, -1).astype(jnp.int32)
    slot_ids = jnp.arange(pg, dtype=jnp.int32)
    page_ok = slot_ids[None, :] * blocks + ((myself - block_ids) % blocks)[:, None] < npages
    page_ok = jnp.repeat(page_ok.astype(jnp.int32).reshape(-1), page_len).reshape(1, -1)
    own_ok = page_ok[:, : pg * page_len]
    first_ok = page_ok[:, pg * page_len : 2 * pg * page_len]
    later_ok = page_ok[:, 2 * pg * page_len :]
    ragged = npages % blocks != 0
    acc, top, total = attention(
        query_start, key_pos, own_ok, q_new, new_all, own, group_size, head_size, ragged
    )
    others_ok = page_ok[:, pg * page_len :]
    return prefix_part(
        others_ok, q_new, gathered[1:], acc, top, total, group_size, head_size, ragged
    )


def solution(mesh):
    return jax.shard_map(
        local,
        mesh=mesh,
        in_specs=(
            P(("groups", "blk"), "pool"),
            P(("groups", "blk"), "pool", None),
            P(("groups", "blk"), "pool", None, None),
            P("groups"),
            P("groups"),
        ),
        out_specs=P(("groups", "blk"), "pool"),
        check_vma=False,
    )
```

```python
import functools
import math

import jax
import jax.numpy as jnp
from jax import lax
from jax.experimental import pallas as pl
from jax.experimental.pallas import tpu as pltpu
from jax.sharding import PartitionSpec as P

CAP = 4


def attention_kernel(
    query_start, q_ref, new_ref, page_ref, key_pos_ref, page_ok_ref, acc_ref, top_ref, total_ref,
    *, head_size, group_size, mask_pages,
):
    scale = 1.0 / math.sqrt(head_size)
    q_rows = q_ref.shape[0]
    new_kv = new_ref[:, 0].reshape(-1, new_ref.shape[-1])
    page_kv = page_ref[:, 0].reshape(-1, page_ref.shape[-1])
    new_keys = new_kv[:, :head_size]
    new_values = new_kv[:, head_size:]
    page_keys = page_kv[:, :head_size]
    page_values = page_kv[:, head_size:]
    row_pos = query_start[0] + lax.broadcasted_iota(jnp.int32, (q_rows, new_kv.shape[0]), 0)
    new_visible = key_pos_ref[...] <= row_pos
    page_visible = page_ok_ref[...] > 0
    dims = (((1,), (1,)), ((), ()))
    pv = (((1,), (0,)), ((), ()))
    stack = 2 if group_size % 2 == 0 else 1
    new_visible = jnp.concatenate([new_visible] * stack, axis=0)
    for c in range(group_size // stack):
        heads = range(c * stack, (c + 1) * stack)
        queries = jnp.concatenate(
            [q_ref[:, h * head_size : (h + 1) * head_size] for h in heads], axis=0
        )
        new_scores = lax.dot_general(
            queries, new_keys, dims, preferred_element_type=jnp.float32
        ) * scale
        page_scores = lax.dot_general(
            queries, page_keys, dims, preferred_element_type=jnp.float32
        ) * scale
        new_scores = jnp.where(new_visible, new_scores, -1e30)
        if mask_pages:
            page_scores = jnp.where(page_visible, page_scores, -1e30)
        row_top = jnp.maximum(
            jnp.max(new_scores, axis=1, keepdims=True),
            jnp.max(page_scores, axis=1, keepdims=True),
        )
        new_weights = jnp.exp(new_scores - row_top)
        page_weights = jnp.exp(page_scores - row_top)
        row_total = jnp.sum(new_weights, axis=1, keepdims=True) + jnp.sum(
            page_weights, axis=1, keepdims=True
        )
        summed = lax.dot_general(
            new_weights.astype(jnp.bfloat16), new_values, pv,
            preferred_element_type=jnp.float32,
        ) + lax.dot_general(
            page_weights.astype(jnp.bfloat16), page_values, pv,
            preferred_element_type=jnp.float32,
        )
        for j, h in enumerate(heads):
            rows = slice(j * q_rows, (j + 1) * q_rows)
            acc_ref[:, h * head_size : (h + 1) * head_size] = summed[rows]
            top_ref[0, :, h : h + 1] = row_top[rows]
            total_ref[0, :, h : h + 1] = row_total[rows]


def prefix_kernel(
    q_ref, *refs, head_size, group_size, mask_pages, final, parts,
):
    page_refs = refs[:parts]
    page_ok_ref, acc_ref, top_ref, total_ref = refs[parts : parts + 4]
    out_refs = refs[parts + 4 :]
    scale = 1.0 / math.sqrt(head_size)
    q_rows = q_ref.shape[0]
    page_kv = jnp.concatenate(
        [r[:, 0].reshape(-1, r.shape[-1]) for r in page_refs], axis=0
    )
    page_keys = page_kv[:, :head_size]
    page_values = page_kv[:, head_size:]
    page_visible = page_ok_ref[...] > 0
    dims = (((1,), (1,)), ((), ()))
    pv = (((1,), (0,)), ((), ()))
    stack = 2 if group_size % 2 == 0 else 1
    for c in range(group_size // stack):
        heads = range(c * stack, (c + 1) * stack)
        queries = jnp.concatenate(
            [q_ref[:, h * head_size : (h + 1) * head_size] for h in heads], axis=0
        )
        top_prev = jnp.concatenate([top_ref[0, :, h : h + 1] for h in heads], axis=0)
        total_prev = jnp.concatenate([total_ref[0, :, h : h + 1] for h in heads], axis=0)
        acc_prev = jnp.concatenate(
            [acc_ref[:, h * head_size : (h + 1) * head_size] for h in heads], axis=0
        )
        scores = lax.dot_general(
            queries, page_keys, dims, preferred_element_type=jnp.float32
        ) * scale
        if mask_pages:
            scores = jnp.where(page_visible, scores, -1e30)
        row_top = jnp.maximum(top_prev, jnp.max(scores, axis=1, keepdims=True))
        factor = jnp.exp(top_prev - row_top)
        weights = jnp.exp(scores - row_top)
        row_total = total_prev * factor + jnp.sum(weights, axis=1, keepdims=True)
        summed = acc_prev * factor + lax.dot_general(
            weights.astype(jnp.bfloat16), page_values, pv, preferred_element_type=jnp.float32
        )
        for j, h in enumerate(heads):
            rows = slice(j * q_rows, (j + 1) * q_rows)
            cols = slice(h * head_size, (h + 1) * head_size)
            if final:
                out_refs[0][:, cols] = (summed[rows] / row_total[rows]).astype(out_refs[0].dtype)
            else:
                out_refs[0][:, cols] = summed[rows]
                out_refs[1][0, :, h : h + 1] = row_top[rows]
                out_refs[2][0, :, h : h + 1] = row_total[rows]


def prefix_part(page_ok, q_new, page_list, acc, top, total, group_size, head_size, mask_pages,
                final=True):
    q_rows = q_new.shape[0]
    part_pages, kv_heads, page_len, width = page_list[0].shape
    npage = part_pages * len(page_list)
    kernel = functools.partial(
        prefix_kernel, head_size=head_size, group_size=group_size, mask_pages=mask_pages,
        final=final, parts=len(page_list),
    )
    span = group_size * head_size
    block = pl.BlockSpec((q_rows, span), lambda g: (0, g))
    stat_spec = pl.BlockSpec((1, q_rows, group_size), lambda g: (g, 0, 0))
    if final:
        out_shape = jax.ShapeDtypeStruct(q_new.shape, q_new.dtype)
        out_specs = block
    else:
        stat = jax.ShapeDtypeStruct(top.shape, jnp.float32)
        out_shape = (jax.ShapeDtypeStruct(q_new.shape, jnp.float32), stat, stat)
        out_specs = (block, stat_spec, stat_spec)
    rows = q_new.shape[0] * q_new.shape[1] // head_size
    keys = npage * page_len
    cost = pl.CostEstimate(
        flops=4 * rows * keys * head_size,
        transcendentals=rows * keys,
        bytes_accessed=q_new.size * 2 + npage * kv_heads * page_len * width * 2 + acc.size * 8,
    )
    return pl.pallas_call(
        kernel,
        out_shape=out_shape,
        cost_estimate=cost,
        grid=(kv_heads,),
        in_specs=[
            block,
            *[pl.BlockSpec((part_pages, 1, page_len, width), lambda g: (0, g, 0, 0))]
            * len(page_list),
            pl.BlockSpec((1, npage * page_len), lambda g: (0, 0)),
            block,
            stat_spec,
            stat_spec,
        ],
        out_specs=out_specs,
    )(q_new, *page_list, page_ok, acc, top, total)


def attention(query_start, key_pos, page_ok, q_new, new_all, pages, group_size, head_size,
              mask_pages):
    q_rows = q_new.shape[0]
    blocks, kv_heads, new_len, width = new_all.shape
    npage, _, page_len, _ = pages.shape
    kernel = functools.partial(
        attention_kernel, head_size=head_size, group_size=group_size, mask_pages=mask_pages
    )
    span = group_size * head_size
    stat = jax.ShapeDtypeStruct((kv_heads, q_rows, group_size), jnp.float32)
    stat_spec = pl.BlockSpec((1, q_rows, group_size), lambda g, s: (g, 0, 0))
    return pl.pallas_call(
        kernel,
        out_shape=(jax.ShapeDtypeStruct(q_new.shape, jnp.float32), stat, stat),
        grid_spec=pltpu.PrefetchScalarGridSpec(
            num_scalar_prefetch=1,
            grid=(kv_heads,),
            in_specs=[
                pl.BlockSpec((q_rows, span), lambda g, s: (0, g)),
                pl.BlockSpec((blocks, 1, new_len, width), lambda g, s: (0, g, 0, 0)),
                pl.BlockSpec((npage, 1, page_len, width), lambda g, s: (0, g, 0, 0)),
                pl.BlockSpec((1, blocks * new_len), lambda g, s: (0, 0)),
                pl.BlockSpec((1, npage * page_len), lambda g, s: (0, 0)),
            ],
            out_specs=(pl.BlockSpec((q_rows, span), lambda g, s: (0, g)), stat_spec, stat_spec),
        ),
    )(query_start, q_new, new_all, pages, key_pos, page_ok)


def local(q_new, kv_new, kv_cache, page_table, block_offsets):
    kv_heads = kv_new.shape[1]
    head_size = kv_new.shape[2] // 2
    group_size = q_new.shape[1] // (head_size * kv_heads)
    slots_dev = kv_cache.shape[0]
    npages = page_table.shape[0]
    blocks = lax.axis_size("blk")
    myself = lax.axis_index("blk")
    pg = -(-npages // blocks)
    block_ids = jnp.arange(blocks, dtype=jnp.int32)
    my_offset = jnp.sum(jnp.where(block_ids == myself, block_offsets, 0))

    own_rows = kv_new.transpose(1, 0, 2)
    new_all = [own_rows]
    for k in range(1, blocks):
        new_all.append(
            lax.ppermute(own_rows, "blk", [(i, (i + k) % blocks) for i in range(blocks)])
        )
    shifted_offsets = block_offsets[(myself - block_ids) % blocks]

    page_owner = page_table // slots_dev
    owned = page_owner == myself
    page_ids = jnp.arange(npages, dtype=jnp.int32)
    page_rank = jnp.sum(
        ((page_ids[None, :] < page_ids[:, None]) & owned[None, :]).astype(jnp.int32), axis=1
    )
    local_slot = page_table % slots_dev
    counts = jnp.sum((page_owner[None, :] == block_ids[:, None]).astype(jnp.int32), axis=1)
    per_peer = (CAP + blocks - 1) // blocks
    starts = jnp.sum((page_owner[None, :] < block_ids[:, None]).astype(jnp.int32), axis=1)
    my_start = jnp.sum(jnp.where(block_ids == myself, starts, 0))
    peer_slots = jnp.arange(per_peer, dtype=jnp.int32)[None, :]
    wanted = (block_ids[:, None] - my_start) % blocks + peer_slots * blocks
    picked = owned[None, None, :] & (page_rank[None, None, :] == wanted[..., None])
    chosen = jnp.sum(jnp.where(picked, local_slot[None, None, :], 0), axis=2).reshape(-1)
    by_shift = chosen.reshape(blocks, per_peer)[(myself + block_ids) % blocks].reshape(-1)
    sent = kv_cache[by_shift].reshape((blocks, per_peer) + kv_cache.shape[1:])
    sent, new_all = lax.optimization_barrier((sent, new_all))
    new_all = jnp.stack(new_all)
    arrived = [sent[0]]
    for k in range(1, blocks):
        arrived.append(
            lax.ppermute(sent[k], "blk", [(i, (i + k) % blocks) for i in range(blocks)])
        )
    received = jnp.stack(arrived).reshape((blocks * per_peer,) + kv_cache.shape[1:])
    arriving = (myself - starts[:, None]) % blocks + peer_slots * blocks
    present = (arriving < counts[:, None])[(myself - block_ids) % blocks].reshape(-1)
    chunk_ids = jnp.arange(blocks * per_peer, dtype=jnp.int32)
    order_rank = jnp.sum(
        ((chunk_ids[None, :] < chunk_ids[:, None]) & present[None, :]).astype(jnp.int32), axis=1
    )
    choose = present[None, :] & (order_rank[None, :] == jnp.arange(pg, dtype=jnp.int32)[:, None])
    positions = jnp.sum(
        jnp.where(choose, jnp.arange(blocks * per_peer, dtype=jnp.int32)[None, :], 0), axis=1
    )
    own = received[positions]
    gathered = [own]
    for k in range(1, blocks):
        gathered.append(
            lax.ppermute(own, "blk", [(i, (i + k) % blocks) for i in range(blocks)])
        )
    later = blocks > 2

    q_rows = q_new.shape[0]
    page_len = kv_cache.shape[2]
    query_start = (my_offset * q_rows).reshape(1).astype(jnp.int32)
    key_pos = (
        jnp.repeat(shifted_offsets, q_rows) * q_rows
        + jnp.tile(jnp.arange(q_rows, dtype=jnp.int32), blocks)
    ).reshape(1, -1).astype(jnp.int32)
    slot_ids = jnp.arange(pg, dtype=jnp.int32)
    page_ok = slot_ids[None, :] * blocks + ((myself - block_ids) % blocks)[:, None] < npages
    page_ok = jnp.repeat(page_ok.astype(jnp.int32).reshape(-1), page_len).reshape(1, -1)
    own_ok = page_ok[:, : pg * page_len]
    first_ok = page_ok[:, pg * page_len : 2 * pg * page_len]
    later_ok = page_ok[:, 2 * pg * page_len :]
    ragged = npages % blocks != 0
    acc, top, total = attention(
        query_start, key_pos, own_ok, q_new, new_all, own, group_size, head_size, ragged
    )
    if not later:
        return prefix_part(
            first_ok, q_new, [gathered[1]], acc, top, total, group_size, head_size, ragged
        )
    acc, top, total = prefix_part(
        first_ok, q_new, [gathered[1]], acc, top, total, group_size, head_size, ragged, False
    )
    acc, top, total, farther = lax.optimization_barrier((acc, top, total, gathered[2:]))
    return prefix_part(later_ok, q_new, list(farther), acc, top, total, group_size, head_size, ragged)


def solution(mesh):
    return jax.shard_map(
        local,
        mesh=mesh,
        in_specs=(
            P(("groups", "blk"), "pool"),
            P(("groups", "blk"), "pool", None),
            P(("groups", "blk"), "pool", None, None),
            P("groups"),
            P("groups"),
        ),
        out_specs=P(("groups", "blk"), "pool"),
        check_vma=False,
    )
```

```python
import functools
import math

import jax
import jax.numpy as jnp
from jax import lax
from jax.experimental import pallas as pl
from jax.experimental.pallas import tpu as pltpu
from jax.sharding import PartitionSpec as P

CAP = 4


def attention_kernel(
    query_start, q_ref, new_ref, page_ref, key_pos_ref, page_ok_ref, acc_ref, top_ref, total_ref,
    *, head_size, group_size, mask_pages,
):
    scale = 1.0 / math.sqrt(head_size)
    q_rows = q_ref.shape[0]
    new_kv = new_ref[:, 0].reshape(-1, new_ref.shape[-1])
    page_kv = page_ref[:, 0].reshape(-1, page_ref.shape[-1])
    new_keys = new_kv[:, :head_size]
    new_values = new_kv[:, head_size:]
    page_keys = page_kv[:, :head_size]
    page_values = page_kv[:, head_size:]
    row_pos = query_start[0] + lax.broadcasted_iota(jnp.int32, (q_rows, new_kv.shape[0]), 0)
    new_visible = key_pos_ref[...] <= row_pos
    page_visible = page_ok_ref[...] > 0
    dims = (((1,), (1,)), ((), ()))
    pv = (((1,), (0,)), ((), ()))
    stack = 2 if group_size % 2 == 0 else 1
    new_visible = jnp.concatenate([new_visible] * stack, axis=0)
    for c in range(group_size // stack):
        heads = range(c * stack, (c + 1) * stack)
        queries = jnp.concatenate(
            [q_ref[:, h * head_size : (h + 1) * head_size] for h in heads], axis=0
        )
        new_scores = lax.dot_general(
            queries, new_keys, dims, preferred_element_type=jnp.float32
        ) * scale
        page_scores = lax.dot_general(
            queries, page_keys, dims, preferred_element_type=jnp.float32
        ) * scale
        new_scores = jnp.where(new_visible, new_scores, -1e30)
        if mask_pages:
            page_scores = jnp.where(page_visible, page_scores, -1e30)
        row_top = jnp.maximum(
            jnp.max(new_scores, axis=1, keepdims=True),
            jnp.max(page_scores, axis=1, keepdims=True),
        )
        new_weights = jnp.exp(new_scores - row_top)
        page_weights = jnp.exp(page_scores - row_top)
        row_total = jnp.sum(new_weights, axis=1, keepdims=True) + jnp.sum(
            page_weights, axis=1, keepdims=True
        )
        summed = lax.dot_general(
            new_weights.astype(jnp.bfloat16), new_values, pv,
            preferred_element_type=jnp.float32,
        ) + lax.dot_general(
            page_weights.astype(jnp.bfloat16), page_values, pv,
            preferred_element_type=jnp.float32,
        )
        for j, h in enumerate(heads):
            rows = slice(j * q_rows, (j + 1) * q_rows)
            acc_ref[:, h * head_size : (h + 1) * head_size] = summed[rows]
            top_ref[0, :, h : h + 1] = row_top[rows]
            total_ref[0, :, h : h + 1] = row_total[rows]


def prefix_kernel(
    q_ref, *refs, head_size, group_size, mask_pages, final, parts,
):
    page_refs = refs[:parts]
    page_ok_ref, acc_ref, top_ref, total_ref = refs[parts : parts + 4]
    out_refs = refs[parts + 4 :]
    scale = 1.0 / math.sqrt(head_size)
    q_rows = q_ref.shape[0]
    page_kv = jnp.concatenate(
        [r[:, 0].reshape(-1, r.shape[-1]) for r in page_refs], axis=0
    )
    page_keys = page_kv[:, :head_size]
    page_values = page_kv[:, head_size:]
    page_visible = page_ok_ref[...] > 0
    dims = (((1,), (1,)), ((), ()))
    pv = (((1,), (0,)), ((), ()))
    stack = 2 if group_size % 2 == 0 else 1
    pair_steps = final and q_ref.shape[1] == stack * head_size
    for c in range(1 if pair_steps else group_size // stack):
        heads = range(c * stack, (c + 1) * stack)
        if pair_steps:
            first = pl.program_id(1) * stack
            lane = lax.broadcasted_iota(jnp.int32, top_ref.shape[1:], 1)

            def pick(ref, j):
                return jnp.max(
                    jnp.where(lane == first + j, ref[0], -jnp.inf), axis=1, keepdims=True
                )

            top_prev = jnp.concatenate([pick(top_ref, j) for j in range(stack)], axis=0)
            total_prev = jnp.concatenate([pick(total_ref, j) for j in range(stack)], axis=0)
            heads = range(stack)
        queries = jnp.concatenate(
            [q_ref[:, h * head_size : (h + 1) * head_size] for h in heads], axis=0
        )
        if not pair_steps:
            top_prev = jnp.concatenate([top_ref[0, :, h : h + 1] for h in heads], axis=0)
            total_prev = jnp.concatenate(
                [total_ref[0, :, h : h + 1] for h in heads], axis=0
            )
        acc_prev = jnp.concatenate(
            [acc_ref[:, h * head_size : (h + 1) * head_size] for h in heads], axis=0
        )
        scores = lax.dot_general(
            queries, page_keys, dims, preferred_element_type=jnp.float32
        ) * scale
        if mask_pages:
            scores = jnp.where(page_visible, scores, -1e30)
        row_top = jnp.maximum(top_prev, jnp.max(scores, axis=1, keepdims=True))
        factor = jnp.exp(top_prev - row_top)
        weights = jnp.exp(scores - row_top)
        row_total = total_prev * factor + jnp.sum(weights, axis=1, keepdims=True)
        summed = acc_prev * factor + lax.dot_general(
            weights.astype(jnp.bfloat16), page_values, pv, preferred_element_type=jnp.float32
        )
        for j, h in enumerate(heads):
            rows = slice(j * q_rows, (j + 1) * q_rows)
            cols = slice(h * head_size, (h + 1) * head_size)
            if final:
                out_refs[0][:, cols] = (summed[rows] / row_total[rows]).astype(out_refs[0].dtype)
            else:
                out_refs[0][:, cols] = summed[rows]
                out_refs[1][0, :, h : h + 1] = row_top[rows]
                out_refs[2][0, :, h : h + 1] = row_total[rows]


def prefix_part(page_ok, q_new, page_list, acc, top, total, group_size, head_size, mask_pages,
                final=True):
    q_rows = q_new.shape[0]
    part_pages, kv_heads, page_len, width = page_list[0].shape
    npage = part_pages * len(page_list)
    kernel = functools.partial(
        prefix_kernel, head_size=head_size, group_size=group_size, mask_pages=mask_pages,
        final=final, parts=len(page_list),
    )
    span = group_size * head_size
    block = pl.BlockSpec((q_rows, span), lambda g: (0, g))
    stat_spec = pl.BlockSpec((1, q_rows, group_size), lambda g: (g, 0, 0))
    if final:
        out_shape = jax.ShapeDtypeStruct(q_new.shape, q_new.dtype)
        out_specs = block
    else:
        stat = jax.ShapeDtypeStruct(top.shape, jnp.float32)
        out_shape = (jax.ShapeDtypeStruct(q_new.shape, jnp.float32), stat, stat)
        out_specs = (block, stat_spec, stat_spec)
    rows = q_new.shape[0] * q_new.shape[1] // head_size
    keys = npage * page_len
    cost = pl.CostEstimate(
        flops=4 * rows * keys * head_size,
        transcendentals=rows * keys,
        bytes_accessed=q_new.size * 2 + npage * kv_heads * page_len * width * 2 + acc.size * 8,
    )
    stack = 2 if group_size % 2 == 0 else 1
    if final:
        pairs = group_size // stack
        part = pl.BlockSpec((q_rows, stack * head_size), lambda g, c: (0, g * pairs + c))
        return pl.pallas_call(
            kernel,
            out_shape=out_shape,
            cost_estimate=cost,
            grid=(kv_heads, pairs),
            in_specs=[
                part,
                *[pl.BlockSpec((part_pages, 1, page_len, width), lambda g, c: (0, g, 0, 0))]
                * len(page_list),
                pl.BlockSpec((1, npage * page_len), lambda g, c: (0, 0)),
                part,
                pl.BlockSpec((1, q_rows, group_size), lambda g, c: (g, 0, 0)),
                pl.BlockSpec((1, q_rows, group_size), lambda g, c: (g, 0, 0)),
            ],
            out_specs=part,
        )(q_new, *page_list, page_ok, acc, top, total)
    return pl.pallas_call(
        kernel,
        out_shape=out_shape,
        cost_estimate=cost,
        grid=(kv_heads,),
        in_specs=[
            block,
            *[pl.BlockSpec((part_pages, 1, page_len, width), lambda g: (0, g, 0, 0))]
            * len(page_list),
            pl.BlockSpec((1, npage * page_len), lambda g: (0, 0)),
            block,
            stat_spec,
            stat_spec,
        ],
        out_specs=out_specs,
    )(q_new, *page_list, page_ok, acc, top, total)


def attention(query_start, key_pos, page_ok, q_new, new_all, pages, group_size, head_size,
              mask_pages):
    q_rows = q_new.shape[0]
    blocks, kv_heads, new_len, width = new_all.shape
    npage, _, page_len, _ = pages.shape
    kernel = functools.partial(
        attention_kernel, head_size=head_size, group_size=group_size, mask_pages=mask_pages
    )
    span = group_size * head_size
    stat = jax.ShapeDtypeStruct((kv_heads, q_rows, group_size), jnp.float32)
    stat_spec = pl.BlockSpec((1, q_rows, group_size), lambda g, s: (g, 0, 0))
    return pl.pallas_call(
        kernel,
        out_shape=(jax.ShapeDtypeStruct(q_new.shape, jnp.float32), stat, stat),
        grid_spec=pltpu.PrefetchScalarGridSpec(
            num_scalar_prefetch=1,
            grid=(kv_heads,),
            in_specs=[
                pl.BlockSpec((q_rows, span), lambda g, s: (0, g)),
                pl.BlockSpec((blocks, 1, new_len, width), lambda g, s: (0, g, 0, 0)),
                pl.BlockSpec((npage, 1, page_len, width), lambda g, s: (0, g, 0, 0)),
                pl.BlockSpec((1, blocks * new_len), lambda g, s: (0, 0)),
                pl.BlockSpec((1, npage * page_len), lambda g, s: (0, 0)),
            ],
            out_specs=(pl.BlockSpec((q_rows, span), lambda g, s: (0, g)), stat_spec, stat_spec),
        ),
    )(query_start, q_new, new_all, pages, key_pos, page_ok)


def local(q_new, kv_new, kv_cache, page_table, block_offsets):
    kv_heads = kv_new.shape[1]
    head_size = kv_new.shape[2] // 2
    group_size = q_new.shape[1] // (head_size * kv_heads)
    slots_dev = kv_cache.shape[0]
    npages = page_table.shape[0]
    blocks = lax.axis_size("blk")
    myself = lax.axis_index("blk")
    pg = -(-npages // blocks)
    block_ids = jnp.arange(blocks, dtype=jnp.int32)
    my_offset = jnp.sum(jnp.where(block_ids == myself, block_offsets, 0))

    own_rows = kv_new.transpose(1, 0, 2)
    new_all = [own_rows]
    for k in range(1, blocks):
        new_all.append(
            lax.ppermute(own_rows, "blk", [(i, (i + k) % blocks) for i in range(blocks)])
        )
    shifted_offsets = block_offsets[(myself - block_ids) % blocks]

    page_owner = page_table // slots_dev
    owned = page_owner == myself
    page_ids = jnp.arange(npages, dtype=jnp.int32)
    page_rank = jnp.sum(
        ((page_ids[None, :] < page_ids[:, None]) & owned[None, :]).astype(jnp.int32), axis=1
    )
    local_slot = page_table % slots_dev
    counts = jnp.sum((page_owner[None, :] == block_ids[:, None]).astype(jnp.int32), axis=1)
    per_peer = (CAP + blocks - 1) // blocks
    starts = jnp.sum((page_owner[None, :] < block_ids[:, None]).astype(jnp.int32), axis=1)
    my_start = jnp.sum(jnp.where(block_ids == myself, starts, 0))
    peer_slots = jnp.arange(per_peer, dtype=jnp.int32)[None, :]
    wanted = (block_ids[:, None] - my_start) % blocks + peer_slots * blocks
    picked = owned[None, None, :] & (page_rank[None, None, :] == wanted[..., None])
    chosen = jnp.sum(jnp.where(picked, local_slot[None, None, :], 0), axis=2).reshape(-1)
    by_shift = chosen.reshape(blocks, per_peer)[(myself + block_ids) % blocks].reshape(-1)
    sent = kv_cache[by_shift].reshape((blocks, per_peer) + kv_cache.shape[1:])
    sent, new_all = lax.optimization_barrier((sent, new_all))
    new_all = jnp.stack(new_all)
    arrived = [sent[0]]
    for k in range(1, blocks):
        arrived.append(
            lax.ppermute(sent[k], "blk", [(i, (i + k) % blocks) for i in range(blocks)])
        )
    received = jnp.stack(arrived).reshape((blocks * per_peer,) + kv_cache.shape[1:])
    arriving = (myself - starts[:, None]) % blocks + peer_slots * blocks
    present = (arriving < counts[:, None])[(myself - block_ids) % blocks].reshape(-1)
    chunk_ids = jnp.arange(blocks * per_peer, dtype=jnp.int32)
    order_rank = jnp.sum(
        ((chunk_ids[None, :] < chunk_ids[:, None]) & present[None, :]).astype(jnp.int32), axis=1
    )
    choose = present[None, :] & (order_rank[None, :] == jnp.arange(pg, dtype=jnp.int32)[:, None])
    positions = jnp.sum(
        jnp.where(choose, jnp.arange(blocks * per_peer, dtype=jnp.int32)[None, :], 0), axis=1
    )
    own = received[positions]
    gathered = [own]
    for k in range(1, blocks):
        gathered.append(
            lax.ppermute(own, "blk", [(i, (i + k) % blocks) for i in range(blocks)])
        )
    later = blocks > 2

    q_rows = q_new.shape[0]
    page_len = kv_cache.shape[2]
    query_start = (my_offset * q_rows).reshape(1).astype(jnp.int32)
    key_pos = (
        jnp.repeat(shifted_offsets, q_rows) * q_rows
        + jnp.tile(jnp.arange(q_rows, dtype=jnp.int32), blocks)
    ).reshape(1, -1).astype(jnp.int32)
    slot_ids = jnp.arange(pg, dtype=jnp.int32)
    page_ok = slot_ids[None, :] * blocks + ((myself - block_ids) % blocks)[:, None] < npages
    page_ok = jnp.repeat(page_ok.astype(jnp.int32).reshape(-1), page_len).reshape(1, -1)
    own_ok = page_ok[:, : pg * page_len]
    first_ok = page_ok[:, pg * page_len : 2 * pg * page_len]
    later_ok = page_ok[:, 2 * pg * page_len :]
    ragged = npages % blocks != 0
    acc, top, total = attention(
        query_start, key_pos, own_ok, q_new, new_all, own, group_size, head_size, ragged
    )
    if not later:
        return prefix_part(
            first_ok, q_new, [gathered[1]], acc, top, total, group_size, head_size, ragged
        )
    acc, top, total = prefix_part(
        first_ok, q_new, [gathered[1]], acc, top, total, group_size, head_size, ragged, False
    )
    acc, top, total, farther = lax.optimization_barrier((acc, top, total, gathered[2:]))
    return prefix_part(later_ok, q_new, list(farther), acc, top, total, group_size, head_size, ragged)


def solution(mesh):
    return jax.shard_map(
        local,
        mesh=mesh,
        in_specs=(
            P(("groups", "blk"), "pool"),
            P(("groups", "blk"), "pool", None),
            P(("groups", "blk"), "pool", None, None),
            P("groups"),
            P("groups"),
        ),
        out_specs=P(("groups", "blk"), "pool"),
        check_vma=False,
    )
```
